32 devices in a mesh: gx: 4 (over z), gy: 4 (over y, x), gz: 2 (over core).
Axes of the slice: x: 2, y: 2, z: 4, core: 2. Of those that a mesh axis runs over, the one named last changes fastest.
Arguments:
- residual: float32 [128, 139264], P(None, ('gx', 'gy', 'gz')), may hold values from -6 to 6
- diag_inverse: bfloat16 [640, 256, 256], P(('gx', 'gy', 'gz'))
- coupling: bfloat16 [608, 256, 256], P(('gx', 'gy', 'gz')), may hold values from -0.09375 to 0.09375
- parent: int32 [640], P(('gx', 'gy', 'gz')), may hold values from 0 to 18, as said below
- send_rows: int32 [192, 128], P(('gx', 'gy', 'gz')), may hold values from 0 to 4351
- counts: int32 [32], P(('gx', 'gy', 'gz')), may hold values from 10 to 40, as said below
- deflation: float32 [40, 139264], P(None, ('gx', 'gy', 'gz')), may hold values from -0.09375 to 0.09375
- coarse_inverse: float32 [1280, 1280], P(('gx', 'gy', 'gz')), as said below
Outputs:
- preconditioned: float32 [128, 139264], P(None, ('gx', 'gy', 'gz'))
The draws below stay inside these ranges and needn't reach their ends.
Inputs may be any that keep to these rules, and one draw needn't show every extreme that they name: The parent of supernode b >= 1 is one of b - 4 to b - 1 of the same subdomain (0 at the least), the last supernode's parent is the one before it, and the entry of supernode 0 is 0. `counts`: every draw has a subdomain with 40 and one with 10 vectors. coarse_inverse is symmetric.
All inputs are finite; a program needn't handle non-finite values.
Results may differ from the reference program's by a relative error of at most 0.005.
Values may be sent and summed in bfloat16 or wider, within the bound.
No kernel may reach another device: no remote copies, remote signals or barrier semaphores. Data moves between devices by JAX's collectives and lax.ppermute only.
A program may use at most 128 MiB of HBM per device.

```python
import jax
import jax.numpy as jnp
from jax import lax

NRHS = 128
SB = 256
NB = 20
OV = 128
KMAX = 40
NI = 4352
ROWS = 139264
NC = 1280
N_GX = 4
N_GY = 4
N_GZ = 2
DEVICES = 32


def draw_diag_inverse(key, part):
    key_noise, key_diag = jax.random.split(key)
    count_all = N_GX * N_GY * N_GZ * NB
    noise = jax.random.normal(key_noise, (count_all, SB, SB), jnp.float32)
    noise = noise * (0.3 / SB ** 0.5)
    scales = jax.random.uniform(key_diag, (count_all, SB, 1), jnp.float32, 0.7, 1.4)
    identity = (lax.iota(jnp.int32, SB)[:, None] == lax.iota(jnp.int32, SB)[None, :]).astype(jnp.float32)
    return (noise + identity[None] * scales).astype(jnp.bfloat16)


def draw_parent(key, part):
    count_all = N_GX * N_GY * N_GZ * NB
    place = lax.iota(jnp.int32, count_all) % NB
    lowest = jnp.maximum(place - 4, 0)
    highest = jnp.maximum(place, 1)
    chosen = jax.random.randint(key, (count_all,), lowest, highest)
    return jnp.where(place == NB - 1, NB - 2, chosen).astype(jnp.int32)


def draw_counts(key, part):
    total_dev = N_GX * N_GY * N_GZ
    key_main, key_high, key_step = jax.random.split(key, 3)
    values = jax.random.randint(key_main, (total_dev,), KMAX // 4, KMAX + 1)
    high_at = jax.random.randint(key_high, (), 0, total_dev)
    low_at = (high_at + 1 + jax.random.randint(key_step, (), 0, total_dev - 1)) % total_dev
    values = values.at[high_at].set(KMAX).at[low_at].set(KMAX // 4)
    return values.astype(jnp.int32)


def draw_coarse_inverse(key, part):
    total = KMAX * N_GX * N_GY * N_GZ
    base = jax.random.normal(key, (total, total), jnp.float32)
    identity = (lax.iota(jnp.int32, total)[:, None] == lax.iota(jnp.int32, total)[None, :]).astype(jnp.float32)
    return (base + base.T) * 0.06 + identity


def place_ends(entries, key, smallest, high):
    longest = entries.shape.index(max(entries.shape))
    spots = []
    for shift in (0, 1):
        where = [jax.random.randint(jax.random.fold_in(key, axis), (), 0, length) for axis, length in enumerate(entries.shape)]
        where[longest] = (where[longest] + shift) % entries.shape[longest]
        spots.append(tuple(where))
    return entries.at[spots[0]].set(smallest).at[spots[1]].set(high)


def block_scale(stream_key, shape, cuts, smallest, high):
    factor_of, own = 1.0, jax.random.fold_in(stream_key, 6)
    for position, parts in cuts:
        steps = jnp.exp(jax.random.uniform(jax.random.fold_in(own, position), (parts,), jnp.float32, smallest / len(cuts), high / len(cuts)))
        factor_of = factor_of * jnp.repeat(steps, shape[position] // parts).reshape([-1 if axis == position else 1 for axis in range(len(shape))])
    return factor_of


def bell_draw(own_key, dims, deviation, reach, cuts=(), held_as=jnp.bfloat16):
    entries = jax.random.normal(own_key, dims, jnp.float32) * deviation
    if len(cuts) > 0:
        entries = block_scale(own_key, dims, cuts, -0.22, 0.18) * entries
    return jnp.clip(entries, min=-reach, max=reach).astype(held_as)


def setup_inputs(seed: int = 0) -> dict:
    key_of = jax.random.split(jax.random.key(seed), 9)
    residual = bell_draw(key_of[0], (NRHS, ROWS), 1.0, 6.0, ((1, 32),), jnp.float32)
    diag_inverse = draw_diag_inverse(jax.random.fold_in(key_of[8], 71), 0)
    coupling = bell_draw(key_of[2], (DEVICES * (NB - 1), SB, SB), (16 * SB) ** -0.5, 0.09375, ((0, 32),))
    parent = draw_parent(jax.random.fold_in(key_of[8], 71), 0)
    send_rows = place_ends(jax.random.randint(key_of[4], (DEVICES * 6, OV), 0, NI), jax.random.fold_in(key_of[4], 1), 0, NI - 1).astype(jnp.int32)
    counts = draw_counts(jax.random.fold_in(key_of[8], 71), 0)
    deflation = bell_draw(key_of[6], (KMAX, ROWS), NI ** -0.5, 0.09375, ((1, 32),), jnp.float32)
    coarse_inverse = draw_coarse_inverse(jax.random.fold_in(key_of[8], 71), 0)
    return {"residual": residual, "diag_inverse": diag_inverse, "coupling": coupling, "parent": parent, "send_rows": send_rows, "counts": counts, "deflation": deflation, "coarse_inverse": coarse_inverse}


def solve_local(extended, diag_inverse, coupling, parent):
    nrhs_here, width_ext = extended.shape
    blocks_n, block_w, _ = diag_inverse.shape
    blocks = extended.reshape(nrhs_here, blocks_n, block_w).transpose(1, 0, 2)
    first = jnp.einsum("rs,ts->rt", blocks[0].astype(jnp.bfloat16), diag_inverse[0], preferred_element_type=jnp.float32).astype(jnp.bfloat16)
    store = jnp.zeros((blocks_n, nrhs_here, block_w), jnp.bfloat16).at[0].set(first)
    places = lax.iota(jnp.int32, blocks_n)

    def forward(store, item):
        block, inverse_blk, couple, link, place = item
        prior = lax.dynamic_index_in_dim(store, link, 0, keepdims=False)
        lower = (block - jnp.einsum("rs,ts->rt", prior, couple, preferred_element_type=jnp.float32)).astype(jnp.bfloat16)
        value = jnp.einsum("rs,ts->rt", lower, inverse_blk, preferred_element_type=jnp.float32).astype(jnp.bfloat16)
        return lax.dynamic_update_index_in_dim(store, value, place, 0), None

    store, _ = lax.scan(forward, store, (blocks[1:], diag_inverse[1:], coupling, parent[1:], places[1:]))

    def backward(carry, item):
        value, inverse_blk, link, place = item
        upper = (value.astype(jnp.float32) - lax.dynamic_index_in_dim(carry, place, 0, keepdims=False)).astype(jnp.bfloat16)
        result = jnp.einsum("rs,st->rt", upper, inverse_blk, preferred_element_type=jnp.float32).astype(jnp.bfloat16)
        couple = lax.dynamic_index_in_dim(coupling, jnp.maximum(place - 1, 0).astype(jnp.int32), 0, keepdims=False)
        push = jnp.einsum("rs,st->rt", result, couple, preferred_element_type=jnp.float32) * (place > 0).astype(jnp.float32)
        target = lax.dynamic_index_in_dim(carry, link, 0, keepdims=False)
        carry = lax.dynamic_update_index_in_dim(carry, target + push, link, 0)
        return carry, result

    empty = jnp.zeros((blocks_n, nrhs_here, block_w), jnp.float32)
    _, solved = lax.scan(backward, empty, (store, diag_inverse, parent, places), reverse=True)
    return solved.transpose(1, 0, 2).reshape(nrhs_here, width_ext)


def shift_grid(array, axis, offset):
    extent = array.shape[axis]
    zero = jnp.zeros_like(lax.slice_in_dim(array, 0, 1, axis=axis))
    if offset == 1:
        return jnp.concatenate([zero, lax.slice_in_dim(array, 0, extent - 1, axis=axis)], axis=axis)
    return jnp.concatenate([lax.slice_in_dim(array, 1, extent, axis=axis), zero], axis=axis)


def reference(residual, diag_inverse, coupling, parent, send_rows, counts, deflation, coarse_inverse):
    total_dev = N_GX * N_GY * N_GZ
    grid = (N_GX, N_GY, N_GZ)
    owned = residual.reshape(NRHS, total_dev, NI).transpose(1, 0, 2)
    lists = send_rows.reshape(total_dev, 6, OV)
    sent = jax.vmap(lambda values, index: jnp.moveaxis(jnp.take(values, index, axis=1), 1, 0))(owned, lists)
    sent = sent.reshape(grid + (6, NRHS, OV))
    slots = []
    for axis_pos in range(3):
        slots.append(shift_grid(sent[:, :, :, 2 * axis_pos], axis_pos, -1))
        slots.append(shift_grid(sent[:, :, :, 2 * axis_pos + 1], axis_pos, 1))
    slots = jnp.stack(slots, axis=3).reshape(total_dev, 6, NRHS, OV)
    slots = jnp.moveaxis(slots, 1, 2).reshape(total_dev, NRHS, 6 * OV)
    extended = jnp.concatenate([owned, slots], axis=2)
    inverses = diag_inverse.reshape(total_dev, NB, SB, SB)
    couples = coupling.reshape(total_dev, NB - 1, SB, SB)
    links = parent.reshape(total_dev, NB)
    solved = lax.map(lambda item: solve_local(*item), (extended, inverses, couples, links))
    corrections = solved[:, :, NI:].reshape(total_dev, NRHS, 6, OV)
    corrections = jnp.moveaxis(corrections, 2, 1).reshape(grid + (6, NRHS, OV))
    returned = []
    for axis_pos in range(3):
        returned.append(shift_grid(corrections[:, :, :, 2 * axis_pos], axis_pos, 1))
        returned.append(shift_grid(corrections[:, :, :, 2 * axis_pos + 1], axis_pos, -1))
    returned = jnp.stack(returned, axis=3).reshape(total_dev, 6, NRHS, OV).astype(jnp.float32)
    local_part = solved[:, :, :NI].astype(jnp.float32)

    def add_faces(values, index, pieces):
        for face in range(6):
            values = values.at[:, index[face]].add(pieces[face])
        return values

    local_part = jax.vmap(add_faces)(local_part, lists, returned)
    mask = (lax.iota(jnp.int32, KMAX)[None, :] < counts[:, None]).astype(jnp.float32)
    vectors = deflation.reshape(KMAX, total_dev, NI).transpose(1, 0, 2) * mask[:, :, None]
    coeffs = jnp.einsum("drn,dkn->rdk", owned, vectors, precision=lax.Precision.HIGHEST).reshape(NRHS, NC)
    solved_coarse = jnp.dot(coeffs, coarse_inverse.T, precision=lax.Precision.HIGHEST, preferred_element_type=jnp.float32)
    solved_coarse = solved_coarse.reshape(NRHS, total_dev, KMAX)
    coarse_part = jnp.einsum("rdk,dkn->drn", solved_coarse, vectors, precision=lax.Precision.HIGHEST)
    total = local_part + coarse_part
    return total.transpose(1, 0, 2).reshape(NRHS, ROWS)
```

```python
import functools

import jax
import jax.numpy as jnp
from jax import lax
from jax.experimental import pallas as pl
from jax.experimental.pallas import tpu as pltpu
from jax.sharding import PartitionSpec as P

AXES = ("gx", "gy", "gz")
NT = (((1,), (1,)), ((), ()))


def solve_kernel(parent_ref, res_ref, slot_ref, inv_ref, cpl_ref, own_ref, zslot_ref, y_ref, carry_ref):
    blocks_n, block_w, _ = inv_ref.shape
    owned_blocks = res_ref.shape[1] // block_w

    def columns(b):
        if b < owned_blocks:
            return res_ref, pl.ds(b * block_w, block_w)
        return slot_ref, pl.ds((b - owned_blocks) * block_w, block_w)

    def link(b):
        return jnp.clip(parent_ref[b], 0, blocks_n - 1)

    for b in range(blocks_n):
        ref, cols = columns(b)
        x = ref[:, cols]
        if b == 0:
            lower = x.astype(jnp.bfloat16)
        else:
            prior = y_ref[link(b)]
            lower = (
                x - lax.dot_general(prior, cpl_ref[b - 1], NT, preferred_element_type=jnp.float32)
            ).astype(jnp.bfloat16)
        y_ref[b] = lax.dot_general(
            lower, inv_ref[b], NT, preferred_element_type=jnp.float32
        ).astype(jnp.bfloat16)

    carry_ref[...] = jnp.zeros(carry_ref.shape, carry_ref.dtype)
    for b in reversed(range(blocks_n)):
        upper = (y_ref[b].astype(jnp.float32) - carry_ref[b]).astype(jnp.bfloat16)
        result = jnp.dot(upper, inv_ref[b], preferred_element_type=jnp.float32).astype(jnp.bfloat16)
        if b < owned_blocks:
            own_ref[:, pl.ds(b * block_w, block_w)] = result
        else:
            zslot_ref[:, pl.ds((b - owned_blocks) * block_w, block_w)] = result
        if b > 0:
            push = jnp.dot(result, cpl_ref[b - 1], preferred_element_type=jnp.float32)
            p = link(b)
            carry_ref[p] = carry_ref[p] + push


def local_solve(parent, residual, slots, diag_inverse, coupling):
    nrhs_here, owned_n = residual.shape
    blocks_n, block_w, _ = diag_inverse.shape
    vmem = pltpu.VMEM
    return pl.pallas_call(
        solve_kernel,
        out_shape=(
            jax.ShapeDtypeStruct((nrhs_here, owned_n), jnp.bfloat16),
            jax.ShapeDtypeStruct(slots.shape, jnp.bfloat16),
        ),
        in_specs=[
            pl.BlockSpec(memory_space=pltpu.SMEM),
            pl.BlockSpec(memory_space=vmem),
            pl.BlockSpec(memory_space=vmem),
            pl.BlockSpec(memory_space=vmem),
            pl.BlockSpec(memory_space=vmem),
        ],
        out_specs=(pl.BlockSpec(memory_space=vmem), pl.BlockSpec(memory_space=vmem)),
        scratch_shapes=[
            pltpu.VMEM((blocks_n, nrhs_here, block_w), jnp.bfloat16),
            pltpu.VMEM((blocks_n, nrhs_here, block_w), jnp.float32),
        ],
        compiler_params=pltpu.CompilerParams(vmem_limit_bytes=48 * 1024 * 1024),
    )(parent, residual, slots, diag_inverse, coupling)


def shift(value, axis, up):
    count = lax.axis_size(axis)
    if up:
        pairs = [(i, i + 1) for i in range(count - 1)]
    else:
        pairs = [(i + 1, i) for i in range(count - 1)]
    return lax.ppermute(value, axis, pairs)


def per_device(
    residual, diag_inverse, coupling, parent, send_rows, counts, deflation, coarse_inverse
):
    nrhs_here, owned_n = residual.shape
    slots_n, face_w = send_rows.shape
    kmax_here = deflation.shape[0]
    mask = (lax.iota(jnp.int32, kmax_here) < counts[0]).astype(jnp.float32)
    vectors = deflation * mask[:, None]
    coeffs = jnp.dot(
        residual, vectors.T, precision=lax.Precision.HIGHEST, preferred_element_type=jnp.float32
    )
    gathered = lax.all_gather(coeffs, AXES, axis=1, tiled=True)
    solved_coarse = lax.dot_general(
        gathered,
        coarse_inverse,
        (((1,), (1,)), ((), ())),
        precision=lax.Precision.HIGHEST,
        preferred_element_type=jnp.float32,
    )

    outgoing = jnp.take(residual, send_rows, axis=1)
    incoming = []
    for axis_pos, axis in enumerate(AXES):
        incoming.append(shift(outgoing[:, 2 * axis_pos], axis, up=False))
        incoming.append(shift(outgoing[:, 2 * axis_pos + 1], axis, up=True))
    slots = jnp.concatenate(incoming, axis=1)

    own, zslots = local_solve(parent, residual, slots, diag_inverse, coupling)

    returned = []
    for axis_pos, axis in enumerate(AXES):
        lo = zslots[:, (2 * axis_pos) * face_w : (2 * axis_pos + 1) * face_w]
        hi = zslots[:, (2 * axis_pos + 1) * face_w : (2 * axis_pos + 2) * face_w]
        returned.append(shift(lo, axis, up=True))
        returned.append(shift(hi, axis, up=False))
    returned = jnp.concatenate(returned, axis=1)
    onehot = (
        send_rows.reshape(slots_n * face_w, 1) == lax.iota(jnp.int32, owned_n)[None, :]
    ).astype(jnp.bfloat16)
    faces = jnp.dot(returned, onehot, preferred_element_type=jnp.float32)
    coarse = jnp.dot(
        solved_coarse, vectors, precision=lax.Precision.HIGHEST, preferred_element_type=jnp.float32
    )
    return own.astype(jnp.float32) + faces + coarse


def solution(mesh):
    return jax.shard_map(
        per_device,
        mesh=mesh,
        in_specs=(
            P(None, AXES),
            P(AXES, None, None),
            P(AXES, None, None),
            P(AXES),
            P(AXES, None),
            P(AXES),
            P(None, AXES),
            P(AXES, None),
        ),
        out_specs=P(None, AXES),
        check_vma=False,
    )
```

```python
import functools

import jax
import jax.numpy as jnp
from jax import lax
from jax.experimental import pallas as pl
from jax.experimental.pallas import tpu as pltpu
from jax.sharding import PartitionSpec as P

AXES = ("gx", "gy", "gz")
NT = (((1,), (1,)), ((), ()))


def solve_kernel(parent_ref, res_ref, slot_ref, inv_ref, cpl_ref, own_ref, zslot_ref, y_ref, carry_ref):
    blocks_n, block_w, _ = inv_ref.shape
    owned_blocks = res_ref.shape[1] // block_w

    def columns(b):
        if b < owned_blocks:
            return res_ref, pl.ds(b * block_w, block_w)
        return slot_ref, pl.ds((b - owned_blocks) * block_w, block_w)

    def link(b):
        return jnp.clip(parent_ref[b], 0, blocks_n - 1)

    for b in range(blocks_n):
        ref, cols = columns(b)
        x = ref[:, cols]
        if b == 0:
            lower = x.astype(jnp.bfloat16)
        else:
            prior = y_ref[link(b)]
            lower = (
                x - lax.dot_general(prior, cpl_ref[b - 1], NT, preferred_element_type=jnp.float32)
            ).astype(jnp.bfloat16)
        y_ref[b] = lax.dot_general(
            lower, inv_ref[b], NT, preferred_element_type=jnp.float32
        ).astype(jnp.bfloat16)

    carry_ref[...] = jnp.zeros(carry_ref.shape, carry_ref.dtype)
    for b in reversed(range(blocks_n)):
        upper = (y_ref[b].astype(jnp.float32) - carry_ref[b]).astype(jnp.bfloat16)
        result = jnp.dot(upper, inv_ref[b], preferred_element_type=jnp.float32).astype(jnp.bfloat16)
        if b < owned_blocks:
            own_ref[:, pl.ds(b * block_w, block_w)] = result
        else:
            zslot_ref[:, pl.ds((b - owned_blocks) * block_w, block_w)] = result
        if b > 0:
            push = jnp.dot(result, cpl_ref[b - 1], preferred_element_type=jnp.float32)
            p = link(b)
            carry_ref[p] = carry_ref[p] + push


def local_solve(parent, residual, slots, diag_inverse, coupling):
    nrhs_here, owned_n = residual.shape
    blocks_n, block_w, _ = diag_inverse.shape
    vmem = pltpu.VMEM
    return pl.pallas_call(
        solve_kernel,
        out_shape=(
            jax.ShapeDtypeStruct((nrhs_here, owned_n), jnp.bfloat16),
            jax.ShapeDtypeStruct(slots.shape, jnp.bfloat16),
        ),
        in_specs=[
            pl.BlockSpec(memory_space=pltpu.SMEM),
            pl.BlockSpec(memory_space=vmem),
            pl.BlockSpec(memory_space=vmem),
            pl.BlockSpec(memory_space=vmem),
            pl.BlockSpec(memory_space=vmem),
        ],
        out_specs=(pl.BlockSpec(memory_space=vmem), pl.BlockSpec(memory_space=vmem)),
        scratch_shapes=[
            pltpu.VMEM((blocks_n, nrhs_here, block_w), jnp.bfloat16),
            pltpu.VMEM((blocks_n, nrhs_here, block_w), jnp.float32),
        ],
        compiler_params=pltpu.CompilerParams(vmem_limit_bytes=48 * 1024 * 1024),
    )(parent, residual, slots, diag_inverse, coupling)


def shift(value, axis, up):
    count = lax.axis_size(axis)
    if up:
        pairs = [(i, i + 1) for i in range(count - 1)]
    else:
        pairs = [(i + 1, i) for i in range(count - 1)]
    return lax.ppermute(value, axis, pairs)


def per_device(
    residual, diag_inverse, coupling, parent, send_rows, counts, deflation, coarse_inverse
):
    nrhs_here, owned_n = residual.shape
    slots_n, face_w = send_rows.shape
    kmax_here = deflation.shape[0]
    mask = (lax.iota(jnp.int32, kmax_here) < counts[0]).astype(jnp.float32)
    vectors = deflation * mask[:, None]
    coeffs_t = lax.dot_general(
        vectors, residual, NT, precision=lax.Precision.HIGHEST, preferred_element_type=jnp.float32
    )
    me = lax.axis_index(AXES)
    placed = jnp.zeros((coarse_inverse.shape[1], coeffs_t.shape[1]), jnp.float32)
    placed = lax.dynamic_update_slice_in_dim(placed, coeffs_t, me * kmax_here, axis=0)
    gathered = lax.psum(placed, AXES)
    solved_t = jnp.dot(
        coarse_inverse, gathered, precision=lax.Precision.HIGHEST, preferred_element_type=jnp.float32
    )

    outgoing = jnp.take(residual, send_rows, axis=1)
    incoming = []
    for axis_pos, axis in enumerate(AXES):
        incoming.append(shift(outgoing[:, 2 * axis_pos], axis, up=False))
        incoming.append(shift(outgoing[:, 2 * axis_pos + 1], axis, up=True))
    slots = jnp.concatenate(incoming, axis=1)

    own, zslots = local_solve(parent, residual, slots, diag_inverse, coupling)

    returned = []
    for axis_pos, axis in enumerate(AXES):
        lo = zslots[:, (2 * axis_pos) * face_w : (2 * axis_pos + 1) * face_w]
        hi = zslots[:, (2 * axis_pos + 1) * face_w : (2 * axis_pos + 2) * face_w]
        returned.append(shift(lo, axis, up=True))
        returned.append(shift(hi, axis, up=False))
    returned = jnp.concatenate(returned, axis=1)
    onehot = (
        send_rows.reshape(slots_n * face_w, 1) == lax.iota(jnp.int32, owned_n)[None, :]
    ).astype(jnp.bfloat16)
    faces = jnp.dot(returned, onehot, preferred_element_type=jnp.float32)
    coarse = lax.dot_general(
        solved_t,
        vectors,
        (((0,), (0,)), ((), ())),
        precision=lax.Precision.HIGHEST,
        preferred_element_type=jnp.float32,
    )
    return own.astype(jnp.float32) + faces + coarse


def solution(mesh):
    return jax.shard_map(
        per_device,
        mesh=mesh,
        in_specs=(
            P(None, AXES),
            P(AXES, None, None),
            P(AXES, None, None),
            P(AXES),
            P(AXES, None),
            P(AXES),
            P(None, AXES),
            P(AXES, None),
        ),
        out_specs=P(None, AXES),
        check_vma=False,
    )
```

```python
import functools

import jax
import jax.numpy as jnp
from jax import lax
from jax.experimental import pallas as pl
from jax.experimental.pallas import tpu as pltpu
from jax.sharding import PartitionSpec as P

AXES = ("gx", "gy", "gz")
NT = (((1,), (1,)), ((), ()))


def solve_kernel(parent_ref, res_ref, slot_ref, inv_ref, cpl_ref, own_ref, zslot_ref, y_ref, carry_ref):
    blocks_n, block_w, _ = inv_ref.shape
    owned_blocks = res_ref.shape[1] // block_w

    def columns(b):
        if b < owned_blocks:
            return res_ref, pl.ds(b * block_w, block_w)
        return slot_ref, pl.ds((b - owned_blocks) * block_w, block_w)

    def link(b):
        return jnp.clip(parent_ref[b], 0, blocks_n - 1)

    for b in range(blocks_n):
        ref, cols = columns(b)
        x = ref[:, cols]
        if b == 0:
            lower = x.astype(jnp.bfloat16)
        else:
            prior = y_ref[link(b)]
            lower = (
                x - lax.dot_general(prior, cpl_ref[b - 1], NT, preferred_element_type=jnp.float32)
            ).astype(jnp.bfloat16)
        y_ref[b] = lax.dot_general(
            lower, inv_ref[b], NT, preferred_element_type=jnp.float32
        ).astype(jnp.bfloat16)

    carry_ref[...] = jnp.zeros(carry_ref.shape, carry_ref.dtype)
    for b in reversed(range(blocks_n)):
        upper = (y_ref[b].astype(jnp.float32) - carry_ref[b]).astype(jnp.bfloat16)
        result = jnp.dot(upper, inv_ref[b], preferred_element_type=jnp.float32).astype(jnp.bfloat16)
        if b < owned_blocks:
            own_ref[:, pl.ds(b * block_w, block_w)] = result
        else:
            zslot_ref[:, pl.ds((b - owned_blocks) * block_w, block_w)] = result
        if b > 0:
            push = jnp.dot(result, cpl_ref[b - 1], preferred_element_type=jnp.float32)
            p = link(b)
            carry_ref[p] = carry_ref[p] + push


def local_solve(parent, residual, slots, diag_inverse, coupling):
    nrhs_here, owned_n = residual.shape
    blocks_n, block_w, _ = diag_inverse.shape
    vmem = pltpu.VMEM
    return pl.pallas_call(
        solve_kernel,
        out_shape=(
            jax.ShapeDtypeStruct((nrhs_here, owned_n), jnp.bfloat16),
            jax.ShapeDtypeStruct(slots.shape, jnp.bfloat16),
        ),
        in_specs=[
            pl.BlockSpec(memory_space=pltpu.SMEM),
            pl.BlockSpec(memory_space=vmem),
            pl.BlockSpec(memory_space=vmem),
            pl.BlockSpec(memory_space=vmem),
            pl.BlockSpec(memory_space=vmem),
        ],
        out_specs=(pl.BlockSpec(memory_space=vmem), pl.BlockSpec(memory_space=vmem)),
        scratch_shapes=[
            pltpu.VMEM((blocks_n, nrhs_here, block_w), jnp.bfloat16),
            pltpu.VMEM((blocks_n, nrhs_here, block_w), jnp.float32),
        ],
        compiler_params=pltpu.CompilerParams(vmem_limit_bytes=48 * 1024 * 1024),
    )(parent, residual, slots, diag_inverse, coupling)


def shift(value, axis, up):
    count = lax.axis_size(axis)
    if up:
        pairs = [(i, i + 1) for i in range(count - 1)]
    else:
        pairs = [(i + 1, i) for i in range(count - 1)]
    return lax.ppermute(value, axis, pairs)


def gather_axis(value, axis):
    count = lax.axis_size(axis)
    if count & (count - 1):
        return lax.all_gather(value, axis, axis=0, tiled=False)
    me = lax.axis_index(axis)
    held = value[None]
    step = 1
    while step < count:
        pairs = [(i, i ^ step) for i in range(count)]
        other = lax.ppermute(held, axis, pairs)
        low = (me // step) % 2 == 0
        held = jnp.where(low, jnp.concatenate([held, other]), jnp.concatenate([other, held]))
        step *= 2
    return held


def gather_all(value):
    for axis in reversed(AXES):
        value = gather_axis(value, axis)
    return value


def per_device(
    residual, diag_inverse, coupling, parent, send_rows, counts, deflation, coarse_inverse
):
    nrhs_here, owned_n = residual.shape
    slots_n, face_w = send_rows.shape
    kmax_here = deflation.shape[0]
    mask = (lax.iota(jnp.int32, kmax_here) < counts[0]).astype(jnp.float32)
    vectors = deflation * mask[:, None]
    coeffs_t = lax.dot_general(
        vectors, residual, NT, precision=lax.Precision.HIGHEST, preferred_element_type=jnp.float32
    )
    gathered = gather_all(coeffs_t).reshape(-1, coeffs_t.shape[1])
    solved_t = jnp.dot(
        coarse_inverse, gathered, precision=lax.Precision.HIGHEST, preferred_element_type=jnp.float32
    )

    outgoing = jnp.take(residual, send_rows, axis=1)
    incoming = []
    for axis_pos, axis in enumerate(AXES):
        incoming.append(shift(outgoing[:, 2 * axis_pos], axis, up=False))
        incoming.append(shift(outgoing[:, 2 * axis_pos + 1], axis, up=True))
    slots = jnp.concatenate(incoming, axis=1)

    own, zslots = local_solve(parent, residual, slots, diag_inverse, coupling)

    returned = []
    for axis_pos, axis in enumerate(AXES):
        lo = zslots[:, (2 * axis_pos) * face_w : (2 * axis_pos + 1) * face_w]
        hi = zslots[:, (2 * axis_pos + 1) * face_w : (2 * axis_pos + 2) * face_w]
        returned.append(shift(lo, axis, up=True))
        returned.append(shift(hi, axis, up=False))
    returned = jnp.concatenate(returned, axis=1)
    onehot = (
        send_rows.reshape(slots_n * face_w, 1) == lax.iota(jnp.int32, owned_n)[None, :]
    ).astype(jnp.bfloat16)
    faces = jnp.dot(returned, onehot, preferred_element_type=jnp.float32)
    coarse = lax.dot_general(
        solved_t,
        vectors,
        (((0,), (0,)), ((), ())),
        precision=lax.Precision.HIGHEST,
        preferred_element_type=jnp.float32,
    )
    return own.astype(jnp.float32) + faces + coarse


def solution(mesh):
    return jax.shard_map(
        per_device,
        mesh=mesh,
        in_specs=(
            P(None, AXES),
            P(AXES, None, None),
            P(AXES, None, None),
            P(AXES),
            P(AXES, None),
            P(AXES),
            P(None, AXES),
            P(AXES, None),
        ),
        out_specs=P(None, AXES),
        check_vma=False,
    )
```

```python
import functools

import jax
import jax.numpy as jnp
from jax import lax
from jax.experimental import pallas as pl
from jax.experimental.pallas import tpu as pltpu
from jax.sharding import PartitionSpec as P

AXES = ("gx", "gy", "gz")
NT = (((1,), (1,)), ((), ()))


def solve_kernel(parent_ref, res_ref, slot_ref, inv_ref, cpl_ref, own_ref, zslot_ref, y_ref, carry_ref):
    blocks_n, block_w, _ = inv_ref.shape
    owned_blocks = res_ref.shape[1] // block_w

    def columns(b):
        if b < owned_blocks:
            return res_ref, pl.ds(b * block_w, block_w)
        return slot_ref, pl.ds((b - owned_blocks) * block_w, block_w)

    def link(b):
        return jnp.clip(parent_ref[b], 0, blocks_n - 1)

    for b in range(blocks_n):
        ref, cols = columns(b)
        x = ref[:, cols]
        if b == 0:
            lower = x.astype(jnp.bfloat16)
        else:
            prior = y_ref[link(b)]
            lower = (
                x - lax.dot_general(prior, cpl_ref[b - 1], NT, preferred_element_type=jnp.float32)
            ).astype(jnp.bfloat16)
        y_ref[b] = lax.dot_general(
            lower, inv_ref[b], NT, preferred_element_type=jnp.float32
        ).astype(jnp.bfloat16)

    carry_ref[...] = jnp.zeros(carry_ref.shape, carry_ref.dtype)
    for b in reversed(range(blocks_n)):
        upper = (y_ref[b].astype(jnp.float32) - carry_ref[b]).astype(jnp.bfloat16)
        result = jnp.dot(upper, inv_ref[b], preferred_element_type=jnp.float32).astype(jnp.bfloat16)
        if b < owned_blocks:
            own_ref[:, pl.ds(b * block_w, block_w)] = result
        else:
            zslot_ref[:, pl.ds((b - owned_blocks) * block_w, block_w)] = result
        if b > 0:
            push = jnp.dot(result, cpl_ref[b - 1], preferred_element_type=jnp.float32)
            p = link(b)
            carry_ref[p] = carry_ref[p] + push


def local_solve(parent, residual, slots, diag_inverse, coupling):
    nrhs_here, owned_n = residual.shape
    blocks_n, block_w, _ = diag_inverse.shape
    vmem = pltpu.VMEM
    return pl.pallas_call(
        solve_kernel,
        out_shape=(
            jax.ShapeDtypeStruct((nrhs_here, owned_n), jnp.bfloat16),
            jax.ShapeDtypeStruct(slots.shape, jnp.bfloat16),
        ),
        in_specs=[
            pl.BlockSpec(memory_space=pltpu.SMEM),
            pl.BlockSpec(memory_space=vmem),
            pl.BlockSpec(memory_space=vmem),
            pl.BlockSpec(memory_space=vmem),
            pl.BlockSpec(memory_space=vmem),
        ],
        out_specs=(pl.BlockSpec(memory_space=vmem), pl.BlockSpec(memory_space=vmem)),
        scratch_shapes=[
            pltpu.VMEM((blocks_n, nrhs_here, block_w), jnp.bfloat16),
            pltpu.VMEM((blocks_n, nrhs_here, block_w), jnp.float32),
        ],
        compiler_params=pltpu.CompilerParams(vmem_limit_bytes=48 * 1024 * 1024),
    )(parent, residual, slots, diag_inverse, coupling)


def shift(value, axis, up):
    count = lax.axis_size(axis)
    if up:
        pairs = [(i, i + 1) for i in range(count - 1)]
    else:
        pairs = [(i + 1, i) for i in range(count - 1)]
    return lax.ppermute(value, axis, pairs)


def gather_axis(held, axis, dim):
    count = lax.axis_size(axis)
    if count & (count - 1):
        return lax.all_gather(held, axis, axis=dim, tiled=True)
    me = lax.axis_index(axis)
    step = 1
    while step < count:
        pairs = [(i, i ^ step) for i in range(count)]
        other = lax.ppermute(held, axis, pairs)
        low = (me // step) % 2 == 0
        held = jnp.where(
            low,
            jnp.concatenate([held, other], axis=dim),
            jnp.concatenate([other, held], axis=dim),
        )
        step *= 2
    return held


def gather_all(value):
    held = value.reshape((1,) * len(AXES) + value.shape)
    for dim, axis in enumerate(AXES):
        held = gather_axis(held, axis, dim)
    return held

def per_device(
    residual, diag_inverse, coupling, parent, send_rows, counts, deflation, coarse_inverse
):
    nrhs_here, owned_n = residual.shape
    slots_n, face_w = send_rows.shape
    kmax_here = deflation.shape[0]
    mask = (lax.iota(jnp.int32, kmax_here) < counts[0]).astype(jnp.float32)
    vectors = deflation * mask[:, None]
    coeffs_t = lax.dot_general(
        vectors, residual, NT, precision=lax.Precision.HIGHEST, preferred_element_type=jnp.float32
    )
    gathered = gather_all(coeffs_t).reshape(-1, coeffs_t.shape[1])
    solved_t = jnp.dot(
        coarse_inverse, gathered, precision=lax.Precision.HIGHEST, preferred_element_type=jnp.float32
    )

    outgoing = jnp.take(residual, send_rows, axis=1)
    incoming = []
    for axis_pos, axis in enumerate(AXES):
        incoming.append(shift(outgoing[:, 2 * axis_pos], axis, up=False))
        incoming.append(shift(outgoing[:, 2 * axis_pos + 1], axis, up=True))
    slots = jnp.concatenate(incoming, axis=1)

    own, zslots = local_solve(parent, residual, slots, diag_inverse, coupling)

    returned = []
    for axis_pos, axis in enumerate(AXES):
        lo = zslots[:, (2 * axis_pos) * face_w : (2 * axis_pos + 1) * face_w]
        hi = zslots[:, (2 * axis_pos + 1) * face_w : (2 * axis_pos + 2) * face_w]
        returned.append(shift(lo, axis, up=True))
        returned.append(shift(hi, axis, up=False))
    returned = jnp.concatenate(returned, axis=1)
    onehot = (
        send_rows.reshape(slots_n * face_w, 1) == lax.iota(jnp.int32, owned_n)[None, :]
    ).astype(jnp.bfloat16)
    faces = jnp.dot(returned, onehot, preferred_element_type=jnp.float32)
    coarse = lax.dot_general(
        solved_t,
        vectors,
        (((0,), (0,)), ((), ())),
        precision=lax.Precision.HIGHEST,
        preferred_element_type=jnp.float32,
    )
    return own.astype(jnp.float32) + faces + coarse


def solution(mesh):
    return jax.shard_map(
        per_device,
        mesh=mesh,
        in_specs=(
            P(None, AXES),
            P(AXES, None, None),
            P(AXES, None, None),
            P(AXES),
            P(AXES, None),
            P(AXES),
            P(None, AXES),
            P(AXES, None),
        ),
        out_specs=P(None, AXES),
        check_vma=False,
    )
```

```python
import functools

import jax
import jax.numpy as jnp
from jax import lax
from jax.experimental import pallas as pl
from jax.experimental.pallas import tpu as pltpu
from jax.sharding import PartitionSpec as P

AXES = ("gx", "gy", "gz")
NT = (((1,), (1,)), ((), ()))


def solve_kernel(parent_ref, res_ref, slot_ref, inv_ref, cpl_ref, own_ref, zslot_ref, y_ref, carry_ref):
    blocks_n, block_w, _ = inv_ref.shape
    owned_blocks = res_ref.shape[1] // block_w

    def columns(b):
        if b < owned_blocks:
            return res_ref, pl.ds(b * block_w, block_w)
        return slot_ref, pl.ds((b - owned_blocks) * block_w, block_w)

    def link(b):
        return jnp.clip(parent_ref[b], 0, blocks_n - 1)

    for b in range(blocks_n):
        ref, cols = columns(b)
        x = ref[:, cols]
        if b == 0:
            lower = x.astype(jnp.bfloat16)
        else:
            prior = y_ref[link(b)]
            lower = (
                x - lax.dot_general(prior, cpl_ref[b - 1], NT, preferred_element_type=jnp.float32)
            ).astype(jnp.bfloat16)
        y_ref[b] = lax.dot_general(
            lower, inv_ref[b], NT, preferred_element_type=jnp.float32
        ).astype(jnp.bfloat16)

    carry_ref[...] = jnp.zeros(carry_ref.shape, carry_ref.dtype)
    for b in reversed(range(blocks_n)):
        upper = (y_ref[b].astype(jnp.float32) - carry_ref[b]).astype(jnp.bfloat16)
        result = jnp.dot(upper, inv_ref[b], preferred_element_type=jnp.float32).astype(jnp.bfloat16)
        if b < owned_blocks:
            own_ref[:, pl.ds(b * block_w, block_w)] = result
        else:
            zslot_ref[:, pl.ds((b - owned_blocks) * block_w, block_w)] = result
        if b > 0:
            push = jnp.dot(result, cpl_ref[b - 1], preferred_element_type=jnp.float32)
            p = link(b)
            carry_ref[p] = carry_ref[p] + push


def local_solve(parent, residual, slots, diag_inverse, coupling):
    nrhs_here, owned_n = residual.shape
    blocks_n, block_w, _ = diag_inverse.shape
    vmem = pltpu.VMEM
    return pl.pallas_call(
        solve_kernel,
        out_shape=(
            jax.ShapeDtypeStruct((nrhs_here, owned_n), jnp.bfloat16),
            jax.ShapeDtypeStruct(slots.shape, jnp.bfloat16),
        ),
        in_specs=[
            pl.BlockSpec(memory_space=pltpu.SMEM),
            pl.BlockSpec(memory_space=vmem),
            pl.BlockSpec(memory_space=vmem),
            pl.BlockSpec(memory_space=vmem),
            pl.BlockSpec(memory_space=vmem),
        ],
        out_specs=(pl.BlockSpec(memory_space=vmem), pl.BlockSpec(memory_space=vmem)),
        scratch_shapes=[
            pltpu.VMEM((blocks_n, nrhs_here, block_w), jnp.bfloat16),
            pltpu.VMEM((blocks_n, nrhs_here, block_w), jnp.float32),
        ],
        compiler_params=pltpu.CompilerParams(vmem_limit_bytes=48 * 1024 * 1024),
    )(parent, residual, slots, diag_inverse, coupling)


def shift(value, axis, up):
    count = lax.axis_size(axis)
    if up:
        pairs = [(i, i + 1) for i in range(count - 1)]
    else:
        pairs = [(i + 1, i) for i in range(count - 1)]
    return lax.ppermute(value, axis, pairs)


def gather_axis(held, axis, dim):
    count = lax.axis_size(axis)
    if count & (count - 1):
        return lax.all_gather(held, axis, axis=dim, tiled=True)
    me = lax.axis_index(axis)
    step = 1
    while step < count:
        pairs = [(i, i ^ step) for i in range(count)]
        other = lax.ppermute(held, axis, pairs)
        low = (me // step) % 2 == 0
        held = jnp.where(
            low,
            jnp.concatenate([held, other], axis=dim),
            jnp.concatenate([other, held], axis=dim),
        )
        step *= 2
    return held


def gather_all(value):
    held = value.reshape((1,) * len(AXES) + value.shape)
    for dim, axis in enumerate(AXES):
        held = gather_axis(held, axis, dim)
    return held

def per_device(
    residual, diag_inverse, coupling, parent, send_rows, counts, deflation, coarse_inverse
):
    nrhs_here, owned_n = residual.shape
    slots_n, face_w = send_rows.shape
    kmax_here = deflation.shape[0]
    mask = (lax.iota(jnp.int32, kmax_here) < counts[0]).astype(jnp.float32)
    vectors = deflation * mask[:, None]
    coeffs_t = lax.dot_general(
        vectors, residual, NT, precision=lax.Precision.HIGHEST, preferred_element_type=jnp.float32
    )
    gathered = lax.all_gather(coeffs_t.reshape(1, -1), AXES, axis=0, tiled=True)
    gathered = gathered.reshape(-1, coeffs_t.shape[1])
    solved_t = jnp.dot(
        coarse_inverse, gathered, precision=lax.Precision.HIGHEST, preferred_element_type=jnp.float32
    )

    outgoing = jnp.take(residual, send_rows, axis=1)
    incoming = []
    for axis_pos, axis in enumerate(AXES):
        incoming.append(shift(outgoing[:, 2 * axis_pos], axis, up=False))
        incoming.append(shift(outgoing[:, 2 * axis_pos + 1], axis, up=True))
    slots = jnp.concatenate(incoming, axis=1)

    own, zslots = local_solve(parent, residual, slots, diag_inverse, coupling)

    returned = []
    for axis_pos, axis in enumerate(AXES):
        lo = zslots[:, (2 * axis_pos) * face_w : (2 * axis_pos + 1) * face_w]
        hi = zslots[:, (2 * axis_pos + 1) * face_w : (2 * axis_pos + 2) * face_w]
        returned.append(shift(lo, axis, up=True))
        returned.append(shift(hi, axis, up=False))
    returned = jnp.concatenate(returned, axis=1)
    onehot = (
        send_rows.reshape(slots_n * face_w, 1) == lax.iota(jnp.int32, owned_n)[None, :]
    ).astype(jnp.bfloat16)
    faces = jnp.dot(returned, onehot, preferred_element_type=jnp.float32)
    coarse = lax.dot_general(
        solved_t,
        vectors,
        (((0,), (0,)), ((), ())),
        precision=lax.Precision.HIGHEST,
        preferred_element_type=jnp.float32,
    )
    return own.astype(jnp.float32) + faces + coarse


def solution(mesh):
    return jax.shard_map(
        per_device,
        mesh=mesh,
        in_specs=(
            P(None, AXES),
            P(AXES, None, None),
            P(AXES, None, None),
            P(AXES),
            P(AXES, None),
            P(AXES),
            P(None, AXES),
            P(AXES, None),
        ),
        out_specs=P(None, AXES),
        check_vma=False,
    )
```

```python
import functools

import jax
import jax.numpy as jnp
from jax import lax
from jax.experimental import pallas as pl
from jax.experimental.pallas import tpu as pltpu
from jax.sharding import PartitionSpec as P

AXES = ("gx", "gy", "gz")
NT = (((1,), (1,)), ((), ()))


def solve_kernel(
    parent_ref, res_ref, slot_ref, inv_hbm, cpl_hbm, own_ref, zslot_ref,
    inv_ref, cpl_ref, sems, y_ref, carry_ref,
):
    blocks_n, block_w, _ = inv_ref.shape
    inv_copies, cpl_copies = [], []
    for b in range(blocks_n):
        if b > 0:
            cpl_copies.append(
                pltpu.make_async_copy(cpl_hbm.at[b - 1], cpl_ref.at[b - 1], sems.at[blocks_n + b - 1])
            )
            cpl_copies[-1].start()
        inv_copies.append(pltpu.make_async_copy(inv_hbm.at[b], inv_ref.at[b], sems.at[b]))
        inv_copies[-1].start()
    owned_blocks = res_ref.shape[1] // block_w

    def columns(b):
        if b < owned_blocks:
            return res_ref, pl.ds(b * block_w, block_w)
        return slot_ref, pl.ds((b - owned_blocks) * block_w, block_w)

    def link(b):
        return jnp.clip(parent_ref[b], 0, blocks_n - 1)

    for b in range(blocks_n):
        ref, cols = columns(b)
        x = ref[:, cols]
        if b == 0:
            lower = x.astype(jnp.bfloat16)
        else:
            cpl_copies[b - 1].wait()
            prior = y_ref[link(b)]
            lower = (
                x - lax.dot_general(prior, cpl_ref[b - 1], NT, preferred_element_type=jnp.float32)
            ).astype(jnp.bfloat16)
        inv_copies[b].wait()
        y_ref[b] = lax.dot_general(
            lower, inv_ref[b], NT, preferred_element_type=jnp.float32
        ).astype(jnp.bfloat16)

    carry_ref[...] = jnp.zeros(carry_ref.shape, carry_ref.dtype)
    for b in reversed(range(blocks_n)):
        upper = (y_ref[b].astype(jnp.float32) - carry_ref[b]).astype(jnp.bfloat16)
        result = jnp.dot(upper, inv_ref[b], preferred_element_type=jnp.float32).astype(jnp.bfloat16)
        if b < owned_blocks:
            own_ref[:, pl.ds(b * block_w, block_w)] = result
        else:
            zslot_ref[:, pl.ds((b - owned_blocks) * block_w, block_w)] = result
        if b > 0:
            push = jnp.dot(result, cpl_ref[b - 1], preferred_element_type=jnp.float32)
            p = link(b)
            carry_ref[p] = carry_ref[p] + push


def local_solve(parent, residual, slots, diag_inverse, coupling):
    nrhs_here, owned_n = residual.shape
    blocks_n, block_w, _ = diag_inverse.shape
    vmem = pltpu.VMEM
    return pl.pallas_call(
        solve_kernel,
        out_shape=(
            jax.ShapeDtypeStruct((nrhs_here, owned_n), jnp.bfloat16),
            jax.ShapeDtypeStruct(slots.shape, jnp.bfloat16),
        ),
        in_specs=[
            pl.BlockSpec(memory_space=pltpu.SMEM),
            pl.BlockSpec(memory_space=vmem),
            pl.BlockSpec(memory_space=vmem),
            pl.BlockSpec(memory_space=pl.ANY),
            pl.BlockSpec(memory_space=pl.ANY),
        ],
        out_specs=(pl.BlockSpec(memory_space=vmem), pl.BlockSpec(memory_space=vmem)),
        scratch_shapes=[
            pltpu.VMEM(diag_inverse.shape, diag_inverse.dtype),
            pltpu.VMEM(coupling.shape, coupling.dtype),
            pltpu.SemaphoreType.DMA((2 * blocks_n - 1,)),
            pltpu.VMEM((blocks_n, nrhs_here, block_w), jnp.bfloat16),
            pltpu.VMEM((blocks_n, nrhs_here, block_w), jnp.float32),
        ],
        compiler_params=pltpu.CompilerParams(vmem_limit_bytes=48 * 1024 * 1024),
    )(parent, residual, slots, diag_inverse, coupling)


def shift(value, axis, up):
    count = lax.axis_size(axis)
    if up:
        pairs = [(i, i + 1) for i in range(count - 1)]
    else:
        pairs = [(i + 1, i) for i in range(count - 1)]
    return lax.ppermute(value, axis, pairs)


def gather_axis(held, axis, dim):
    count = lax.axis_size(axis)
    if count & (count - 1):
        return lax.all_gather(held, axis, axis=dim, tiled=True)
    me = lax.axis_index(axis)
    step = 1
    while step < count:
        pairs = [(i, i ^ step) for i in range(count)]
        other = lax.ppermute(held, axis, pairs)
        low = (me // step) % 2 == 0
        held = jnp.where(
            low,
            jnp.concatenate([held, other], axis=dim),
            jnp.concatenate([other, held], axis=dim),
        )
        step *= 2
    return held


def gather_all(value):
    held = value.reshape((1,) * len(AXES) + value.shape)
    for dim, axis in enumerate(AXES):
        held = gather_axis(held, axis, dim)
    return held

def per_device(
    residual, diag_inverse, coupling, parent, send_rows, counts, deflation, coarse_inverse
):
    nrhs_here, owned_n = residual.shape
    slots_n, face_w = send_rows.shape
    kmax_here = deflation.shape[0]
    mask = (lax.iota(jnp.int32, kmax_here) < counts[0]).astype(jnp.float32)
    vectors = deflation * mask[:, None]
    coeffs_t = lax.dot_general(
        vectors, residual, NT, precision=lax.Precision.HIGHEST, preferred_element_type=jnp.float32
    )
    gathered = gather_all(coeffs_t).reshape(-1, coeffs_t.shape[1])
    solved_t = jnp.dot(
        coarse_inverse, gathered, precision=lax.Precision.HIGHEST, preferred_element_type=jnp.float32
    )

    outgoing = jnp.take(residual, send_rows, axis=1)
    incoming = []
    for axis_pos, axis in enumerate(AXES):
        incoming.append(shift(outgoing[:, 2 * axis_pos], axis, up=False))
        incoming.append(shift(outgoing[:, 2 * axis_pos + 1], axis, up=True))
    slots = jnp.concatenate(incoming, axis=1)

    own, zslots = local_solve(parent, residual, slots, diag_inverse, coupling)

    returned = []
    for axis_pos, axis in enumerate(AXES):
        lo = zslots[:, (2 * axis_pos) * face_w : (2 * axis_pos + 1) * face_w]
        hi = zslots[:, (2 * axis_pos + 1) * face_w : (2 * axis_pos + 2) * face_w]
        returned.append(shift(lo, axis, up=True))
        returned.append(shift(hi, axis, up=False))
    returned = jnp.concatenate(returned, axis=1)
    onehot = (
        send_rows.reshape(slots_n * face_w, 1) == lax.iota(jnp.int32, owned_n)[None, :]
    ).astype(jnp.bfloat16)
    faces = jnp.dot(returned, onehot, preferred_element_type=jnp.float32)
    coarse = lax.dot_general(
        solved_t,
        vectors,
        (((0,), (0,)), ((), ())),
        precision=lax.Precision.HIGHEST,
        preferred_element_type=jnp.float32,
    )
    return own.astype(jnp.float32) + faces + coarse


def solution(mesh):
    return jax.shard_map(
        per_device,
        mesh=mesh,
        in_specs=(
            P(None, AXES),
            P(AXES, None, None),
            P(AXES, None, None),
            P(AXES),
            P(AXES, None),
            P(AXES),
            P(None, AXES),
            P(AXES, None),
        ),
        out_specs=P(None, AXES),
        check_vma=False,
    )
```

```python
import functools

import jax
import jax.numpy as jnp
from jax import lax
from jax.experimental import pallas as pl
from jax.experimental.pallas import tpu as pltpu
from jax.sharding import PartitionSpec as P

AXES = ("gx", "gy", "gz")
NT = (((1,), (1,)), ((), ()))


def solve_kernel(parent_ref, res_ref, slot_ref, inv_ref, cpl_ref, own_ref, zslot_ref, y_ref, carry_ref):
    blocks_n, block_w, _ = inv_ref.shape
    owned_blocks = res_ref.shape[1] // block_w

    def columns(b):
        if b < owned_blocks:
            return res_ref, pl.ds(b * block_w, block_w)
        return slot_ref, pl.ds((b - owned_blocks) * block_w, block_w)

    def link(b):
        return jnp.clip(parent_ref[b], 0, blocks_n - 1)

    for b in range(blocks_n):
        ref, cols = columns(b)
        x = ref[:, cols]
        if b == 0:
            lower = x.astype(jnp.bfloat16)
        else:
            prior = y_ref[link(b)]
            lower = (
                x - lax.dot_general(prior, cpl_ref[b - 1], NT, preferred_element_type=jnp.float32)
            ).astype(jnp.bfloat16)
        y_ref[b] = lax.dot_general(
            lower, inv_ref[b], NT, preferred_element_type=jnp.float32
        ).astype(jnp.bfloat16)

    carry_ref[...] = jnp.zeros(carry_ref.shape, carry_ref.dtype)
    for b in reversed(range(blocks_n)):
        upper = (y_ref[b].astype(jnp.float32) - carry_ref[b]).astype(jnp.bfloat16)
        result = jnp.dot(upper, inv_ref[b], preferred_element_type=jnp.float32).astype(jnp.bfloat16)
        if b < owned_blocks:
            own_ref[:, pl.ds(b * block_w, block_w)] = result
        else:
            zslot_ref[:, pl.ds((b - owned_blocks) * block_w, block_w)] = result
        if b > 0:
            push = jnp.dot(result, cpl_ref[b - 1], preferred_element_type=jnp.float32)
            p = link(b)
            carry_ref[p] = carry_ref[p] + push


def local_solve(parent, residual, slots, diag_inverse, coupling):
    nrhs_here, owned_n = residual.shape
    blocks_n, block_w, _ = diag_inverse.shape
    vmem = pltpu.VMEM
    return pl.pallas_call(
        solve_kernel,
        out_shape=(
            jax.ShapeDtypeStruct((nrhs_here, owned_n), jnp.bfloat16),
            jax.ShapeDtypeStruct(slots.shape, jnp.bfloat16),
        ),
        in_specs=[
            pl.BlockSpec(memory_space=pltpu.SMEM),
            pl.BlockSpec(memory_space=vmem),
            pl.BlockSpec(memory_space=vmem),
            pl.BlockSpec(memory_space=vmem),
            pl.BlockSpec(memory_space=vmem),
        ],
        out_specs=(pl.BlockSpec(memory_space=vmem), pl.BlockSpec(memory_space=vmem)),
        scratch_shapes=[
            pltpu.VMEM((blocks_n, nrhs_here, block_w), jnp.bfloat16),
            pltpu.VMEM((blocks_n, nrhs_here, block_w), jnp.float32),
        ],
        compiler_params=pltpu.CompilerParams(vmem_limit_bytes=48 * 1024 * 1024),
    )(parent, residual, slots, diag_inverse, coupling)


def matchings(count):
    first = [(i, i + 1) for i in range(0, count - 1, 2)] + [(i + 1, i) for i in range(0, count - 1, 2)]
    second = [(i, i + 1) for i in range(1, count - 1, 2)] + [(i + 1, i) for i in range(1, count - 1, 2)]
    return first, second


def swap(value, axis, pairs, extra=None):
    if not pairs:
        return jnp.zeros_like(value), None
    if extra is None:
        return lax.ppermute(value, axis, pairs), None
    rows = value.shape[0]
    packed = jnp.concatenate([value.astype(extra.dtype), extra], axis=0)
    got = lax.ppermute(packed, axis, pairs)
    return got[:rows].astype(value.dtype), got[rows:]


def halo_out(down, up, axis, extra=None):
    even = lax.axis_index(axis) % 2 == 0
    first, second = matchings(lax.axis_size(axis))
    r1, got = swap(jnp.where(even, up, down), axis, first, extra)
    r2, _ = swap(jnp.where(even, down, up), axis, second)
    return jnp.where(even, r1, r2), jnp.where(even, r2, r1), got


def halo_back(lo, hi, axis, extra=None):
    even = lax.axis_index(axis) % 2 == 0
    first, second = matchings(lax.axis_size(axis))
    r1, got = swap(jnp.where(even, lo, hi), axis, first, extra)
    r2, _ = swap(jnp.where(even, hi, lo), axis, second)
    return jnp.where(even, r2, r1), jnp.where(even, r1, r2), got


def doubling(axis):
    count = lax.axis_size(axis)
    return count > 1 and not count & (count - 1)


def merge(held, other, axis, dim, step):
    low = (lax.axis_index(axis) // step) % 2 == 0
    return jnp.where(
        low,
        jnp.concatenate([held, other], axis=dim),
        jnp.concatenate([other, held], axis=dim),
    )


def gather_axis(held, axis, dim, step=1):
    count = lax.axis_size(axis)
    if not doubling(axis):
        return lax.all_gather(held, axis, axis=dim, tiled=True)
    while step < count:
        pairs = [(i, i ^ step) for i in range(count)]
        held = merge(held, lax.ppermute(held, axis, pairs), axis, dim, step)
        step *= 2
    return held


def rows_of(held):
    return held.reshape(-1, held.shape[-1])


def per_device(
    residual, diag_inverse, coupling, parent, send_rows, counts, deflation, coarse_inverse
):
    nrhs_here, owned_n = residual.shape
    slots_n, face_w = send_rows.shape
    kmax_here = deflation.shape[0]
    mask = (lax.iota(jnp.int32, kmax_here) < counts[0]).astype(jnp.float32)
    vectors = deflation * mask[:, None]
    coeffs_t = lax.dot_general(
        vectors, residual, NT, precision=lax.Precision.HIGHEST, preferred_element_type=jnp.float32
    )
    held = coeffs_t.reshape((1,) * len(AXES) + coeffs_t.shape)

    outgoing = jnp.take(residual, send_rows, axis=1)
    incoming = []
    for axis_pos, axis in enumerate(AXES):
        ride = axis_pos == 0 and doubling(axis)
        low, high, got = halo_out(
            outgoing[:, 2 * axis_pos],
            outgoing[:, 2 * axis_pos + 1],
            axis,
            rows_of(held) if ride else None,
        )
        incoming += [low, high]
        if axis_pos == 0:
            if ride:
                held = gather_axis(merge(held, got.reshape(held.shape), axis, 0, 1), axis, 0, 2)
            else:
                held = gather_axis(held, axis, 0)
    for axis_pos in range(1, len(AXES) - 1):
        held = gather_axis(held, AXES[axis_pos], axis_pos)
    last = len(AXES) - 1
    late = lax.axis_size(AXES[last]) == 2
    if not late:
        held = gather_axis(held, AXES[last], last)
    slots = jnp.concatenate(incoming, axis=1)

    own, zslots = local_solve(parent, residual, slots, diag_inverse, coupling)

    returned = []
    for axis_pos, axis in enumerate(AXES):
        ride = axis_pos == last and late
        low, high, got = halo_back(
            zslots[:, (2 * axis_pos) * face_w : (2 * axis_pos + 1) * face_w],
            zslots[:, (2 * axis_pos + 1) * face_w : (2 * axis_pos + 2) * face_w],
            axis,
            rows_of(held) if ride else None,
        )
        returned += [low, high]
        if ride:
            held = merge(held, got.reshape(held.shape), axis, last, 1)
    returned = jnp.concatenate(returned, axis=1)

    solved_t = jnp.dot(
        coarse_inverse, rows_of(held), precision=lax.Precision.HIGHEST, preferred_element_type=jnp.float32
    )
    onehot = (
        send_rows.reshape(slots_n * face_w, 1) == lax.iota(jnp.int32, owned_n)[None, :]
    ).astype(jnp.bfloat16)
    faces = jnp.dot(returned, onehot, preferred_element_type=jnp.float32)
    coarse = lax.dot_general(
        solved_t,
        vectors,
        (((0,), (0,)), ((), ())),
        precision=lax.Precision.HIGHEST,
        preferred_element_type=jnp.float32,
    )
    return own.astype(jnp.float32) + faces + coarse


def solution(mesh):
    return jax.shard_map(
        per_device,
        mesh=mesh,
        in_specs=(
            P(None, AXES),
            P(AXES, None, None),
            P(AXES, None, None),
            P(AXES),
            P(AXES, None),
            P(AXES),
            P(None, AXES),
            P(AXES, None),
        ),
        out_specs=P(None, AXES),
        check_vma=False,
    )
```

```python
import functools

import jax
import jax.numpy as jnp
from jax import lax
from jax.experimental import pallas as pl
from jax.experimental.pallas import tpu as pltpu
from jax.sharding import PartitionSpec as P

AXES = ("gx", "gy", "gz")
NT = (((1,), (1,)), ((), ()))


def solve_kernel(
    parent_ref, res_ref, slot_ref, inv_ref, cpl_ref, after_ref, own_ref, zslot_ref, y_ref, carry_ref
):
    del after_ref
    blocks_n, block_w, _ = inv_ref.shape
    owned_blocks = res_ref.shape[1] // block_w

    def columns(b):
        if b < owned_blocks:
            return res_ref, pl.ds(b * block_w, block_w)
        return slot_ref, pl.ds((b - owned_blocks) * block_w, block_w)

    def link(b):
        return jnp.clip(parent_ref[b], 0, blocks_n - 1)

    for b in range(blocks_n):
        ref, cols = columns(b)
        x = ref[:, cols]
        if b == 0:
            lower = x.astype(jnp.bfloat16)
        else:
            prior = y_ref[link(b)]
            lower = (
                x - lax.dot_general(prior, cpl_ref[b - 1], NT, preferred_element_type=jnp.float32)
            ).astype(jnp.bfloat16)
        y_ref[b] = lax.dot_general(
            lower, inv_ref[b], NT, preferred_element_type=jnp.float32
        ).astype(jnp.bfloat16)

    carry_ref[...] = jnp.zeros(carry_ref.shape, carry_ref.dtype)
    for b in reversed(range(blocks_n)):
        upper = (y_ref[b].astype(jnp.float32) - carry_ref[b]).astype(jnp.bfloat16)
        result = jnp.dot(upper, inv_ref[b], preferred_element_type=jnp.float32).astype(jnp.bfloat16)
        if b < owned_blocks:
            own_ref[:, pl.ds(b * block_w, block_w)] = result
        else:
            zslot_ref[:, pl.ds((b - owned_blocks) * block_w, block_w)] = result
        if b > 0:
            push = jnp.dot(result, cpl_ref[b - 1], preferred_element_type=jnp.float32)
            p = link(b)
            carry_ref[p] = carry_ref[p] + push


def local_solve(parent, residual, slots, diag_inverse, coupling, after):
    nrhs_here, owned_n = residual.shape
    blocks_n, block_w, _ = diag_inverse.shape
    vmem = pltpu.VMEM
    return pl.pallas_call(
        solve_kernel,
        out_shape=(
            jax.ShapeDtypeStruct((nrhs_here, owned_n), jnp.bfloat16),
            jax.ShapeDtypeStruct(slots.shape, jnp.bfloat16),
        ),
        in_specs=[
            pl.BlockSpec(memory_space=pltpu.SMEM),
            pl.BlockSpec(memory_space=vmem),
            pl.BlockSpec(memory_space=vmem),
            pl.BlockSpec(memory_space=vmem),
            pl.BlockSpec(memory_space=vmem),
            pl.BlockSpec(memory_space=pl.ANY),
        ],
        out_specs=(pl.BlockSpec(memory_space=vmem), pl.BlockSpec(memory_space=vmem)),
        scratch_shapes=[
            pltpu.VMEM((blocks_n, nrhs_here, block_w), jnp.bfloat16),
            pltpu.VMEM((blocks_n, nrhs_here, block_w), jnp.float32),
        ],
        compiler_params=pltpu.CompilerParams(vmem_limit_bytes=48 * 1024 * 1024),
    )(parent, residual, slots, diag_inverse, coupling, after)


def matchings(count):
    first = [(i, i + 1) for i in range(0, count - 1, 2)] + [(i + 1, i) for i in range(0, count - 1, 2)]
    second = [(i, i + 1) for i in range(1, count - 1, 2)] + [(i + 1, i) for i in range(1, count - 1, 2)]
    return first, second


def swap(value, axis, pairs, extra=None):
    if not pairs:
        return jnp.zeros_like(value), None
    if extra is None:
        return lax.ppermute(value, axis, pairs), None
    rows = value.shape[0]
    packed = jnp.concatenate([value.astype(extra.dtype), extra], axis=0)
    got = lax.ppermute(packed, axis, pairs)
    return got[:rows].astype(value.dtype), got[rows:]


def halo_out(down, up, axis, extra=None):
    even = lax.axis_index(axis) % 2 == 0
    first, second = matchings(lax.axis_size(axis))
    r1, got = swap(jnp.where(even, up, down), axis, first, extra)
    r2, _ = swap(jnp.where(even, down, up), axis, second)
    return jnp.where(even, r1, r2), jnp.where(even, r2, r1), got


def halo_back(lo, hi, axis, extra=None):
    even = lax.axis_index(axis) % 2 == 0
    first, second = matchings(lax.axis_size(axis))
    r1, got = swap(jnp.where(even, lo, hi), axis, first, extra)
    r2, _ = swap(jnp.where(even, hi, lo), axis, second)
    return jnp.where(even, r2, r1), jnp.where(even, r1, r2), got


def doubling(axis):
    count = lax.axis_size(axis)
    return count > 1 and not count & (count - 1)


def merge(held, other, axis, dim, step):
    low = (lax.axis_index(axis) // step) % 2 == 0
    return jnp.where(
        low,
        jnp.concatenate([held, other], axis=dim),
        jnp.concatenate([other, held], axis=dim),
    )


def gather_axis(held, axis, dim, step=1):
    count = lax.axis_size(axis)
    if not doubling(axis):
        return lax.all_gather(held, axis, axis=dim, tiled=True)
    while step < count:
        pairs = [(i, i ^ step) for i in range(count)]
        held = merge(held, lax.ppermute(held, axis, pairs), axis, dim, step)
        step *= 2
    return held


def rows_of(held):
    return held.reshape(-1, held.shape[-1])


def per_device(
    residual, diag_inverse, coupling, parent, send_rows, counts, deflation, coarse_inverse
):
    nrhs_here, owned_n = residual.shape
    slots_n, face_w = send_rows.shape
    kmax_here = deflation.shape[0]
    mask = (lax.iota(jnp.int32, kmax_here) < counts[0]).astype(jnp.float32)
    vectors = deflation * mask[:, None]
    coeffs_t = lax.dot_general(
        vectors, residual, NT, precision=lax.Precision.HIGHEST, preferred_element_type=jnp.float32
    )
    held = coeffs_t.reshape((1,) * len(AXES) + coeffs_t.shape)

    outgoing = jnp.take(residual, send_rows, axis=1)
    incoming = []
    for axis_pos, axis in enumerate(AXES):
        ride = axis_pos == 0 and doubling(axis)
        low, high, got = halo_out(
            outgoing[:, 2 * axis_pos],
            outgoing[:, 2 * axis_pos + 1],
            axis,
            rows_of(held) if ride else None,
        )
        incoming += [low, high]
        if axis_pos == 0:
            if ride:
                held = gather_axis(merge(held, got.reshape(held.shape), axis, 0, 1), axis, 0, 2)
            else:
                held = gather_axis(held, axis, 0)
    after = held
    for axis_pos in range(1, len(AXES) - 1):
        axis = AXES[axis_pos]
        if doubling(axis):
            held = merge(held, lax.ppermute(held, axis, matchings(lax.axis_size(axis))[0]), axis, axis_pos, 1)
            after = held
            held = gather_axis(held, axis, axis_pos, 2)
        else:
            held = gather_axis(held, axis, axis_pos)
    last = len(AXES) - 1
    late = lax.axis_size(AXES[last]) == 2
    if not late:
        held = gather_axis(held, AXES[last], last)
    slots = jnp.concatenate(incoming, axis=1)

    own, zslots = local_solve(parent, residual, slots, diag_inverse, coupling, after)

    returned = []
    for axis_pos, axis in enumerate(AXES):
        ride = axis_pos == last and late
        low, high, got = halo_back(
            zslots[:, (2 * axis_pos) * face_w : (2 * axis_pos + 1) * face_w],
            zslots[:, (2 * axis_pos + 1) * face_w : (2 * axis_pos + 2) * face_w],
            axis,
            rows_of(held) if ride else None,
        )
        returned += [low, high]
        if ride:
            held = merge(held, got.reshape(held.shape), axis, last, 1)
    returned = jnp.concatenate(returned, axis=1)

    solved_t = jnp.dot(
        coarse_inverse, rows_of(held), precision=lax.Precision.HIGHEST, preferred_element_type=jnp.float32
    )
    onehot = (
        send_rows.reshape(slots_n * face_w, 1) == lax.iota(jnp.int32, owned_n)[None, :]
    ).astype(jnp.bfloat16)
    faces = jnp.dot(returned, onehot, preferred_element_type=jnp.float32)
    coarse = lax.dot_general(
        solved_t,
        vectors,
        (((0,), (0,)), ((), ())),
        precision=lax.Precision.HIGHEST,
        preferred_element_type=jnp.float32,
    )
    return own.astype(jnp.float32) + faces + coarse


def solution(mesh):
    return jax.shard_map(
        per_device,
        mesh=mesh,
        in_specs=(
            P(None, AXES),
            P(AXES, None, None),
            P(AXES, None, None),
            P(AXES),
            P(AXES, None),
            P(AXES),
            P(None, AXES),
            P(AXES, None),
        ),
        out_specs=P(None, AXES),
        check_vma=False,
    )
```

```python
import functools

import jax
import jax.numpy as jnp
from jax import lax
from jax.experimental import pallas as pl
from jax.experimental.pallas import tpu as pltpu
from jax.sharding import PartitionSpec as P

AXES = ("gx", "gy", "gz")
NT = (((1,), (1,)), ((), ()))


def solve_kernel(
    parent_ref, res_ref, slot_ref, inv_ref, cpl_ref, after_ref, own_ref, zslot_ref, y_ref, carry_ref
):
    del after_ref
    blocks_n, block_w, _ = inv_ref.shape
    owned_blocks = res_ref.shape[1] // block_w

    def columns(b):
        if b < owned_blocks:
            return res_ref, pl.ds(b * block_w, block_w)
        return slot_ref, pl.ds((b - owned_blocks) * block_w, block_w)

    def link(b):
        return jnp.clip(parent_ref[b], 0, blocks_n - 1)

    for b in range(blocks_n):
        ref, cols = columns(b)
        x = ref[:, cols]
        if b == 0:
            lower = x.astype(jnp.bfloat16)
        else:
            prior = y_ref[link(b)]
            lower = (
                x - lax.dot_general(prior, cpl_ref[b - 1], NT, preferred_element_type=jnp.float32)
            ).astype(jnp.bfloat16)
        y_ref[b] = lax.dot_general(
            lower, inv_ref[b], NT, preferred_element_type=jnp.float32
        ).astype(jnp.bfloat16)

    carry_ref[...] = jnp.zeros(carry_ref.shape, carry_ref.dtype)
    for b in reversed(range(blocks_n)):
        upper = (y_ref[b].astype(jnp.float32) - carry_ref[b]).astype(jnp.bfloat16)
        result = jnp.dot(upper, inv_ref[b], preferred_element_type=jnp.float32).astype(jnp.bfloat16)
        if b < owned_blocks:
            own_ref[:, pl.ds(b * block_w, block_w)] = result
        else:
            zslot_ref[:, pl.ds((b - owned_blocks) * block_w, block_w)] = result
        if b > 0:
            push = jnp.dot(result, cpl_ref[b - 1], preferred_element_type=jnp.float32)
            p = link(b)
            carry_ref[p] = carry_ref[p] + push


def local_solve(parent, residual, slots, diag_inverse, coupling, after):
    nrhs_here, owned_n = residual.shape
    blocks_n, block_w, _ = diag_inverse.shape
    vmem = pltpu.VMEM
    return pl.pallas_call(
        solve_kernel,
        out_shape=(
            jax.ShapeDtypeStruct((nrhs_here, owned_n), jnp.bfloat16),
            jax.ShapeDtypeStruct(slots.shape, jnp.bfloat16),
        ),
        in_specs=[
            pl.BlockSpec(memory_space=pltpu.SMEM),
            pl.BlockSpec(memory_space=vmem),
            pl.BlockSpec(memory_space=vmem),
            pl.BlockSpec(memory_space=vmem),
            pl.BlockSpec(memory_space=vmem),
            pl.BlockSpec(memory_space=pl.ANY),
        ],
        out_specs=(pl.BlockSpec(memory_space=vmem), pl.BlockSpec(memory_space=vmem)),
        scratch_shapes=[
            pltpu.VMEM((blocks_n, nrhs_here, block_w), jnp.bfloat16),
            pltpu.VMEM((blocks_n, nrhs_here, block_w), jnp.float32),
        ],
        compiler_params=pltpu.CompilerParams(vmem_limit_bytes=48 * 1024 * 1024),
    )(parent, residual, slots, diag_inverse, coupling, after)


def matchings(count):
    first = [(i, i + 1) for i in range(0, count - 1, 2)] + [(i + 1, i) for i in range(0, count - 1, 2)]
    second = [(i, i + 1) for i in range(1, count - 1, 2)] + [(i + 1, i) for i in range(1, count - 1, 2)]
    return first, second


def swap(value, axis, pairs, extra=None):
    if not pairs:
        return jnp.zeros_like(value), None
    if extra is None:
        return lax.ppermute(value, axis, pairs), None
    rows = value.shape[0]
    packed = jnp.concatenate([value.astype(extra.dtype), extra], axis=0)
    got = lax.ppermute(packed, axis, pairs)
    return got[:rows].astype(value.dtype), got[rows:]


def halo_out(down, up, axis, extra=None):
    even = lax.axis_index(axis) % 2 == 0
    first, second = matchings(lax.axis_size(axis))
    r1, got = swap(jnp.where(even, up, down), axis, first, extra)
    r2, _ = swap(jnp.where(even, down, up), axis, second)
    return jnp.where(even, r1, r2), jnp.where(even, r2, r1), got


def halo_back(lo, hi, axis, extra=None):
    even = lax.axis_index(axis) % 2 == 0
    first, second = matchings(lax.axis_size(axis))
    r1, got = swap(jnp.where(even, lo, hi), axis, first, extra)
    r2, _ = swap(jnp.where(even, hi, lo), axis, second)
    return jnp.where(even, r2, r1), jnp.where(even, r1, r2), got


def doubling(axis):
    count = lax.axis_size(axis)
    return count > 1 and not count & (count - 1)


def merge(held, other, axis, dim, step):
    low = (lax.axis_index(axis) // step) % 2 == 0
    return jnp.where(
        low,
        jnp.concatenate([held, other], axis=dim),
        jnp.concatenate([other, held], axis=dim),
    )


def gather_axis(held, axis, dim, step=1):
    count = lax.axis_size(axis)
    if not doubling(axis):
        return lax.all_gather(held, axis, axis=dim, tiled=True)
    while step < count:
        pairs = [(i, i ^ step) for i in range(count)]
        held = merge(held, lax.ppermute(held, axis, pairs), axis, dim, step)
        step *= 2
    return held


def rows_of(held):
    return held.reshape(-1, held.shape[-1])


def per_device(
    residual, diag_inverse, coupling, parent, send_rows, counts, deflation, coarse_inverse
):
    nrhs_here, owned_n = residual.shape
    slots_n, face_w = send_rows.shape
    kmax_here = deflation.shape[0]
    mask = (lax.iota(jnp.int32, kmax_here) < counts[0]).astype(jnp.float32)
    vectors = deflation * mask[:, None]
    coeffs_t = lax.dot_general(
        vectors, residual, NT, precision=lax.Precision.HIGHEST, preferred_element_type=jnp.float32
    )
    total_dev = coarse_inverse.shape[1] // kmax_here
    spread = jnp.broadcast_to(coeffs_t[None], (total_dev,) + coeffs_t.shape)
    held = lax.all_to_all(spread, AXES, 0, 0, tiled=True)

    outgoing = jnp.take(residual, send_rows, axis=1)
    incoming = []
    for axis_pos, axis in enumerate(AXES):
        low, high, _ = halo_out(outgoing[:, 2 * axis_pos], outgoing[:, 2 * axis_pos + 1], axis)
        incoming += [low, high]
    slots = jnp.concatenate(incoming, axis=1)
    after = coeffs_t

    own, zslots = local_solve(parent, residual, slots, diag_inverse, coupling, after)

    returned = []
    for axis_pos, axis in enumerate(AXES):
        low, high, _ = halo_back(
            zslots[:, (2 * axis_pos) * face_w : (2 * axis_pos + 1) * face_w],
            zslots[:, (2 * axis_pos + 1) * face_w : (2 * axis_pos + 2) * face_w],
            axis,
        )
        returned += [low, high]
    returned = jnp.concatenate(returned, axis=1)

    solved_t = jnp.dot(
        coarse_inverse, rows_of(held), precision=lax.Precision.HIGHEST, preferred_element_type=jnp.float32
    )
    onehot = (
        send_rows.reshape(slots_n * face_w, 1) == lax.iota(jnp.int32, owned_n)[None, :]
    ).astype(jnp.bfloat16)
    faces = jnp.dot(returned, onehot, preferred_element_type=jnp.float32)
    coarse = lax.dot_general(
        solved_t,
        vectors,
        (((0,), (0,)), ((), ())),
        precision=lax.Precision.HIGHEST,
        preferred_element_type=jnp.float32,
    )
    return own.astype(jnp.float32) + faces + coarse


def solution(mesh):
    return jax.shard_map(
        per_device,
        mesh=mesh,
        in_specs=(
            P(None, AXES),
            P(AXES, None, None),
            P(AXES, None, None),
            P(AXES),
            P(AXES, None),
            P(AXES),
            P(None, AXES),
            P(AXES, None),
        ),
        out_specs=P(None, AXES),
        check_vma=False,
    )
```

```python
import functools

import jax
import jax.numpy as jnp
from jax import lax
from jax.experimental import pallas as pl
from jax.experimental.pallas import tpu as pltpu
from jax.sharding import PartitionSpec as P

AXES = ("gx", "gy", "gz")
NT = (((1,), (1,)), ((), ()))


def solve_kernel(
    parent_ref, res_ref, slot_ref, inv_ref, cpl_ref, after_ref, own_ref, zslot_ref, y_ref, carry_ref
):
    del after_ref
    blocks_n, block_w, _ = inv_ref.shape
    owned_blocks = res_ref.shape[1] // block_w

    def columns(b):
        if b < owned_blocks:
            return res_ref, pl.ds(b * block_w, block_w)
        return slot_ref, pl.ds((b - owned_blocks) * block_w, block_w)

    def link(b):
        return jnp.clip(parent_ref[b], 0, blocks_n - 1)

    for b in range(blocks_n):
        ref, cols = columns(b)
        x = ref[:, cols]
        if b == 0:
            lower = x.astype(jnp.bfloat16)
        else:
            prior = y_ref[link(b)]
            lower = (
                x - lax.dot_general(prior, cpl_ref[b - 1], NT, preferred_element_type=jnp.float32)
            ).astype(jnp.bfloat16)
        y_ref[b] = lax.dot_general(
            lower, inv_ref[b], NT, preferred_element_type=jnp.float32
        ).astype(jnp.bfloat16)

    carry_ref[...] = jnp.zeros(carry_ref.shape, carry_ref.dtype)
    for b in reversed(range(blocks_n)):
        upper = (y_ref[b].astype(jnp.float32) - carry_ref[b]).astype(jnp.bfloat16)
        result = jnp.dot(upper, inv_ref[b], preferred_element_type=jnp.float32).astype(jnp.bfloat16)
        if b < owned_blocks:
            own_ref[:, pl.ds(b * block_w, block_w)] = result
        else:
            zslot_ref[:, pl.ds((b - owned_blocks) * block_w, block_w)] = result
        if b > 0:
            push = jnp.dot(result, cpl_ref[b - 1], preferred_element_type=jnp.float32)
            p = link(b)
            carry_ref[p] = carry_ref[p] + push


def local_solve(parent, residual, slots, diag_inverse, coupling, after):
    nrhs_here, owned_n = residual.shape
    blocks_n, block_w, _ = diag_inverse.shape
    vmem = pltpu.VMEM
    return pl.pallas_call(
        solve_kernel,
        out_shape=(
            jax.ShapeDtypeStruct((nrhs_here, owned_n), jnp.bfloat16),
            jax.ShapeDtypeStruct(slots.shape, jnp.bfloat16),
        ),
        in_specs=[
            pl.BlockSpec(memory_space=pltpu.SMEM),
            pl.BlockSpec(memory_space=vmem),
            pl.BlockSpec(memory_space=vmem),
            pl.BlockSpec(memory_space=vmem),
            pl.BlockSpec(memory_space=vmem),
            pl.BlockSpec(memory_space=pl.ANY),
        ],
        out_specs=(pl.BlockSpec(memory_space=vmem), pl.BlockSpec(memory_space=vmem)),
        scratch_shapes=[
            pltpu.VMEM((blocks_n, nrhs_here, block_w), jnp.bfloat16),
            pltpu.VMEM((blocks_n, nrhs_here, block_w), jnp.float32),
        ],
        compiler_params=pltpu.CompilerParams(vmem_limit_bytes=48 * 1024 * 1024),
        cost_estimate=pl.CostEstimate(
            flops=4 * (2 * blocks_n - 1) * nrhs_here * block_w * block_w,
            transcendentals=0,
            bytes_accessed=2 * (diag_inverse.size + coupling.size) + 6 * residual.size,
        ),
    )(parent, residual, slots, diag_inverse, coupling, after)


def matchings(count):
    first = [(i, i + 1) for i in range(0, count - 1, 2)] + [(i + 1, i) for i in range(0, count - 1, 2)]
    second = [(i, i + 1) for i in range(1, count - 1, 2)] + [(i + 1, i) for i in range(1, count - 1, 2)]
    return first, second


def swap(value, axis, pairs, extra=None):
    if not pairs:
        return jnp.zeros_like(value), None
    if extra is None:
        return lax.ppermute(value, axis, pairs), None
    rows = value.shape[0]
    packed = jnp.concatenate([value.astype(extra.dtype), extra], axis=0)
    got = lax.ppermute(packed, axis, pairs)
    return got[:rows].astype(value.dtype), got[rows:]


def halo_out(down, up, axis, extra=None):
    even = lax.axis_index(axis) % 2 == 0
    first, second = matchings(lax.axis_size(axis))
    r1, got = swap(jnp.where(even, up, down), axis, first, extra)
    r2, _ = swap(jnp.where(even, down, up), axis, second)
    return jnp.where(even, r1, r2), jnp.where(even, r2, r1), got


def halo_back(lo, hi, axis, extra=None):
    even = lax.axis_index(axis) % 2 == 0
    first, second = matchings(lax.axis_size(axis))
    r1, got = swap(jnp.where(even, lo, hi), axis, first, extra)
    r2, _ = swap(jnp.where(even, hi, lo), axis, second)
    return jnp.where(even, r2, r1), jnp.where(even, r1, r2), got


def doubling(axis):
    count = lax.axis_size(axis)
    return count > 1 and not count & (count - 1)


def merge(held, other, axis, dim, step):
    low = (lax.axis_index(axis) // step) % 2 == 0
    return jnp.where(
        low,
        jnp.concatenate([held, other], axis=dim),
        jnp.concatenate([other, held], axis=dim),
    )


def gather_axis(held, axis, dim, step=1):
    count = lax.axis_size(axis)
    if not doubling(axis):
        return lax.all_gather(held, axis, axis=dim, tiled=True)
    while step < count:
        pairs = [(i, i ^ step) for i in range(count)]
        held = merge(held, lax.ppermute(held, axis, pairs), axis, dim, step)
        step *= 2
    return held


def rows_of(held):
    return held.reshape(-1, held.shape[-1])


def per_device(
    residual, diag_inverse, coupling, parent, send_rows, counts, deflation, coarse_inverse
):
    nrhs_here, owned_n = residual.shape
    slots_n, face_w = send_rows.shape
    kmax_here = deflation.shape[0]
    mask = (lax.iota(jnp.int32, kmax_here) < counts[0]).astype(jnp.float32)
    vectors = deflation * mask[:, None]
    coeffs_t = lax.dot_general(
        vectors, residual, NT, precision=lax.Precision.HIGHEST, preferred_element_type=jnp.float32
    )
    held = coeffs_t.reshape((1,) * len(AXES) + coeffs_t.shape)

    outgoing = jnp.take(residual, send_rows, axis=1)
    last = len(AXES) - 1
    late = lax.axis_size(AXES[last]) == 2
    incoming = []
    for axis_pos, axis in enumerate(AXES):
        ride = axis_pos < last and doubling(axis)
        low, high, got = halo_out(
            outgoing[:, 2 * axis_pos],
            outgoing[:, 2 * axis_pos + 1],
            axis,
            rows_of(held) if ride else None,
        )
        incoming += [low, high]
        if ride:
            held = gather_axis(merge(held, got.reshape(held.shape), axis, axis_pos, 1), axis, axis_pos, 2)
        elif axis_pos < last or not late:
            held = gather_axis(held, axis, axis_pos)
    after = coeffs_t
    slots = jnp.concatenate(incoming, axis=1)

    own, zslots = local_solve(parent, residual, slots, diag_inverse, coupling, after)

    returned = []
    for axis_pos, axis in enumerate(AXES):
        ride = axis_pos == last and late
        low, high, got = halo_back(
            zslots[:, (2 * axis_pos) * face_w : (2 * axis_pos + 1) * face_w],
            zslots[:, (2 * axis_pos + 1) * face_w : (2 * axis_pos + 2) * face_w],
            axis,
            rows_of(held) if ride else None,
        )
        returned += [low, high]
        if ride:
            held = merge(held, got.reshape(held.shape), axis, last, 1)
    returned = jnp.concatenate(returned, axis=1)

    solved_t = jnp.dot(
        coarse_inverse, rows_of(held), precision=lax.Precision.HIGHEST, preferred_element_type=jnp.float32
    )
    onehot = (
        send_rows.reshape(slots_n * face_w, 1) == lax.iota(jnp.int32, owned_n)[None, :]
    ).astype(jnp.bfloat16)
    faces = jnp.dot(returned, onehot, preferred_element_type=jnp.float32)
    coarse = lax.dot_general(
        solved_t,
        vectors,
        (((0,), (0,)), ((), ())),
        precision=lax.Precision.HIGHEST,
        preferred_element_type=jnp.float32,
    )
    return own.astype(jnp.float32) + faces + coarse


def solution(mesh):
    return jax.shard_map(
        per_device,
        mesh=mesh,
        in_specs=(
            P(None, AXES),
            P(AXES, None, None),
            P(AXES, None, None),
            P(AXES),
            P(AXES, None),
            P(AXES),
            P(None, AXES),
            P(AXES, None),
        ),
        out_specs=P(None, AXES),
        check_vma=False,
    )
```

```python
import functools

import jax
import jax.numpy as jnp
from jax import lax
from jax.experimental import pallas as pl
from jax.experimental.pallas import tpu as pltpu
from jax.sharding import PartitionSpec as P

AXES = ("gx", "gy", "gz")
NT = (((1,), (1,)), ((), ()))


def solve_kernel(
    parent_ref, res_ref, slot_ref, inv_ref, cpl_ref, after_ref, own_ref, zslot_ref, y_ref, carry_ref
):
    del after_ref
    blocks_n, block_w, _ = inv_ref.shape
    owned_blocks = res_ref.shape[1] // block_w

    def columns(b):
        if b < owned_blocks:
            return res_ref, pl.ds(b * block_w, block_w)
        return slot_ref, pl.ds((b - owned_blocks) * block_w, block_w)

    def link(b):
        return jnp.clip(parent_ref[b], 0, blocks_n - 1)

    for b in range(blocks_n):
        ref, cols = columns(b)
        x = ref[:, cols]
        if b == 0:
            lower = x.astype(jnp.bfloat16)
        else:
            prior = y_ref[link(b)]
            lower = (
                x - lax.dot_general(prior, cpl_ref[b - 1], NT, preferred_element_type=jnp.float32)
            ).astype(jnp.bfloat16)
        y_ref[b] = lax.dot_general(
            lower, inv_ref[b], NT, preferred_element_type=jnp.float32
        ).astype(jnp.bfloat16)

    carry_ref[...] = jnp.zeros(carry_ref.shape, carry_ref.dtype)
    for b in reversed(range(blocks_n)):
        upper = (y_ref[b].astype(jnp.float32) - carry_ref[b]).astype(jnp.bfloat16)
        result = jnp.dot(upper, inv_ref[b], preferred_element_type=jnp.float32).astype(jnp.bfloat16)
        if b < owned_blocks:
            own_ref[:, pl.ds(b * block_w, block_w)] = result
        else:
            zslot_ref[:, pl.ds((b - owned_blocks) * block_w, block_w)] = result
        if b > 0:
            push = jnp.dot(result, cpl_ref[b - 1], preferred_element_type=jnp.float32)
            p = link(b)
            carry_ref[p] = carry_ref[p] + push


def local_solve(parent, residual, slots, diag_inverse, coupling, after):
    nrhs_here, owned_n = residual.shape
    blocks_n, block_w, _ = diag_inverse.shape
    vmem = pltpu.VMEM
    return pl.pallas_call(
        solve_kernel,
        out_shape=(
            jax.ShapeDtypeStruct((nrhs_here, owned_n), jnp.bfloat16),
            jax.ShapeDtypeStruct(slots.shape, jnp.bfloat16),
        ),
        in_specs=[
            pl.BlockSpec(memory_space=pltpu.SMEM),
            pl.BlockSpec(memory_space=vmem),
            pl.BlockSpec(memory_space=vmem),
            pl.BlockSpec(memory_space=vmem),
            pl.BlockSpec(memory_space=vmem),
            pl.BlockSpec(memory_space=pl.ANY),
        ],
        out_specs=(pl.BlockSpec(memory_space=vmem), pl.BlockSpec(memory_space=vmem)),
        scratch_shapes=[
            pltpu.VMEM((blocks_n, nrhs_here, block_w), jnp.bfloat16),
            pltpu.VMEM((blocks_n, nrhs_here, block_w), jnp.float32),
        ],
        compiler_params=pltpu.CompilerParams(vmem_limit_bytes=48 * 1024 * 1024),
        cost_estimate=pl.CostEstimate(
            flops=4 * (2 * blocks_n - 1) * nrhs_here * block_w * block_w,
            transcendentals=0,
            bytes_accessed=2 * (diag_inverse.size + coupling.size) + 6 * residual.size,
        ),
    )(parent, residual, slots, diag_inverse, coupling, after)


def split3(value):
    first = value.astype(jnp.bfloat16)
    rest = value - first.astype(jnp.float32)
    second = rest.astype(jnp.bfloat16)
    third = (rest - second.astype(jnp.float32)).astype(jnp.bfloat16)
    return first, second, third


def finish_kernel(rows_ref, own_ref, back_ref, solved_ref, vec_ref, out_ref):
    owned_n = own_ref.shape[1]
    chunk = 256
    rows = rows_ref[...]
    back = back_ref[...]
    s1, s2, s3 = split3(solved_ref[...])
    for start in range(0, owned_n, chunk):
        cols = pl.ds(start, chunk)
        here = lax.broadcasted_iota(jnp.int32, (rows.shape[0], chunk), 1) + start
        onehot = (rows == here).astype(jnp.bfloat16)
        total = own_ref[:, cols].astype(jnp.float32)
        total += jnp.dot(back, onehot, preferred_element_type=jnp.float32)
        v1, v2, v3 = split3(vec_ref[:, cols])
        for left, right in ((s1, v1), (s1, v2), (s2, v1), (s1, v3), (s3, v1), (s2, v2)):
            total += jnp.dot(left, right, preferred_element_type=jnp.float32)
        out_ref[:, cols] = total


def finish(send_rows, own, returned, solved, vectors):
    vmem = pltpu.VMEM
    return pl.pallas_call(
        finish_kernel,
        out_shape=jax.ShapeDtypeStruct(own.shape, jnp.float32),
        in_specs=[pl.BlockSpec(memory_space=vmem)] * 5,
        out_specs=pl.BlockSpec(memory_space=vmem),
        compiler_params=pltpu.CompilerParams(vmem_limit_bytes=48 * 1024 * 1024),
    )(send_rows.reshape(-1, 1), own, returned, solved, vectors)


def matchings(count):
    first = [(i, i + 1) for i in range(0, count - 1, 2)] + [(i + 1, i) for i in range(0, count - 1, 2)]
    second = [(i, i + 1) for i in range(1, count - 1, 2)] + [(i + 1, i) for i in range(1, count - 1, 2)]
    return first, second


def swap(value, axis, pairs, extra=None):
    if not pairs:
        return jnp.zeros_like(value), None
    if extra is None:
        return lax.ppermute(value, axis, pairs), None
    rows = value.shape[0]
    packed = jnp.concatenate([value.astype(extra.dtype), extra], axis=0)
    got = lax.ppermute(packed, axis, pairs)
    return got[:rows].astype(value.dtype), got[rows:]


def halo_out(down, up, axis, extra=None):
    even = lax.axis_index(axis) % 2 == 0
    first, second = matchings(lax.axis_size(axis))
    r1, got = swap(jnp.where(even, up, down), axis, first, extra)
    r2, _ = swap(jnp.where(even, down, up), axis, second)
    return jnp.where(even, r1, r2), jnp.where(even, r2, r1), got


def halo_back(lo, hi, axis, extra=None):
    even = lax.axis_index(axis) % 2 == 0
    first, second = matchings(lax.axis_size(axis))
    r1, got = swap(jnp.where(even, lo, hi), axis, first, extra)
    r2, _ = swap(jnp.where(even, hi, lo), axis, second)
    return jnp.where(even, r2, r1), jnp.where(even, r1, r2), got


def doubling(axis):
    count = lax.axis_size(axis)
    return count > 1 and not count & (count - 1)


def merge(held, other, axis, dim, step):
    low = (lax.axis_index(axis) // step) % 2 == 0
    return jnp.where(
        low,
        jnp.concatenate([held, other], axis=dim),
        jnp.concatenate([other, held], axis=dim),
    )


def gather_axis(held, axis, dim, step=1):
    count = lax.axis_size(axis)
    if not doubling(axis):
        return lax.all_gather(held, axis, axis=dim, tiled=True)
    while step < count:
        pairs = [(i, i ^ step) for i in range(count)]
        held = merge(held, lax.ppermute(held, axis, pairs), axis, dim, step)
        step *= 2
    return held


def rows_of(held):
    return held.reshape(-1, held.shape[-1])


def per_device(
    residual, diag_inverse, coupling, parent, send_rows, counts, deflation, coarse_inverse
):
    nrhs_here, owned_n = residual.shape
    slots_n, face_w = send_rows.shape
    kmax_here = deflation.shape[0]
    mask = (lax.iota(jnp.int32, kmax_here) < counts[0]).astype(jnp.float32)
    vectors = deflation * mask[:, None]
    coeffs_t = lax.dot_general(
        vectors, residual, NT, precision=lax.Precision.HIGHEST, preferred_element_type=jnp.float32
    )
    held = coeffs_t.reshape((1,) * len(AXES) + coeffs_t.shape)

    outgoing = jnp.take(residual, send_rows, axis=1)
    last = len(AXES) - 1
    late = lax.axis_size(AXES[last]) == 2
    incoming = []
    for axis_pos, axis in enumerate(AXES):
        ride = axis_pos < last and doubling(axis)
        low, high, got = halo_out(
            outgoing[:, 2 * axis_pos],
            outgoing[:, 2 * axis_pos + 1],
            axis,
            rows_of(held) if ride else None,
        )
        incoming += [low, high]
        if ride:
            held = gather_axis(merge(held, got.reshape(held.shape), axis, axis_pos, 1), axis, axis_pos, 2)
        elif axis_pos < last or not late:
            held = gather_axis(held, axis, axis_pos)
    after = coeffs_t
    slots = jnp.concatenate(incoming, axis=1)

    own, zslots = local_solve(parent, residual, slots, diag_inverse, coupling, after)

    returned = []
    for axis_pos, axis in enumerate(AXES):
        ride = axis_pos == last and late
        low, high, got = halo_back(
            zslots[:, (2 * axis_pos) * face_w : (2 * axis_pos + 1) * face_w],
            zslots[:, (2 * axis_pos + 1) * face_w : (2 * axis_pos + 2) * face_w],
            axis,
            rows_of(held) if ride else None,
        )
        returned += [low, high]
        if ride:
            held = merge(held, got.reshape(held.shape), axis, last, 1)
    returned = jnp.concatenate(returned, axis=1)

    solved = lax.dot_general(
        rows_of(held),
        coarse_inverse,
        (((0,), (1,)), ((), ())),
        precision=lax.Precision.HIGHEST,
        preferred_element_type=jnp.float32,
    )
    return finish(send_rows, own, returned, solved, vectors)


def solution(mesh):
    return jax.shard_map(
        per_device,
        mesh=mesh,
        in_specs=(
            P(None, AXES),
            P(AXES, None, None),
            P(AXES, None, None),
            P(AXES),
            P(AXES, None),
            P(AXES),
            P(None, AXES),
            P(AXES, None),
        ),
        out_specs=P(None, AXES),
        check_vma=False,
    )
```

```python
import functools

import jax
import jax.numpy as jnp
from jax import lax
from jax.experimental import pallas as pl
from jax.experimental.pallas import tpu as pltpu
from jax.sharding import PartitionSpec as P

AXES = ("gx", "gy", "gz")
NT = (((1,), (1,)), ((), ()))


def solve_kernel(
    parent_ref, res_ref, slot_ref, inv_ref, cpl_ref, after_ref, own_ref, zslot_ref, y_ref, carry_ref
):
    del after_ref
    blocks_n, block_w, _ = inv_ref.shape
    owned_blocks = res_ref.shape[1] // block_w

    def columns(b):
        if b < owned_blocks:
            return res_ref, pl.ds(b * block_w, block_w)
        return slot_ref, pl.ds((b - owned_blocks) * block_w, block_w)

    def link(b):
        return jnp.clip(parent_ref[b], 0, blocks_n - 1)

    for b in range(blocks_n):
        ref, cols = columns(b)
        x = ref[:, cols]
        if b == 0:
            lower = x.astype(jnp.bfloat16)
        else:
            prior = y_ref[link(b)]
            lower = (
                x - lax.dot_general(prior, cpl_ref[b - 1], NT, preferred_element_type=jnp.float32)
            ).astype(jnp.bfloat16)
        y_ref[b] = lax.dot_general(
            lower, inv_ref[b], NT, preferred_element_type=jnp.float32
        ).astype(jnp.bfloat16)

    carry_ref[...] = jnp.zeros(carry_ref.shape, carry_ref.dtype)
    for b in reversed(range(blocks_n)):
        upper = (y_ref[b].astype(jnp.float32) - carry_ref[b]).astype(jnp.bfloat16)
        result = jnp.dot(upper, inv_ref[b], preferred_element_type=jnp.float32).astype(jnp.bfloat16)
        if b < owned_blocks:
            own_ref[:, pl.ds(b * block_w, block_w)] = result
        else:
            zslot_ref[:, pl.ds((b - owned_blocks) * block_w, block_w)] = result
        if b > 0:
            push = jnp.dot(result, cpl_ref[b - 1], preferred_element_type=jnp.float32)
            p = link(b)
            carry_ref[p] = carry_ref[p] + push


def local_solve(parent, residual, slots, diag_inverse, coupling, after):
    nrhs_here, owned_n = residual.shape
    blocks_n, block_w, _ = diag_inverse.shape
    vmem = pltpu.VMEM
    return pl.pallas_call(
        solve_kernel,
        out_shape=(
            jax.ShapeDtypeStruct((nrhs_here, owned_n), jnp.bfloat16),
            jax.ShapeDtypeStruct(slots.shape, jnp.bfloat16),
        ),
        in_specs=[
            pl.BlockSpec(memory_space=pltpu.SMEM),
            pl.BlockSpec(memory_space=vmem),
            pl.BlockSpec(memory_space=vmem),
            pl.BlockSpec(memory_space=vmem),
            pl.BlockSpec(memory_space=vmem),
            pl.BlockSpec(memory_space=pl.ANY),
        ],
        out_specs=(pl.BlockSpec(memory_space=vmem), pl.BlockSpec(memory_space=vmem)),
        scratch_shapes=[
            pltpu.VMEM((blocks_n, nrhs_here, block_w), jnp.bfloat16),
            pltpu.VMEM((blocks_n, nrhs_here, block_w), jnp.float32),
        ],
        compiler_params=pltpu.CompilerParams(vmem_limit_bytes=48 * 1024 * 1024),
        cost_estimate=pl.CostEstimate(
            flops=4 * (2 * blocks_n - 1) * nrhs_here * block_w * block_w,
            transcendentals=0,
            bytes_accessed=2 * (diag_inverse.size + coupling.size) + 6 * residual.size,
        ),
    )(parent, residual, slots, diag_inverse, coupling, after)


def split3(value):
    first = value.astype(jnp.bfloat16)
    rest = value - first.astype(jnp.float32)
    second = rest.astype(jnp.bfloat16)
    third = (rest - second.astype(jnp.float32)).astype(jnp.bfloat16)
    return first, second, third


def finish_kernel(count_ref, rows_ref, own_ref, back_ref, solved_ref, vec_ref, out_ref):
    owned_n = own_ref.shape[1]
    kmax_here = vec_ref.shape[0]
    keep = lax.broadcasted_iota(jnp.int32, (kmax_here, 1), 0) < count_ref[0]
    chunk = 256
    rows = rows_ref[...]
    back = back_ref[...]
    s1, s2, s3 = split3(solved_ref[...])
    for start in range(0, owned_n, chunk):
        cols = pl.ds(start, chunk)
        here = lax.broadcasted_iota(jnp.int32, (rows.shape[0], chunk), 1) + start
        onehot = (rows == here).astype(jnp.bfloat16)
        total = own_ref[:, cols].astype(jnp.float32)
        total += jnp.dot(back, onehot, preferred_element_type=jnp.float32)
        v1, v2, v3 = split3(jnp.where(keep, vec_ref[:, cols], 0.0))
        for left, right in ((s1, v1), (s1, v2), (s2, v1), (s1, v3), (s3, v1), (s2, v2)):
            total += jnp.dot(left, right, preferred_element_type=jnp.float32)
        out_ref[:, cols] = total


def finish(send_rows, counts, own, returned, solved, deflation):
    vmem = pltpu.VMEM
    return pl.pallas_call(
        finish_kernel,
        out_shape=jax.ShapeDtypeStruct(own.shape, jnp.float32),
        in_specs=[pl.BlockSpec(memory_space=pltpu.SMEM)] + [pl.BlockSpec(memory_space=vmem)] * 5,
        out_specs=pl.BlockSpec(memory_space=vmem),
        compiler_params=pltpu.CompilerParams(vmem_limit_bytes=48 * 1024 * 1024),
    )(counts, send_rows.reshape(-1, 1), own, returned, solved, deflation)


def matchings(count):
    first = [(i, i + 1) for i in range(0, count - 1, 2)] + [(i + 1, i) for i in range(0, count - 1, 2)]
    second = [(i, i + 1) for i in range(1, count - 1, 2)] + [(i + 1, i) for i in range(1, count - 1, 2)]
    return first, second


def swap(value, axis, pairs, extra=None):
    if not pairs:
        return jnp.zeros_like(value), None
    if extra is None:
        return lax.ppermute(value, axis, pairs), None
    rows = value.shape[0]
    packed = jnp.concatenate([value.astype(extra.dtype), extra], axis=0)
    got = lax.ppermute(packed, axis, pairs)
    return got[:rows].astype(value.dtype), got[rows:]


def halo_out(down, up, axis, extra=None):
    even = lax.axis_index(axis) % 2 == 0
    first, second = matchings(lax.axis_size(axis))
    r1, got = swap(jnp.where(even, up, down), axis, first, extra)
    r2, _ = swap(jnp.where(even, down, up), axis, second)
    return jnp.where(even, r1, r2), jnp.where(even, r2, r1), got


def halo_back(lo, hi, axis, extra=None):
    even = lax.axis_index(axis) % 2 == 0
    first, second = matchings(lax.axis_size(axis))
    r1, got = swap(jnp.where(even, lo, hi), axis, first, extra)
    r2, _ = swap(jnp.where(even, hi, lo), axis, second)
    return jnp.where(even, r2, r1), jnp.where(even, r1, r2), got


def doubling(axis):
    count = lax.axis_size(axis)
    return count > 1 and not count & (count - 1)


def merge(held, other, axis, dim, step):
    low = (lax.axis_index(axis) // step) % 2 == 0
    return jnp.where(
        low,
        jnp.concatenate([held, other], axis=dim),
        jnp.concatenate([other, held], axis=dim),
    )


def gather_axis(held, axis, dim, step=1):
    count = lax.axis_size(axis)
    if not doubling(axis):
        return lax.all_gather(held, axis, axis=dim, tiled=True)
    while step < count:
        pairs = [(i, i ^ step) for i in range(count)]
        held = merge(held, lax.ppermute(held, axis, pairs), axis, dim, step)
        step *= 2
    return held


def rows_of(held):
    return held.reshape(-1, held.shape[-1])


def per_device(
    residual, diag_inverse, coupling, parent, send_rows, counts, deflation, coarse_inverse
):
    nrhs_here, owned_n = residual.shape
    slots_n, face_w = send_rows.shape
    kmax_here = deflation.shape[0]
    mask = (lax.iota(jnp.int32, kmax_here) < counts[0]).astype(jnp.float32)
    vectors = deflation * mask[:, None]
    coeffs_t = lax.dot_general(
        vectors, residual, NT, precision=lax.Precision.HIGHEST, preferred_element_type=jnp.float32
    )
    held = coeffs_t.reshape((1,) * len(AXES) + coeffs_t.shape)

    outgoing = jnp.take(residual, send_rows, axis=1)
    last = len(AXES) - 1
    late = lax.axis_size(AXES[last]) == 2
    incoming = []
    for axis_pos, axis in enumerate(AXES):
        ride = axis_pos < last and doubling(axis)
        low, high, got = halo_out(
            outgoing[:, 2 * axis_pos],
            outgoing[:, 2 * axis_pos + 1],
            axis,
            rows_of(held) if ride else None,
        )
        incoming += [low, high]
        if ride:
            held = gather_axis(merge(held, got.reshape(held.shape), axis, axis_pos, 1), axis, axis_pos, 2)
        elif axis_pos < last or not late:
            held = gather_axis(held, axis, axis_pos)
    after = coeffs_t
    slots = jnp.concatenate(incoming, axis=1)

    own, zslots = local_solve(parent, residual, slots, diag_inverse, coupling, after)

    returned = []
    for axis_pos, axis in enumerate(AXES):
        ride = axis_pos == last and late
        low, high, got = halo_back(
            zslots[:, (2 * axis_pos) * face_w : (2 * axis_pos + 1) * face_w],
            zslots[:, (2 * axis_pos + 1) * face_w : (2 * axis_pos + 2) * face_w],
            axis,
            rows_of(held) if ride else None,
        )
        returned += [low, high]
        if ride:
            held = merge(held, got.reshape(held.shape), axis, last, 1)
    returned = jnp.concatenate(returned, axis=1)

    solved_t = jnp.dot(
        coarse_inverse, rows_of(held), precision=lax.Precision.HIGHEST, preferred_element_type=jnp.float32
    )
    return finish(send_rows, counts, own, returned, solved_t.T, deflation)


def solution(mesh):
    return jax.shard_map(
        per_device,
        mesh=mesh,
        in_specs=(
            P(None, AXES),
            P(AXES, None, None),
            P(AXES, None, None),
            P(AXES),
            P(AXES, None),
            P(AXES),
            P(None, AXES),
            P(AXES, None),
        ),
        out_specs=P(None, AXES),
        check_vma=False,
    )
```

```python
import functools

import jax
import jax.numpy as jnp
from jax import lax
from jax.experimental import pallas as pl
from jax.experimental.pallas import tpu as pltpu
from jax.sharding import PartitionSpec as P

AXES = ("gx", "gy", "gz")
NT = (((1,), (1,)), ((), ()))


def solve_kernel(
    parent_ref, res_ref, slot_ref, inv_ref, cpl_ref, after_ref, own_ref, zslot_ref, y_ref, carry_ref
):
    del after_ref
    blocks_n, block_w, _ = inv_ref.shape
    owned_blocks = res_ref.shape[1] // block_w

    def columns(b):
        if b < owned_blocks:
            return res_ref, pl.ds(b * block_w, block_w)
        return slot_ref, pl.ds((b - owned_blocks) * block_w, block_w)

    def link(b):
        return jnp.clip(parent_ref[b], 0, blocks_n - 1)

    for b in range(blocks_n):
        ref, cols = columns(b)
        x = ref[:, cols]
        if b == 0:
            lower = x.astype(jnp.bfloat16)
        else:
            prior = y_ref[link(b)]
            lower = (
                x - lax.dot_general(prior, cpl_ref[b - 1], NT, preferred_element_type=jnp.float32)
            ).astype(jnp.bfloat16)
        y_ref[b] = lax.dot_general(
            lower, inv_ref[b], NT, preferred_element_type=jnp.float32
        ).astype(jnp.bfloat16)

    carry_ref[...] = jnp.zeros(carry_ref.shape, carry_ref.dtype)
    for b in reversed(range(blocks_n)):
        upper = (y_ref[b].astype(jnp.float32) - carry_ref[b]).astype(jnp.bfloat16)
        result = jnp.dot(upper, inv_ref[b], preferred_element_type=jnp.float32).astype(jnp.bfloat16)
        if b < owned_blocks:
            own_ref[:, pl.ds(b * block_w, block_w)] = result
        else:
            zslot_ref[:, pl.ds((b - owned_blocks) * block_w, block_w)] = result
        if b > 0:
            push = jnp.dot(result, cpl_ref[b - 1], preferred_element_type=jnp.float32)
            p = link(b)
            carry_ref[p] = carry_ref[p] + push


def local_solve(parent, residual, slots, diag_inverse, coupling, after):
    nrhs_here, owned_n = residual.shape
    blocks_n, block_w, _ = diag_inverse.shape
    vmem = pltpu.VMEM
    return pl.pallas_call(
        solve_kernel,
        out_shape=(
            jax.ShapeDtypeStruct((nrhs_here, owned_n), jnp.bfloat16),
            jax.ShapeDtypeStruct(slots.shape, jnp.bfloat16),
        ),
        in_specs=[
            pl.BlockSpec(memory_space=pltpu.SMEM),
            pl.BlockSpec(memory_space=vmem),
            pl.BlockSpec(memory_space=vmem),
            pl.BlockSpec(memory_space=vmem),
            pl.BlockSpec(memory_space=vmem),
            pl.BlockSpec(memory_space=pl.ANY),
        ],
        out_specs=(pl.BlockSpec(memory_space=vmem), pl.BlockSpec(memory_space=vmem)),
        scratch_shapes=[
            pltpu.VMEM((blocks_n, nrhs_here, block_w), jnp.bfloat16),
            pltpu.VMEM((blocks_n, nrhs_here, block_w), jnp.float32),
        ],
        compiler_params=pltpu.CompilerParams(vmem_limit_bytes=48 * 1024 * 1024),
    )(parent, residual, slots, diag_inverse, coupling, after)


def matchings(count):
    first = [(i, i + 1) for i in range(0, count - 1, 2)] + [(i + 1, i) for i in range(0, count - 1, 2)]
    second = [(i, i + 1) for i in range(1, count - 1, 2)] + [(i + 1, i) for i in range(1, count - 1, 2)]
    return first, second


def swap(value, axis, pairs, extra=None):
    if not pairs:
        return jnp.zeros_like(value), None
    if extra is None:
        return lax.ppermute(value, axis, pairs), None
    rows = value.shape[0]
    packed = jnp.concatenate([value.astype(extra.dtype), extra], axis=0)
    got = lax.ppermute(packed, axis, pairs)
    return got[:rows].astype(value.dtype), got[rows:]


def halo_out(down, up, axis, extra=None):
    even = lax.axis_index(axis) % 2 == 0
    first, second = matchings(lax.axis_size(axis))
    r1, got = swap(jnp.where(even, up, down), axis, first, extra)
    r2, _ = swap(jnp.where(even, down, up), axis, second)
    return jnp.where(even, r1, r2), jnp.where(even, r2, r1), got


def halo_back(lo, hi, axis, extra=None):
    even = lax.axis_index(axis) % 2 == 0
    first, second = matchings(lax.axis_size(axis))
    r1, got = swap(jnp.where(even, lo, hi), axis, first, extra)
    r2, _ = swap(jnp.where(even, hi, lo), axis, second)
    return jnp.where(even, r2, r1), jnp.where(even, r1, r2), got


def doubling(axis):
    count = lax.axis_size(axis)
    return count > 1 and not count & (count - 1)


def merge(held, other, axis, dim, step):
    low = (lax.axis_index(axis) // step) % 2 == 0
    return jnp.where(
        low,
        jnp.concatenate([held, other], axis=dim),
        jnp.concatenate([other, held], axis=dim),
    )


def gather_axis(held, axis, dim, step=1):
    count = lax.axis_size(axis)
    if not doubling(axis):
        return lax.all_gather(held, axis, axis=dim, tiled=True)
    while step < count:
        pairs = [(i, i ^ step) for i in range(count)]
        held = merge(held, lax.ppermute(held, axis, pairs), axis, dim, step)
        step *= 2
    return held


def rows_of(held):
    return held.reshape(-1, held.shape[-1])


def per_device(
    residual, diag_inverse, coupling, parent, send_rows, counts, deflation, coarse_inverse
):
    nrhs_here, owned_n = residual.shape
    slots_n, face_w = send_rows.shape
    kmax_here = deflation.shape[0]
    mask = (lax.iota(jnp.int32, kmax_here) < counts[0]).astype(jnp.float32)
    vectors = deflation * mask[:, None]
    coeffs_t = lax.dot_general(
        vectors, residual, NT, precision=lax.Precision.HIGHEST, preferred_element_type=jnp.float32
    )
    total_dev = coarse_inverse.shape[1] // kmax_here
    spread = jnp.broadcast_to(coeffs_t[None], (total_dev,) + coeffs_t.shape)
    held = lax.all_to_all(spread, AXES, 0, 0, tiled=True)

    outgoing = jnp.take(residual, send_rows, axis=1)
    incoming = []
    for axis_pos, axis in enumerate(AXES):
        low, high, _ = halo_out(outgoing[:, 2 * axis_pos], outgoing[:, 2 * axis_pos + 1], axis)
        incoming += [low, high]
    slots = jnp.concatenate(incoming, axis=1)
    after = coeffs_t

    own, zslots = local_solve(parent, residual, slots, diag_inverse, coupling, after)
    zslots, held = lax.optimization_barrier((zslots, held))

    returned = []
    for axis_pos, axis in enumerate(AXES):
        low, high, _ = halo_back(
            zslots[:, (2 * axis_pos) * face_w : (2 * axis_pos + 1) * face_w],
            zslots[:, (2 * axis_pos + 1) * face_w : (2 * axis_pos + 2) * face_w],
            axis,
        )
        returned += [low, high]
    returned = jnp.concatenate(returned, axis=1)

    solved_t = jnp.dot(
        coarse_inverse, rows_of(held), precision=lax.Precision.HIGHEST, preferred_element_type=jnp.float32
    )
    onehot = (
        send_rows.reshape(slots_n * face_w, 1) == lax.iota(jnp.int32, owned_n)[None, :]
    ).astype(jnp.bfloat16)
    faces = jnp.dot(returned, onehot, preferred_element_type=jnp.float32)
    coarse = lax.dot_general(
        solved_t,
        vectors,
        (((0,), (0,)), ((), ())),
        precision=lax.Precision.HIGHEST,
        preferred_element_type=jnp.float32,
    )
    return own.astype(jnp.float32) + faces + coarse


def solution(mesh):
    return jax.shard_map(
        per_device,
        mesh=mesh,
        in_specs=(
            P(None, AXES),
            P(AXES, None, None),
            P(AXES, None, None),
            P(AXES),
            P(AXES, None),
            P(AXES),
            P(None, AXES),
            P(AXES, None),
        ),
        out_specs=P(None, AXES),
        check_vma=False,
    )
```

```python
import functools

import jax
import jax.numpy as jnp
from jax import lax
from jax.experimental import pallas as pl
from jax.experimental.pallas import tpu as pltpu
from jax.sharding import PartitionSpec as P

AXES = ("gx", "gy", "gz")
NT = (((1,), (1,)), ((), ()))


def solve_kernel(
    parent_ref, res_ref, slot_ref, inv_ref, cpl_ref, after_ref, own_ref, zslot_ref, y_ref, carry_ref
):
    del after_ref
    blocks_n, block_w, _ = inv_ref.shape
    owned_blocks = res_ref.shape[1] // block_w

    def columns(b):
        if b < owned_blocks:
            return res_ref, pl.ds(b * block_w, block_w)
        return slot_ref, pl.ds((b - owned_blocks) * block_w, block_w)

    def link(b):
        return jnp.clip(parent_ref[b], 0, blocks_n - 1)

    for b in range(blocks_n):
        ref, cols = columns(b)
        x = ref[:, cols]
        if b == 0:
            lower = x.astype(jnp.bfloat16)
        else:
            prior = y_ref[link(b)]
            lower = (
                x - lax.dot_general(prior, cpl_ref[b - 1], NT, preferred_element_type=jnp.float32)
            ).astype(jnp.bfloat16)
        y_ref[b] = lax.dot_general(
            lower, inv_ref[b], NT, preferred_element_type=jnp.float32
        ).astype(jnp.bfloat16)

    carry_ref[...] = jnp.zeros(carry_ref.shape, carry_ref.dtype)
    for b in reversed(range(blocks_n)):
        upper = (y_ref[b].astype(jnp.float32) - carry_ref[b]).astype(jnp.bfloat16)
        result = jnp.dot(upper, inv_ref[b], preferred_element_type=jnp.float32).astype(jnp.bfloat16)
        if b < owned_blocks:
            own_ref[:, pl.ds(b * block_w, block_w)] = result
        else:
            zslot_ref[:, pl.ds((b - owned_blocks) * block_w, block_w)] = result
        if b > 0:
            push = jnp.dot(result, cpl_ref[b - 1], preferred_element_type=jnp.float32)
            p = link(b)
            carry_ref[p] = carry_ref[p] + push


def local_solve(parent, residual, slots, diag_inverse, coupling, after):
    nrhs_here, owned_n = residual.shape
    blocks_n, block_w, _ = diag_inverse.shape
    vmem = pltpu.VMEM
    return pl.pallas_call(
        solve_kernel,
        out_shape=(
            jax.ShapeDtypeStruct((nrhs_here, owned_n), jnp.bfloat16),
            jax.ShapeDtypeStruct(slots.shape, jnp.bfloat16),
        ),
        in_specs=[
            pl.BlockSpec(memory_space=pltpu.SMEM),
            pl.BlockSpec(memory_space=vmem),
            pl.BlockSpec(memory_space=vmem),
            pl.BlockSpec(memory_space=vmem),
            pl.BlockSpec(memory_space=vmem),
            pl.BlockSpec(memory_space=pl.ANY),
        ],
        out_specs=(pl.BlockSpec(memory_space=vmem), pl.BlockSpec(memory_space=vmem)),
        scratch_shapes=[
            pltpu.VMEM((blocks_n, nrhs_here, block_w), jnp.bfloat16),
            pltpu.VMEM((blocks_n, nrhs_here, block_w), jnp.float32),
        ],
        compiler_params=pltpu.CompilerParams(vmem_limit_bytes=48 * 1024 * 1024),
    )(parent, residual, slots, diag_inverse, coupling, after)


def matchings(count):
    first = [(i, i + 1) for i in range(0, count - 1, 2)] + [(i + 1, i) for i in range(0, count - 1, 2)]
    second = [(i, i + 1) for i in range(1, count - 1, 2)] + [(i + 1, i) for i in range(1, count - 1, 2)]
    return first, second


def swap(value, axis, pairs, extra=None):
    if not pairs:
        return jnp.zeros_like(value), None
    if extra is None:
        return lax.ppermute(value, axis, pairs), None
    rows = value.shape[0]
    packed = jnp.concatenate([value.astype(extra.dtype), extra], axis=0)
    got = lax.ppermute(packed, axis, pairs)
    return got[:rows].astype(value.dtype), got[rows:]


def halo_out(down, up, axis, extra=None):
    even = lax.axis_index(axis) % 2 == 0
    first, second = matchings(lax.axis_size(axis))
    r1, got = swap(jnp.where(even, up, down), axis, first, extra)
    r2, _ = swap(jnp.where(even, down, up), axis, second)
    return jnp.where(even, r1, r2), jnp.where(even, r2, r1), got


def halo_back(lo, hi, axis, extra=None):
    even = lax.axis_index(axis) % 2 == 0
    first, second = matchings(lax.axis_size(axis))
    r1, got = swap(jnp.where(even, lo, hi), axis, first, extra)
    r2, _ = swap(jnp.where(even, hi, lo), axis, second)
    return jnp.where(even, r2, r1), jnp.where(even, r1, r2), got


def doubling(axis):
    count = lax.axis_size(axis)
    return count > 1 and not count & (count - 1)


def merge(held, other, axis, dim, step):
    low = (lax.axis_index(axis) // step) % 2 == 0
    return jnp.where(
        low,
        jnp.concatenate([held, other], axis=dim),
        jnp.concatenate([other, held], axis=dim),
    )


def gather_axis(held, axis, dim, step=1):
    count = lax.axis_size(axis)
    if not doubling(axis):
        return lax.all_gather(held, axis, axis=dim, tiled=True)
    while step < count:
        pairs = [(i, i ^ step) for i in range(count)]
        held = merge(held, lax.ppermute(held, axis, pairs), axis, dim, step)
        step *= 2
    return held


def rows_of(held):
    return held.reshape(-1, held.shape[-1])


def per_device(
    residual, diag_inverse, coupling, parent, send_rows, counts, deflation, coarse_inverse
):
    nrhs_here, owned_n = residual.shape
    slots_n, face_w = send_rows.shape
    kmax_here = deflation.shape[0]
    mask = (lax.iota(jnp.int32, kmax_here) < counts[0]).astype(jnp.float32)
    vectors = deflation * mask[:, None]
    coeffs_t = lax.dot_general(
        vectors, residual, NT, precision=lax.Precision.HIGHEST, preferred_element_type=jnp.float32
    )
    total_dev = coarse_inverse.shape[1] // kmax_here

    outgoing = jnp.take(residual, send_rows, axis=1)
    incoming = []
    for axis_pos, axis in enumerate(AXES):
        low, high, _ = halo_out(outgoing[:, 2 * axis_pos], outgoing[:, 2 * axis_pos + 1], axis)
        incoming += [low, high]
    slots = jnp.concatenate(incoming, axis=1)
    slots, coeffs_t = lax.optimization_barrier((slots, coeffs_t))
    spread = jnp.broadcast_to(coeffs_t[None], (total_dev,) + coeffs_t.shape)
    held = lax.all_to_all(spread, AXES, 0, 0, tiled=True)
    after = coeffs_t

    own, zslots = local_solve(parent, residual, slots, diag_inverse, coupling, after)
    zslots, held = lax.optimization_barrier((zslots, held))

    returned = []
    for axis_pos, axis in enumerate(AXES):
        low, high, _ = halo_back(
            zslots[:, (2 * axis_pos) * face_w : (2 * axis_pos + 1) * face_w],
            zslots[:, (2 * axis_pos + 1) * face_w : (2 * axis_pos + 2) * face_w],
            axis,
        )
        returned += [low, high]
    returned = jnp.concatenate(returned, axis=1)

    solved_t = jnp.dot(
        coarse_inverse, rows_of(held), precision=lax.Precision.HIGHEST, preferred_element_type=jnp.float32
    )
    onehot = (
        send_rows.reshape(slots_n * face_w, 1) == lax.iota(jnp.int32, owned_n)[None, :]
    ).astype(jnp.bfloat16)
    faces = jnp.dot(returned, onehot, preferred_element_type=jnp.float32)
    coarse = lax.dot_general(
        solved_t,
        vectors,
        (((0,), (0,)), ((), ())),
        precision=lax.Precision.HIGHEST,
        preferred_element_type=jnp.float32,
    )
    return own.astype(jnp.float32) + faces + coarse


def solution(mesh):
    return jax.shard_map(
        per_device,
        mesh=mesh,
        in_specs=(
            P(None, AXES),
            P(AXES, None, None),
            P(AXES, None, None),
            P(AXES),
            P(AXES, None),
            P(AXES),
            P(None, AXES),
            P(AXES, None),
        ),
        out_specs=P(None, AXES),
        check_vma=False,
    )
```

```python
import functools

import jax
import jax.numpy as jnp
from jax import lax
from jax.experimental import pallas as pl
from jax.experimental.pallas import tpu as pltpu
from jax.sharding import PartitionSpec as P

AXES = ("gx", "gy", "gz")
NT = (((1,), (1,)), ((), ()))


def solve_kernel(
    parent_ref, res_ref, slot_ref, inv_ref, cpl_ref, after_ref, own_ref, zslot_ref, y_ref, carry_ref
):
    del after_ref
    blocks_n, block_w, _ = inv_ref.shape
    owned_blocks = res_ref.shape[1] // block_w

    def columns(b):
        if b < owned_blocks:
            return res_ref, pl.ds(b * block_w, block_w)
        return slot_ref, pl.ds((b - owned_blocks) * block_w, block_w)

    def link(b):
        return jnp.clip(parent_ref[b], 0, blocks_n - 1)

    for b in range(blocks_n):
        ref, cols = columns(b)
        x = ref[:, cols]
        if b == 0:
            lower = x.astype(jnp.bfloat16)
        else:
            prior = y_ref[link(b)]
            lower = (
                x - lax.dot_general(prior, cpl_ref[b - 1], NT, preferred_element_type=jnp.float32)
            ).astype(jnp.bfloat16)
        y_ref[b] = lax.dot_general(
            lower, inv_ref[b], NT, preferred_element_type=jnp.float32
        ).astype(jnp.bfloat16)

    carry_ref[...] = jnp.zeros(carry_ref.shape, carry_ref.dtype)
    for b in reversed(range(blocks_n)):
        upper = (y_ref[b].astype(jnp.float32) - carry_ref[b]).astype(jnp.bfloat16)
        result = jnp.dot(upper, inv_ref[b], preferred_element_type=jnp.float32).astype(jnp.bfloat16)
        if b < owned_blocks:
            own_ref[:, pl.ds(b * block_w, block_w)] = result
        else:
            zslot_ref[:, pl.ds((b - owned_blocks) * block_w, block_w)] = result
        if b > 0:
            push = jnp.dot(result, cpl_ref[b - 1], preferred_element_type=jnp.float32)
            p = link(b)
            carry_ref[p] = carry_ref[p] + push


def local_solve(parent, residual, slots, diag_inverse, coupling, after):
    nrhs_here, owned_n = residual.shape
    blocks_n, block_w, _ = diag_inverse.shape
    vmem = pltpu.VMEM
    return pl.pallas_call(
        solve_kernel,
        out_shape=(
            jax.ShapeDtypeStruct((nrhs_here, owned_n), jnp.bfloat16),
            jax.ShapeDtypeStruct(slots.shape, jnp.bfloat16),
        ),
        in_specs=[
            pl.BlockSpec(memory_space=pltpu.SMEM),
            pl.BlockSpec(memory_space=vmem),
            pl.BlockSpec(memory_space=vmem),
            pl.BlockSpec(memory_space=vmem),
            pl.BlockSpec(memory_space=vmem),
            pl.BlockSpec(memory_space=pl.ANY),
        ],
        out_specs=(pl.BlockSpec(memory_space=vmem), pl.BlockSpec(memory_space=vmem)),
        scratch_shapes=[
            pltpu.VMEM((blocks_n, nrhs_here, block_w), jnp.bfloat16),
            pltpu.VMEM((blocks_n, nrhs_here, block_w), jnp.float32),
        ],
        compiler_params=pltpu.CompilerParams(vmem_limit_bytes=48 * 1024 * 1024),
    )(parent, residual, slots, diag_inverse, coupling, after)


def split3(value):
    first = value.astype(jnp.bfloat16)
    rest = value - first.astype(jnp.float32)
    second = rest.astype(jnp.bfloat16)
    third = (rest - second.astype(jnp.float32)).astype(jnp.bfloat16)
    return first, second, third


def finish_kernel(count_ref, rows_ref, own_ref, back_ref, solved_ref, vec_ref, out_ref):
    owned_n = own_ref.shape[1]
    kmax_here = vec_ref.shape[0]
    keep = lax.broadcasted_iota(jnp.int32, (kmax_here, 1), 0) < count_ref[0]
    chunk = 256
    rows = rows_ref[...]
    back = back_ref[...]
    s1, s2, s3 = split3(solved_ref[...])
    for start in range(0, owned_n, chunk):
        cols = pl.ds(start, chunk)
        here = lax.broadcasted_iota(jnp.int32, (rows.shape[0], chunk), 1) + start
        onehot = (rows == here).astype(jnp.bfloat16)
        total = own_ref[:, cols].astype(jnp.float32)
        total += jnp.dot(back, onehot, preferred_element_type=jnp.float32)
        v1, v2, v3 = split3(jnp.where(keep, vec_ref[:, cols], 0.0))
        for left, right in ((s1, v1), (s1, v2), (s2, v1), (s1, v3), (s3, v1), (s2, v2)):
            total += jnp.dot(left, right, preferred_element_type=jnp.float32)
        out_ref[:, cols] = total


def finish(send_rows, counts, own, returned, solved, deflation):
    vmem = pltpu.VMEM
    return pl.pallas_call(
        finish_kernel,
        out_shape=jax.ShapeDtypeStruct(own.shape, jnp.float32),
        in_specs=[pl.BlockSpec(memory_space=pltpu.SMEM)] + [pl.BlockSpec(memory_space=vmem)] * 5,
        out_specs=pl.BlockSpec(memory_space=vmem),
        compiler_params=pltpu.CompilerParams(vmem_limit_bytes=48 * 1024 * 1024),
    )(counts, send_rows.reshape(-1, 1), own, returned, solved, deflation)


def matchings(count):
    first = [(i, i + 1) for i in range(0, count - 1, 2)] + [(i + 1, i) for i in range(0, count - 1, 2)]
    second = [(i, i + 1) for i in range(1, count - 1, 2)] + [(i + 1, i) for i in range(1, count - 1, 2)]
    return first, second


def swap(value, axis, pairs, extra=None):
    if not pairs:
        return jnp.zeros_like(value), None
    if extra is None:
        return lax.ppermute(value, axis, pairs), None
    rows = value.shape[0]
    packed = jnp.concatenate([value.astype(extra.dtype), extra], axis=0)
    got = lax.ppermute(packed, axis, pairs)
    return got[:rows].astype(value.dtype), got[rows:]


def halo_out(down, up, axis, extra=None):
    even = lax.axis_index(axis) % 2 == 0
    first, second = matchings(lax.axis_size(axis))
    r1, got = swap(jnp.where(even, up, down), axis, first, extra)
    r2, _ = swap(jnp.where(even, down, up), axis, second)
    return jnp.where(even, r1, r2), jnp.where(even, r2, r1), got


def halo_back(lo, hi, axis, extra=None):
    even = lax.axis_index(axis) % 2 == 0
    first, second = matchings(lax.axis_size(axis))
    r1, got = swap(jnp.where(even, lo, hi), axis, first, extra)
    r2, _ = swap(jnp.where(even, hi, lo), axis, second)
    return jnp.where(even, r2, r1), jnp.where(even, r1, r2), got


def doubling(axis):
    count = lax.axis_size(axis)
    return count > 1 and not count & (count - 1)


def merge(held, other, axis, dim, step):
    low = (lax.axis_index(axis) // step) % 2 == 0
    return jnp.where(
        low,
        jnp.concatenate([held, other], axis=dim),
        jnp.concatenate([other, held], axis=dim),
    )


def gather_axis(held, axis, dim, step=1):
    count = lax.axis_size(axis)
    if not doubling(axis):
        return lax.all_gather(held, axis, axis=dim, tiled=True)
    while step < count:
        pairs = [(i, i ^ step) for i in range(count)]
        held = merge(held, lax.ppermute(held, axis, pairs), axis, dim, step)
        step *= 2
    return held


def rows_of(held):
    return held.reshape(-1, held.shape[-1])


def per_device(
    residual, diag_inverse, coupling, parent, send_rows, counts, deflation, coarse_inverse
):
    nrhs_here, owned_n = residual.shape
    slots_n, face_w = send_rows.shape
    kmax_here = deflation.shape[0]
    mask = (lax.iota(jnp.int32, kmax_here) < counts[0]).astype(jnp.float32)
    vectors = deflation * mask[:, None]
    coeffs_t = lax.dot_general(
        vectors, residual, NT, precision=lax.Precision.HIGHEST, preferred_element_type=jnp.float32
    )
    total_dev = coarse_inverse.shape[1] // kmax_here

    outgoing = jnp.take(residual, send_rows, axis=1)
    incoming = []
    for axis_pos, axis in enumerate(AXES):
        low, high, _ = halo_out(outgoing[:, 2 * axis_pos], outgoing[:, 2 * axis_pos + 1], axis)
        incoming += [low, high]
    slots = jnp.concatenate(incoming, axis=1)
    slots, coeffs_t = lax.optimization_barrier((slots, coeffs_t))
    spread = jnp.broadcast_to(coeffs_t[None], (total_dev,) + coeffs_t.shape)
    held = lax.all_to_all(spread, AXES, 0, 0, tiled=True)
    after = coeffs_t

    own, zslots = local_solve(parent, residual, slots, diag_inverse, coupling, after)
    zslots, held = lax.optimization_barrier((zslots, held))

    returned = []
    for axis_pos, axis in enumerate(AXES):
        low, high, _ = halo_back(
            zslots[:, (2 * axis_pos) * face_w : (2 * axis_pos + 1) * face_w],
            zslots[:, (2 * axis_pos + 1) * face_w : (2 * axis_pos + 2) * face_w],
            axis,
        )
        returned += [low, high]
    returned = jnp.concatenate(returned, axis=1)

    solved_t = jnp.dot(
        coarse_inverse, rows_of(held), precision=lax.Precision.HIGHEST, preferred_element_type=jnp.float32
    )
    return finish(send_rows, counts, own, returned, solved_t.T, deflation)


def solution(mesh):
    return jax.shard_map(
        per_device,
        mesh=mesh,
        in_specs=(
            P(None, AXES),
            P(AXES, None, None),
            P(AXES, None, None),
            P(AXES),
            P(AXES, None),
            P(AXES),
            P(None, AXES),
            P(AXES, None),
        ),
        out_specs=P(None, AXES),
        check_vma=False,
    )
```

```python
import functools

import jax
import jax.numpy as jnp
from jax import lax
from jax.experimental import pallas as pl
from jax.experimental.pallas import tpu as pltpu
from jax.sharding import PartitionSpec as P

AXES = ("gx", "gy", "gz")
NT = (((1,), (1,)), ((), ()))


def solve_kernel(
    parent_ref, res_ref, slot_ref, inv_ref, cpl_ref, after_ref, own_ref, zslot_ref, y_ref, carry_ref
):
    del after_ref
    blocks_n, block_w, _ = inv_ref.shape
    owned_blocks = res_ref.shape[1] // block_w

    def columns(b):
        if b < owned_blocks:
            return res_ref, pl.ds(b * block_w, block_w)
        return slot_ref, pl.ds((b - owned_blocks) * block_w, block_w)

    def link(b):
        return jnp.clip(parent_ref[b], 0, blocks_n - 1)

    for b in range(blocks_n):
        ref, cols = columns(b)
        x = ref[:, cols]
        if b == 0:
            lower = x.astype(jnp.bfloat16)
        else:
            prior = y_ref[link(b)]
            lower = (
                x - lax.dot_general(prior, cpl_ref[b - 1], NT, preferred_element_type=jnp.float32)
            ).astype(jnp.bfloat16)
        y_ref[b] = lax.dot_general(
            lower, inv_ref[b], NT, preferred_element_type=jnp.float32
        ).astype(jnp.bfloat16)

    carry_ref[...] = jnp.zeros(carry_ref.shape, carry_ref.dtype)
    for b in reversed(range(blocks_n)):
        upper = (y_ref[b].astype(jnp.float32) - carry_ref[b]).astype(jnp.bfloat16)
        result = jnp.dot(upper, inv_ref[b], preferred_element_type=jnp.float32).astype(jnp.bfloat16)
        if b < owned_blocks:
            own_ref[:, pl.ds(b * block_w, block_w)] = result
        else:
            zslot_ref[:, pl.ds((b - owned_blocks) * block_w, block_w)] = result
        if b > 0:
            push = jnp.dot(result, cpl_ref[b - 1], preferred_element_type=jnp.float32)
            p = link(b)
            carry_ref[p] = carry_ref[p] + push


def local_solve(parent, residual, slots, diag_inverse, coupling, after):
    nrhs_here, owned_n = residual.shape
    blocks_n, block_w, _ = diag_inverse.shape
    vmem = pltpu.VMEM
    return pl.pallas_call(
        solve_kernel,
        out_shape=(
            jax.ShapeDtypeStruct((nrhs_here, owned_n), jnp.bfloat16),
            jax.ShapeDtypeStruct(slots.shape, jnp.bfloat16),
        ),
        in_specs=[
            pl.BlockSpec(memory_space=pltpu.SMEM),
            pl.BlockSpec(memory_space=vmem),
            pl.BlockSpec(memory_space=vmem),
            pl.BlockSpec(memory_space=vmem),
            pl.BlockSpec(memory_space=vmem),
            pl.BlockSpec(memory_space=pl.ANY),
        ],
        out_specs=(pl.BlockSpec(memory_space=vmem), pl.BlockSpec(memory_space=vmem)),
        scratch_shapes=[
            pltpu.VMEM((blocks_n, nrhs_here, block_w), jnp.bfloat16),
            pltpu.VMEM((blocks_n, nrhs_here, block_w), jnp.float32),
        ],
        compiler_params=pltpu.CompilerParams(vmem_limit_bytes=48 * 1024 * 1024),
    )(parent, residual, slots, diag_inverse, coupling, after)


def split3(value):
    first = value.astype(jnp.bfloat16)
    rest = value - first.astype(jnp.float32)
    second = rest.astype(jnp.bfloat16)
    third = (rest - second.astype(jnp.float32)).astype(jnp.bfloat16)
    return first, second, third


def finish_kernel(count_ref, rows_ref, own_ref, back_ref, solved_ref, vec_ref, out_ref):
    owned_n = own_ref.shape[1]
    kmax_here = vec_ref.shape[0]
    keep = lax.broadcasted_iota(jnp.int32, (kmax_here, 1), 0) < count_ref[0]
    chunk = 256
    rows = rows_ref[...]
    back = back_ref[...]
    s1, s2, s3 = split3(solved_ref[...])
    for start in range(0, owned_n, chunk):
        cols = pl.ds(start, chunk)
        here = lax.broadcasted_iota(jnp.int32, (rows.shape[0], chunk), 1) + start
        onehot = (rows == here).astype(jnp.bfloat16)
        total = own_ref[:, cols].astype(jnp.float32)
        total += jnp.dot(back, onehot, preferred_element_type=jnp.float32)
        v1, v2, v3 = split3(jnp.where(keep, vec_ref[:, cols], 0.0))
        for left, right in ((s1, v1), (s1, v2), (s2, v1), (s1, v3), (s3, v1), (s2, v2)):
            total += jnp.dot(left, right, preferred_element_type=jnp.float32)
        out_ref[:, cols] = total


def finish(send_rows, counts, own, returned, solved, deflation):
    vmem = pltpu.VMEM
    return pl.pallas_call(
        finish_kernel,
        out_shape=jax.ShapeDtypeStruct(own.shape, jnp.float32),
        in_specs=[pl.BlockSpec(memory_space=pltpu.SMEM)] + [pl.BlockSpec(memory_space=vmem)] * 5,
        out_specs=pl.BlockSpec(memory_space=vmem),
        compiler_params=pltpu.CompilerParams(vmem_limit_bytes=48 * 1024 * 1024),
    )(counts, send_rows.reshape(-1, 1), own, returned, solved, deflation)


def matchings(count):
    first = [(i, i + 1) for i in range(0, count - 1, 2)] + [(i + 1, i) for i in range(0, count - 1, 2)]
    second = [(i, i + 1) for i in range(1, count - 1, 2)] + [(i + 1, i) for i in range(1, count - 1, 2)]
    return first, second


def swap(value, axis, pairs, extra=None):
    if not pairs:
        return jnp.zeros_like(value), None
    if extra is None:
        return lax.ppermute(value, axis, pairs), None
    rows = value.shape[0]
    packed = jnp.concatenate([value.astype(extra.dtype), extra], axis=0)
    got = lax.ppermute(packed, axis, pairs)
    return got[:rows].astype(value.dtype), got[rows:]


def halo_out(down, up, axis, extra=None):
    even = lax.axis_index(axis) % 2 == 0
    first, second = matchings(lax.axis_size(axis))
    r1, got = swap(jnp.where(even, up, down), axis, first, extra)
    r2, _ = swap(jnp.where(even, down, up), axis, second)
    return jnp.where(even, r1, r2), jnp.where(even, r2, r1), got


def halo_back(lo, hi, axis, extra=None):
    even = lax.axis_index(axis) % 2 == 0
    first, second = matchings(lax.axis_size(axis))
    r1, got = swap(jnp.where(even, lo, hi), axis, first, extra)
    r2, _ = swap(jnp.where(even, hi, lo), axis, second)
    return jnp.where(even, r2, r1), jnp.where(even, r1, r2), got


def doubling(axis):
    count = lax.axis_size(axis)
    return count > 1 and not count & (count - 1)


def merge(held, other, axis, dim, step):
    low = (lax.axis_index(axis) // step) % 2 == 0
    return jnp.where(
        low,
        jnp.concatenate([held, other], axis=dim),
        jnp.concatenate([other, held], axis=dim),
    )


def gather_axis(held, axis, dim, step=1):
    count = lax.axis_size(axis)
    if not doubling(axis):
        return lax.all_gather(held, axis, axis=dim, tiled=True)
    while step < count:
        pairs = [(i, i ^ step) for i in range(count)]
        held = merge(held, lax.ppermute(held, axis, pairs), axis, dim, step)
        step *= 2
    return held


def rows_of(held):
    return held.reshape(-1, held.shape[-1])


def per_device(
    residual, diag_inverse, coupling, parent, send_rows, counts, deflation, coarse_inverse
):
    nrhs_here, owned_n = residual.shape
    slots_n, face_w = send_rows.shape
    kmax_here = deflation.shape[0]
    mask = (lax.iota(jnp.int32, kmax_here) < counts[0]).astype(jnp.float32)
    vectors = deflation * mask[:, None]
    coeffs_t = lax.dot_general(
        vectors, residual, NT, precision=lax.Precision.HIGHEST, preferred_element_type=jnp.float32
    )
    total_dev = coarse_inverse.shape[1] // kmax_here

    outgoing = jnp.take(residual, send_rows, axis=1)
    incoming = []
    for axis_pos, axis in enumerate(AXES):
        low, high, _ = halo_out(outgoing[:, 2 * axis_pos], outgoing[:, 2 * axis_pos + 1], axis)
        incoming += [low, high]
    slots = jnp.concatenate(incoming, axis=1)
    slots, coeffs_t = lax.optimization_barrier((slots, coeffs_t))
    last = len(AXES) - 1
    late = lax.axis_size(AXES[last]) == 2
    spread_axes = AXES[:last] if late else AXES
    spread_n = 1
    for axis in spread_axes:
        spread_n *= lax.axis_size(axis)
    spread = jnp.broadcast_to(coeffs_t[None], (spread_n,) + coeffs_t.shape)
    held = lax.all_to_all(spread, spread_axes, 0, 0, tiled=True)
    held = held.reshape(tuple(lax.axis_size(a) for a in spread_axes) + (1,) * (len(AXES) - len(spread_axes)) + coeffs_t.shape)
    after = coeffs_t

    own, zslots = local_solve(parent, residual, slots, diag_inverse, coupling, after)
    zslots, held = lax.optimization_barrier((zslots, held))

    returned = []
    for axis_pos, axis in enumerate(AXES):
        ride = axis_pos == last and late
        low, high, got = halo_back(
            zslots[:, (2 * axis_pos) * face_w : (2 * axis_pos + 1) * face_w],
            zslots[:, (2 * axis_pos + 1) * face_w : (2 * axis_pos + 2) * face_w],
            axis,
            rows_of(held) if ride else None,
        )
        returned += [low, high]
        if ride:
            held = merge(held, got.reshape(held.shape), axis, last, 1)
    returned = jnp.concatenate(returned, axis=1)

    solved_t = jnp.dot(
        coarse_inverse, rows_of(held), precision=lax.Precision.HIGHEST, preferred_element_type=jnp.float32
    )
    return finish(send_rows, counts, own, returned, solved_t.T, deflation)


def solution(mesh):
    return jax.shard_map(
        per_device,
        mesh=mesh,
        in_specs=(
            P(None, AXES),
            P(AXES, None, None),
            P(AXES, None, None),
            P(AXES),
            P(AXES, None),
            P(AXES),
            P(None, AXES),
            P(AXES, None),
        ),
        out_specs=P(None, AXES),
        check_vma=False,
    )
```

```python
import functools

import jax
import jax.numpy as jnp
from jax import lax
from jax.experimental import pallas as pl
from jax.experimental.pallas import tpu as pltpu
from jax.sharding import PartitionSpec as P

AXES = ("gx", "gy", "gz")
NT = (((1,), (1,)), ((), ()))


def solve_kernel(
    parent_ref, res_ref, slot_ref, inv_ref, cpl_ref, after_ref, own_ref, zslot_ref, y_ref, carry_ref
):
    del after_ref
    blocks_n, block_w, _ = inv_ref.shape
    owned_blocks = res_ref.shape[1] // block_w

    def columns(b):
        if b < owned_blocks:
            return res_ref, pl.ds(b * block_w, block_w)
        return slot_ref, pl.ds((b - owned_blocks) * block_w, block_w)

    def link(b):
        return jnp.clip(parent_ref[b], 0, blocks_n - 1)

    for b in range(blocks_n):
        ref, cols = columns(b)
        x = ref[:, cols]
        if b == 0:
            lower = x.astype(jnp.bfloat16)
        else:
            prior = y_ref[link(b)]
            lower = (
                x - lax.dot_general(prior, cpl_ref[b - 1], NT, preferred_element_type=jnp.float32)
            ).astype(jnp.bfloat16)
        y_ref[b] = lax.dot_general(
            lower, inv_ref[b], NT, preferred_element_type=jnp.float32
        ).astype(jnp.bfloat16)

    carry_ref[...] = jnp.zeros(carry_ref.shape, carry_ref.dtype)
    for b in reversed(range(blocks_n)):
        upper = (y_ref[b].astype(jnp.float32) - carry_ref[b]).astype(jnp.bfloat16)
        result = jnp.dot(upper, inv_ref[b], preferred_element_type=jnp.float32).astype(jnp.bfloat16)
        if b < owned_blocks:
            own_ref[:, pl.ds(b * block_w, block_w)] = result
        else:
            zslot_ref[:, pl.ds((b - owned_blocks) * block_w, block_w)] = result
        if b > 0:
            push = jnp.dot(result, cpl_ref[b - 1], preferred_element_type=jnp.float32)
            p = link(b)
            carry_ref[p] = carry_ref[p] + push


def local_solve(parent, residual, slots, diag_inverse, coupling, after):
    nrhs_here, owned_n = residual.shape
    blocks_n, block_w, _ = diag_inverse.shape
    vmem = pltpu.VMEM
    return pl.pallas_call(
        solve_kernel,
        out_shape=(
            jax.ShapeDtypeStruct((nrhs_here, owned_n), jnp.bfloat16),
            jax.ShapeDtypeStruct(slots.shape, jnp.bfloat16),
        ),
        in_specs=[
            pl.BlockSpec(memory_space=pltpu.SMEM),
            pl.BlockSpec(memory_space=vmem),
            pl.BlockSpec(memory_space=vmem),
            pl.BlockSpec(memory_space=vmem),
            pl.BlockSpec(memory_space=vmem),
            pl.BlockSpec(memory_space=pl.ANY),
        ],
        out_specs=(pl.BlockSpec(memory_space=vmem), pl.BlockSpec(memory_space=vmem)),
        scratch_shapes=[
            pltpu.VMEM((blocks_n, nrhs_here, block_w), jnp.bfloat16),
            pltpu.VMEM((blocks_n, nrhs_here, block_w), jnp.float32),
        ],
        compiler_params=pltpu.CompilerParams(vmem_limit_bytes=12 * 1024 * 1024),
    )(parent, residual, slots, diag_inverse, coupling, after)


def split3(value):
    first = value.astype(jnp.bfloat16)
    rest = value - first.astype(jnp.float32)
    second = rest.astype(jnp.bfloat16)
    third = (rest - second.astype(jnp.float32)).astype(jnp.bfloat16)
    return first, second, third


def finish_kernel(count_ref, rows_ref, own_ref, back_ref, solved_ref, vec_ref, out_ref):
    owned_n = own_ref.shape[1]
    kmax_here = vec_ref.shape[0]
    keep = lax.broadcasted_iota(jnp.int32, (kmax_here, 1), 0) < count_ref[0]
    chunk = 256
    rows = rows_ref[...]
    back = back_ref[...]
    s1, s2, s3 = split3(solved_ref[...])
    for start in range(0, owned_n, chunk):
        cols = pl.ds(start, chunk)
        here = lax.broadcasted_iota(jnp.int32, (rows.shape[0], chunk), 1) + start
        onehot = (rows == here).astype(jnp.bfloat16)
        total = own_ref[:, cols].astype(jnp.float32)
        total += jnp.dot(back, onehot, preferred_element_type=jnp.float32)
        v1, v2, v3 = split3(jnp.where(keep, vec_ref[:, cols], 0.0))
        for left, right in ((s1, v1), (s1, v2), (s2, v1), (s1, v3), (s3, v1), (s2, v2)):
            total += jnp.dot(left, right, preferred_element_type=jnp.float32)
        out_ref[:, cols] = total


def finish(send_rows, counts, own, returned, solved, deflation):
    vmem = pltpu.VMEM
    return pl.pallas_call(
        finish_kernel,
        out_shape=jax.ShapeDtypeStruct(own.shape, jnp.float32),
        in_specs=[pl.BlockSpec(memory_space=pltpu.SMEM)] + [pl.BlockSpec(memory_space=vmem)] * 5,
        out_specs=pl.BlockSpec(memory_space=vmem),
        compiler_params=pltpu.CompilerParams(vmem_limit_bytes=8 * 1024 * 1024),
    )(counts, send_rows.reshape(-1, 1), own, returned, solved, deflation)


def matchings(count):
    first = [(i, i + 1) for i in range(0, count - 1, 2)] + [(i + 1, i) for i in range(0, count - 1, 2)]
    second = [(i, i + 1) for i in range(1, count - 1, 2)] + [(i + 1, i) for i in range(1, count - 1, 2)]
    return first, second


def swap(value, axis, pairs, extra=None):
    if not pairs:
        return jnp.zeros_like(value), None
    if extra is None:
        return lax.ppermute(value, axis, pairs), None
    rows = value.shape[0]
    packed = jnp.concatenate([value.astype(extra.dtype), extra], axis=0)
    got = lax.ppermute(packed, axis, pairs)
    return got[:rows].astype(value.dtype), got[rows:]


def halo_out(down, up, axis, extra=None):
    even = lax.axis_index(axis) % 2 == 0
    first, second = matchings(lax.axis_size(axis))
    r1, got = swap(jnp.where(even, up, down), axis, first, extra)
    r2, _ = swap(jnp.where(even, down, up), axis, second)
    return jnp.where(even, r1, r2), jnp.where(even, r2, r1), got


def halo_back(lo, hi, axis, extra=None):
    even = lax.axis_index(axis) % 2 == 0
    first, second = matchings(lax.axis_size(axis))
    r1, got = swap(jnp.where(even, lo, hi), axis, first, extra)
    r2, _ = swap(jnp.where(even, hi, lo), axis, second)
    return jnp.where(even, r2, r1), jnp.where(even, r1, r2), got


def doubling(axis):
    count = lax.axis_size(axis)
    return count > 1 and not count & (count - 1)


def merge(held, other, axis, dim, step):
    low = (lax.axis_index(axis) // step) % 2 == 0
    return jnp.where(
        low,
        jnp.concatenate([held, other], axis=dim),
        jnp.concatenate([other, held], axis=dim),
    )


def gather_axis(held, axis, dim, step=1):
    count = lax.axis_size(axis)
    if not doubling(axis):
        return lax.all_gather(held, axis, axis=dim, tiled=True)
    while step < count:
        pairs = [(i, i ^ step) for i in range(count)]
        held = merge(held, lax.ppermute(held, axis, pairs), axis, dim, step)
        step *= 2
    return held


def rows_of(held):
    return held.reshape(-1, held.shape[-1])


def per_device(
    residual, diag_inverse, coupling, parent, send_rows, counts, deflation, coarse_inverse
):
    nrhs_here, owned_n = residual.shape
    slots_n, face_w = send_rows.shape
    kmax_here = deflation.shape[0]
    mask = (lax.iota(jnp.int32, kmax_here) < counts[0]).astype(jnp.float32)
    vectors = deflation * mask[:, None]
    coeffs_t = lax.dot_general(
        vectors, residual, NT, precision=lax.Precision.HIGHEST, preferred_element_type=jnp.float32
    )
    total_dev = coarse_inverse.shape[1] // kmax_here

    outgoing = jnp.take(residual, send_rows, axis=1)
    incoming = []
    for axis_pos, axis in enumerate(AXES):
        low, high, _ = halo_out(outgoing[:, 2 * axis_pos], outgoing[:, 2 * axis_pos + 1], axis)
        incoming += [low, high]
    slots = jnp.concatenate(incoming, axis=1)
    slots, coeffs_t = lax.optimization_barrier((slots, coeffs_t))
    spread = jnp.broadcast_to(coeffs_t[None], (total_dev,) + coeffs_t.shape)
    held = lax.all_to_all(spread, AXES, 0, 0, tiled=True)
    after = coeffs_t

    own, zslots = local_solve(parent, residual, slots, diag_inverse, coupling, after)
    zslots, held = lax.optimization_barrier((zslots, held))

    returned = []
    for axis_pos, axis in enumerate(AXES):
        low, high, _ = halo_back(
            zslots[:, (2 * axis_pos) * face_w : (2 * axis_pos + 1) * face_w],
            zslots[:, (2 * axis_pos + 1) * face_w : (2 * axis_pos + 2) * face_w],
            axis,
        )
        returned += [low, high]
    returned = jnp.concatenate(returned, axis=1)

    solved_t = jnp.dot(
        coarse_inverse, rows_of(held), precision=lax.Precision.HIGHEST, preferred_element_type=jnp.float32
    )
    return finish(send_rows, counts, own, returned, solved_t.T, deflation)


def solution(mesh):
    return jax.shard_map(
        per_device,
        mesh=mesh,
        in_specs=(
            P(None, AXES),
            P(AXES, None, None),
            P(AXES, None, None),
            P(AXES),
            P(AXES, None),
            P(AXES),
            P(None, AXES),
            P(AXES, None),
        ),
        out_specs=P(None, AXES),
        check_vma=False,
    )
```

```python
import functools

import jax
import jax.numpy as jnp
from jax import lax
from jax.experimental import pallas as pl
from jax.experimental.pallas import tpu as pltpu
from jax.sharding import PartitionSpec as P

AXES = ("gx", "gy", "gz")
NT = (((1,), (1,)), ((), ()))


def solve_kernel(
    parent_ref, res_ref, slot_ref, inv_ref, cpl_ref, after_ref, own_ref, zslot_ref, y_ref, carry_ref
):
    del after_ref
    blocks_n, block_w, _ = inv_ref.shape
    owned_blocks = res_ref.shape[1] // block_w

    def columns(b):
        if b < owned_blocks:
            return res_ref, pl.ds(b * block_w, block_w)
        return slot_ref, pl.ds((b - owned_blocks) * block_w, block_w)

    def link(b):
        return jnp.clip(parent_ref[b], 0, blocks_n - 1)

    for b in range(blocks_n):
        ref, cols = columns(b)
        x = ref[:, cols]
        if b == 0:
            lower = x.astype(jnp.bfloat16)
        else:
            prior = y_ref[link(b)]
            lower = (
                x - lax.dot_general(prior, cpl_ref[b - 1], NT, preferred_element_type=jnp.float32)
            ).astype(jnp.bfloat16)
        y_ref[b] = lax.dot_general(
            lower, inv_ref[b], NT, preferred_element_type=jnp.float32
        ).astype(jnp.bfloat16)

    carry_ref[...] = jnp.zeros(carry_ref.shape, carry_ref.dtype)
    for b in reversed(range(blocks_n)):
        upper = (y_ref[b].astype(jnp.float32) - carry_ref[b]).astype(jnp.bfloat16)
        result = jnp.dot(upper, inv_ref[b], preferred_element_type=jnp.float32).astype(jnp.bfloat16)
        if b < owned_blocks:
            own_ref[:, pl.ds(b * block_w, block_w)] = result
        else:
            zslot_ref[:, pl.ds((b - owned_blocks) * block_w, block_w)] = result
        if b > 0:
            push = jnp.dot(result, cpl_ref[b - 1], preferred_element_type=jnp.float32)
            p = link(b)
            carry_ref[p] = carry_ref[p] + push


def local_solve(parent, residual, slots, diag_inverse, coupling, after):
    nrhs_here, owned_n = residual.shape
    blocks_n, block_w, _ = diag_inverse.shape
    vmem = pltpu.VMEM
    return pl.pallas_call(
        solve_kernel,
        out_shape=(
            jax.ShapeDtypeStruct((nrhs_here, owned_n), jnp.bfloat16),
            jax.ShapeDtypeStruct(slots.shape, jnp.bfloat16),
        ),
        in_specs=[
            pl.BlockSpec(memory_space=pltpu.SMEM),
            pl.BlockSpec(memory_space=vmem),
            pl.BlockSpec(memory_space=vmem),
            pl.BlockSpec(memory_space=vmem),
            pl.BlockSpec(memory_space=vmem),
            pl.BlockSpec(memory_space=pl.ANY),
        ],
        out_specs=(pl.BlockSpec(memory_space=vmem), pl.BlockSpec(memory_space=vmem)),
        scratch_shapes=[
            pltpu.VMEM((blocks_n, nrhs_here, block_w), jnp.bfloat16),
            pltpu.VMEM((blocks_n, nrhs_here, block_w), jnp.float32),
        ],
        compiler_params=pltpu.CompilerParams(vmem_limit_bytes=48 * 1024 * 1024),
    )(parent, residual, slots, diag_inverse, coupling, after)


def split3(value):
    first = value.astype(jnp.bfloat16)
    rest = value - first.astype(jnp.float32)
    second = rest.astype(jnp.bfloat16)
    third = (rest - second.astype(jnp.float32)).astype(jnp.bfloat16)
    return first, second, third


def finish_kernel(count_ref, rows_ref, own_ref, back_ref, solved_ref, vec_ref, out_ref):
    owned_n = own_ref.shape[1]
    kmax_here = vec_ref.shape[0]
    keep = lax.broadcasted_iota(jnp.int32, (kmax_here, 1), 0) < count_ref[0]
    chunk = 256
    rows = rows_ref[...]
    back = back_ref[...]
    s1, s2, s3 = split3(solved_ref[...])
    for start in range(0, owned_n, chunk):
        cols = pl.ds(start, chunk)
        here = lax.broadcasted_iota(jnp.int32, (rows.shape[0], chunk), 1) + start
        onehot = (rows == here).astype(jnp.bfloat16)
        total = own_ref[:, cols].astype(jnp.float32)
        total += jnp.dot(back, onehot, preferred_element_type=jnp.float32)
        v1, v2, _ = split3(jnp.where(keep, vec_ref[:, cols], 0.0))
        for left, right in ((s1, v1), (s1, v2), (s2, v1)):
            total += jnp.dot(left, right, preferred_element_type=jnp.float32)
        out_ref[:, cols] = total


def finish(send_rows, counts, own, returned, solved, deflation):
    vmem = pltpu.VMEM
    return pl.pallas_call(
        finish_kernel,
        out_shape=jax.ShapeDtypeStruct(own.shape, jnp.float32),
        in_specs=[pl.BlockSpec(memory_space=pltpu.SMEM)] + [pl.BlockSpec(memory_space=vmem)] * 5,
        out_specs=pl.BlockSpec(memory_space=vmem),
        compiler_params=pltpu.CompilerParams(vmem_limit_bytes=48 * 1024 * 1024),
    )(counts, send_rows.reshape(-1, 1), own, returned, solved, deflation)


def matchings(count):
    first = [(i, i + 1) for i in range(0, count - 1, 2)] + [(i + 1, i) for i in range(0, count - 1, 2)]
    second = [(i, i + 1) for i in range(1, count - 1, 2)] + [(i + 1, i) for i in range(1, count - 1, 2)]
    return first, second


def swap(value, axis, pairs, extra=None):
    if not pairs:
        return jnp.zeros_like(value), None
    if extra is None:
        return lax.ppermute(value, axis, pairs), None
    rows = value.shape[0]
    packed = jnp.concatenate([value.astype(extra.dtype), extra], axis=0)
    got = lax.ppermute(packed, axis, pairs)
    return got[:rows].astype(value.dtype), got[rows:]


def halo_out(down, up, axis, extra=None):
    even = lax.axis_index(axis) % 2 == 0
    first, second = matchings(lax.axis_size(axis))
    r1, got = swap(jnp.where(even, up, down), axis, first, extra)
    r2, _ = swap(jnp.where(even, down, up), axis, second)
    return jnp.where(even, r1, r2), jnp.where(even, r2, r1), got


def halo_back(lo, hi, axis, extra=None):
    even = lax.axis_index(axis) % 2 == 0
    first, second = matchings(lax.axis_size(axis))
    r1, got = swap(jnp.where(even, lo, hi), axis, first, extra)
    r2, _ = swap(jnp.where(even, hi, lo), axis, second)
    return jnp.where(even, r2, r1), jnp.where(even, r1, r2), got


def doubling(axis):
    count = lax.axis_size(axis)
    return count > 1 and not count & (count - 1)


def merge(held, other, axis, dim, step):
    low = (lax.axis_index(axis) // step) % 2 == 0
    return jnp.where(
        low,
        jnp.concatenate([held, other], axis=dim),
        jnp.concatenate([other, held], axis=dim),
    )


def gather_axis(held, axis, dim, step=1):
    count = lax.axis_size(axis)
    if not doubling(axis):
        return lax.all_gather(held, axis, axis=dim, tiled=True)
    while step < count:
        pairs = [(i, i ^ step) for i in range(count)]
        held = merge(held, lax.ppermute(held, axis, pairs), axis, dim, step)
        step *= 2
    return held


def rows_of(held):
    return held.reshape(-1, held.shape[-1])


def per_device(
    residual, diag_inverse, coupling, parent, send_rows, counts, deflation, coarse_inverse
):
    nrhs_here, owned_n = residual.shape
    slots_n, face_w = send_rows.shape
    kmax_here = deflation.shape[0]
    mask = (lax.iota(jnp.int32, kmax_here) < counts[0]).astype(jnp.float32)
    vectors = deflation * mask[:, None]
    coeffs_t = lax.dot_general(
        vectors, residual, NT, precision=lax.Precision.HIGH, preferred_element_type=jnp.float32
    )
    total_dev = coarse_inverse.shape[1] // kmax_here

    outgoing = jnp.take(residual, send_rows, axis=1)
    incoming = []
    for axis_pos, axis in enumerate(AXES):
        low, high, _ = halo_out(outgoing[:, 2 * axis_pos], outgoing[:, 2 * axis_pos + 1], axis)
        incoming += [low, high]
    slots = jnp.concatenate(incoming, axis=1)
    slots, coeffs_t = lax.optimization_barrier((slots, coeffs_t))
    spread = jnp.broadcast_to(coeffs_t[None], (total_dev,) + coeffs_t.shape)
    held = lax.all_to_all(spread, AXES, 0, 0, tiled=True)
    after = coeffs_t

    own, zslots = local_solve(parent, residual, slots, diag_inverse, coupling, after)
    zslots, held = lax.optimization_barrier((zslots, held))

    returned = []
    for axis_pos, axis in enumerate(AXES):
        low, high, _ = halo_back(
            zslots[:, (2 * axis_pos) * face_w : (2 * axis_pos + 1) * face_w],
            zslots[:, (2 * axis_pos + 1) * face_w : (2 * axis_pos + 2) * face_w],
            axis,
        )
        returned += [low, high]
    returned = jnp.concatenate(returned, axis=1)

    solved_t = jnp.dot(
        coarse_inverse, rows_of(held), precision=lax.Precision.HIGH, preferred_element_type=jnp.float32
    )
    return finish(send_rows, counts, own, returned, solved_t.T, deflation)


def solution(mesh):
    return jax.shard_map(
        per_device,
        mesh=mesh,
        in_specs=(
            P(None, AXES),
            P(AXES, None, None),
            P(AXES, None, None),
            P(AXES),
            P(AXES, None),
            P(AXES),
            P(None, AXES),
            P(AXES, None),
        ),
        out_specs=P(None, AXES),
        check_vma=False,
    )
```

```python
import functools

import jax
import jax.numpy as jnp
from jax import lax
from jax.experimental import pallas as pl
from jax.experimental.pallas import tpu as pltpu
from jax.sharding import PartitionSpec as P

AXES = ("gx", "gy", "gz")
NT = (((1,), (1,)), ((), ()))


def solve_kernel(
    parent_ref, res_ref, slot_ref, inv_ref, cpl_ref, after_ref, own_ref, zslot_ref, y_ref, carry_ref
):
    del after_ref
    blocks_n, block_w, _ = inv_ref.shape
    owned_blocks = res_ref.shape[1] // block_w

    def columns(b):
        if b < owned_blocks:
            return res_ref, pl.ds(b * block_w, block_w)
        return slot_ref, pl.ds((b - owned_blocks) * block_w, block_w)

    def link(b):
        return jnp.clip(parent_ref[b], 0, blocks_n - 1)

    for b in range(blocks_n):
        ref, cols = columns(b)
        x = ref[:, cols]
        if b == 0:
            lower = x.astype(jnp.bfloat16)
        else:
            prior = y_ref[link(b)]
            lower = (
                x - lax.dot_general(prior, cpl_ref[b - 1], NT, preferred_element_type=jnp.float32)
            ).astype(jnp.bfloat16)
        y_ref[b] = lax.dot_general(
            lower, inv_ref[b], NT, preferred_element_type=jnp.float32
        ).astype(jnp.bfloat16)

    carry_ref[...] = jnp.zeros(carry_ref.shape, carry_ref.dtype)
    for b in reversed(range(blocks_n)):
        upper = (y_ref[b].astype(jnp.float32) - carry_ref[b]).astype(jnp.bfloat16)
        result = jnp.dot(upper, inv_ref[b], preferred_element_type=jnp.float32).astype(jnp.bfloat16)
        if b < owned_blocks:
            own_ref[:, pl.ds(b * block_w, block_w)] = result
        else:
            zslot_ref[:, pl.ds((b - owned_blocks) * block_w, block_w)] = result
        if b > 0:
            push = jnp.dot(result, cpl_ref[b - 1], preferred_element_type=jnp.float32)
            p = link(b)
            carry_ref[p] = carry_ref[p] + push


def local_solve(parent, residual, slots, diag_inverse, coupling, after):
    nrhs_here, owned_n = residual.shape
    blocks_n, block_w, _ = diag_inverse.shape
    vmem = pltpu.VMEM
    return pl.pallas_call(
        solve_kernel,
        out_shape=(
            jax.ShapeDtypeStruct((nrhs_here, owned_n), jnp.bfloat16),
            jax.ShapeDtypeStruct(slots.shape, jnp.bfloat16),
        ),
        in_specs=[
            pl.BlockSpec(memory_space=pltpu.SMEM),
            pl.BlockSpec(memory_space=vmem),
            pl.BlockSpec(memory_space=vmem),
            pl.BlockSpec(memory_space=vmem),
            pl.BlockSpec(memory_space=vmem),
            pl.BlockSpec(memory_space=pl.ANY),
        ],
        out_specs=(pl.BlockSpec(memory_space=vmem), pl.BlockSpec(memory_space=vmem)),
        scratch_shapes=[
            pltpu.VMEM((blocks_n, nrhs_here, block_w), jnp.bfloat16),
            pltpu.VMEM((blocks_n, nrhs_here, block_w), jnp.float32),
        ],
        compiler_params=pltpu.CompilerParams(vmem_limit_bytes=48 * 1024 * 1024),
    )(parent, residual, slots, diag_inverse, coupling, after)


def split3(value):
    first = value.astype(jnp.bfloat16)
    rest = value - first.astype(jnp.float32)
    second = rest.astype(jnp.bfloat16)
    third = (rest - second.astype(jnp.float32)).astype(jnp.bfloat16)
    return first, second, third


def finish_kernel(count_ref, rows_ref, own_ref, back_ref, solved_ref, vec_ref, out_ref):
    owned_n = own_ref.shape[1]
    kmax_here = vec_ref.shape[0]
    keep = lax.broadcasted_iota(jnp.int32, (kmax_here, 1), 0) < count_ref[0]
    chunk = 512
    rows = rows_ref[...]
    back = back_ref[...]
    s1, s2, _ = split3(solved_ref[...])
    for start in range(0, owned_n, chunk):
        width = min(chunk, owned_n - start)
        cols = pl.ds(start, width)
        here = lax.broadcasted_iota(jnp.int32, (rows.shape[0], width), 1) + start
        onehot = (rows == here).astype(jnp.bfloat16)
        total = own_ref[:, cols].astype(jnp.float32)
        total += jnp.dot(back, onehot, preferred_element_type=jnp.float32)
        v1, v2, _ = split3(jnp.where(keep, vec_ref[:, cols], 0.0))
        for left, right in ((s1, v1), (s1, v2), (s2, v1)):
            total += jnp.dot(left, right, preferred_element_type=jnp.float32)
        out_ref[:, cols] = total


def finish(send_rows, counts, own, returned, solved, deflation):
    vmem = pltpu.VMEM
    return pl.pallas_call(
        finish_kernel,
        out_shape=jax.ShapeDtypeStruct(own.shape, jnp.float32),
        in_specs=[pl.BlockSpec(memory_space=pltpu.SMEM)] + [pl.BlockSpec(memory_space=vmem)] * 5,
        out_specs=pl.BlockSpec(memory_space=vmem),
        compiler_params=pltpu.CompilerParams(vmem_limit_bytes=48 * 1024 * 1024),
    )(counts, send_rows.reshape(-1, 1), own, returned, solved, deflation)


def matchings(count):
    first = [(i, i + 1) for i in range(0, count - 1, 2)] + [(i + 1, i) for i in range(0, count - 1, 2)]
    second = [(i, i + 1) for i in range(1, count - 1, 2)] + [(i + 1, i) for i in range(1, count - 1, 2)]
    return first, second


def swap(value, axis, pairs, extra=None):
    if not pairs:
        return jnp.zeros_like(value), None
    if extra is None:
        return lax.ppermute(value, axis, pairs), None
    rows = value.shape[0]
    packed = jnp.concatenate([value.astype(extra.dtype), extra], axis=0)
    got = lax.ppermute(packed, axis, pairs)
    return got[:rows].astype(value.dtype), got[rows:]


def halo_out(down, up, axis, extra=None):
    even = lax.axis_index(axis) % 2 == 0
    first, second = matchings(lax.axis_size(axis))
    r1, got = swap(jnp.where(even, up, down), axis, first, extra)
    r2, _ = swap(jnp.where(even, down, up), axis, second)
    return jnp.where(even, r1, r2), jnp.where(even, r2, r1), got


def halo_back(lo, hi, axis, extra=None):
    even = lax.axis_index(axis) % 2 == 0
    first, second = matchings(lax.axis_size(axis))
    r1, got = swap(jnp.where(even, lo, hi), axis, first, extra)
    r2, _ = swap(jnp.where(even, hi, lo), axis, second)
    return jnp.where(even, r2, r1), jnp.where(even, r1, r2), got


def doubling(axis):
    count = lax.axis_size(axis)
    return count > 1 and not count & (count - 1)


def merge(held, other, axis, dim, step):
    low = (lax.axis_index(axis) // step) % 2 == 0
    return jnp.where(
        low,
        jnp.concatenate([held, other], axis=dim),
        jnp.concatenate([other, held], axis=dim),
    )


def gather_axis(held, axis, dim, step=1):
    count = lax.axis_size(axis)
    if not doubling(axis):
        return lax.all_gather(held, axis, axis=dim, tiled=True)
    while step < count:
        pairs = [(i, i ^ step) for i in range(count)]
        held = merge(held, lax.ppermute(held, axis, pairs), axis, dim, step)
        step *= 2
    return held


def rows_of(held):
    return held.reshape(-1, held.shape[-1])


def per_device(
    residual, diag_inverse, coupling, parent, send_rows, counts, deflation, coarse_inverse
):
    nrhs_here, owned_n = residual.shape
    slots_n, face_w = send_rows.shape
    kmax_here = deflation.shape[0]
    mask = (lax.iota(jnp.int32, kmax_here) < counts[0]).astype(jnp.float32)
    vectors = deflation * mask[:, None]
    coeffs_t = lax.dot_general(
        vectors, residual, NT, precision=lax.Precision.HIGH, preferred_element_type=jnp.float32
    )
    total_dev = coarse_inverse.shape[1] // kmax_here

    outgoing = jnp.take(residual, send_rows, axis=1)
    incoming = []
    for axis_pos, axis in enumerate(AXES):
        low, high, _ = halo_out(outgoing[:, 2 * axis_pos], outgoing[:, 2 * axis_pos + 1], axis)
        incoming += [low, high]
    slots = jnp.concatenate(incoming, axis=1)
    slots, coeffs_t = lax.optimization_barrier((slots, coeffs_t))
    spread = jnp.broadcast_to(coeffs_t[None], (total_dev,) + coeffs_t.shape)
    held = lax.all_to_all(spread, AXES, 0, 0, tiled=True)
    after = coeffs_t

    own, zslots = local_solve(parent, residual, slots, diag_inverse, coupling, after)
    zslots, held = lax.optimization_barrier((zslots, held))

    returned = []
    for axis_pos, axis in enumerate(AXES):
        low, high, _ = halo_back(
            zslots[:, (2 * axis_pos) * face_w : (2 * axis_pos + 1) * face_w],
            zslots[:, (2 * axis_pos + 1) * face_w : (2 * axis_pos + 2) * face_w],
            axis,
        )
        returned += [low, high]
    returned = jnp.concatenate(returned, axis=1)

    solved_t = jnp.dot(
        coarse_inverse, rows_of(held), precision=lax.Precision.HIGH, preferred_element_type=jnp.float32
    )
    return finish(send_rows, counts, own, returned, solved_t.T, deflation)


def solution(mesh):
    return jax.shard_map(
        per_device,
        mesh=mesh,
        in_specs=(
            P(None, AXES),
            P(AXES, None, None),
            P(AXES, None, None),
            P(AXES),
            P(AXES, None),
            P(AXES),
            P(None, AXES),
            P(AXES, None),
        ),
        out_specs=P(None, AXES),
        check_vma=False,
    )
```

```python
import functools

import jax
import jax.numpy as jnp
from jax import lax
from jax.experimental import pallas as pl
from jax.experimental.pallas import tpu as pltpu
from jax.sharding import PartitionSpec as P

AXES = ("gx", "gy", "gz")
NT = (((1,), (1,)), ((), ()))


def solve_kernel(
    parent_ref, res_ref, slot_ref, inv_ref, cpl_ref, after_ref, own_ref, zslot_ref, y_ref, carry_ref
):
    del after_ref
    blocks_n, block_w, _ = inv_ref.shape
    owned_blocks = res_ref.shape[1] // block_w

    def columns(b):
        if b < owned_blocks:
            return res_ref, pl.ds(b * block_w, block_w)
        return slot_ref, pl.ds((b - owned_blocks) * block_w, block_w)

    def link(b):
        return jnp.clip(parent_ref[b], 0, blocks_n - 1)

    for b in range(blocks_n):
        carry_ref[b] = jnp.zeros(carry_ref.shape[1:], carry_ref.dtype)
        ref, cols = columns(b)
        x = ref[:, cols]
        if b == 0:
            lower = x.astype(jnp.bfloat16)
        else:
            prior = y_ref[link(b)]
            lower = (
                x - lax.dot_general(prior, cpl_ref[b - 1], NT, preferred_element_type=jnp.float32)
            ).astype(jnp.bfloat16)
        y_ref[b] = lax.dot_general(
            lower, inv_ref[b], NT, preferred_element_type=jnp.float32
        ).astype(jnp.bfloat16)

    for b in reversed(range(blocks_n)):
        upper = (y_ref[b].astype(jnp.float32) - carry_ref[b]).astype(jnp.bfloat16)
        result = jnp.dot(upper, inv_ref[b], preferred_element_type=jnp.float32).astype(jnp.bfloat16)
        if b < owned_blocks:
            own_ref[:, pl.ds(b * block_w, block_w)] = result
        else:
            zslot_ref[:, pl.ds((b - owned_blocks) * block_w, block_w)] = result
        if b > 0:
            push = jnp.dot(result, cpl_ref[b - 1], preferred_element_type=jnp.float32)
            p = link(b)
            carry_ref[p] = carry_ref[p] + push


def local_solve(parent, residual, slots, diag_inverse, coupling, after):
    nrhs_here, owned_n = residual.shape
    blocks_n, block_w, _ = diag_inverse.shape
    vmem = pltpu.VMEM
    return pl.pallas_call(
        solve_kernel,
        out_shape=(
            jax.ShapeDtypeStruct((nrhs_here, owned_n), jnp.bfloat16),
            jax.ShapeDtypeStruct(slots.shape, jnp.bfloat16),
        ),
        in_specs=[
            pl.BlockSpec(memory_space=pltpu.SMEM),
            pl.BlockSpec(memory_space=vmem),
            pl.BlockSpec(memory_space=vmem),
            pl.BlockSpec(memory_space=vmem),
            pl.BlockSpec(memory_space=vmem),
            pl.BlockSpec(memory_space=pl.ANY),
        ],
        out_specs=(pl.BlockSpec(memory_space=vmem), pl.BlockSpec(memory_space=vmem)),
        scratch_shapes=[
            pltpu.VMEM((blocks_n, nrhs_here, block_w), jnp.bfloat16),
            pltpu.VMEM((blocks_n, nrhs_here, block_w), jnp.float32),
        ],
        compiler_params=pltpu.CompilerParams(vmem_limit_bytes=48 * 1024 * 1024),
    )(parent, residual, slots, diag_inverse, coupling, after)


def split3(value):
    first = value.astype(jnp.bfloat16)
    rest = value - first.astype(jnp.float32)
    second = rest.astype(jnp.bfloat16)
    third = (rest - second.astype(jnp.float32)).astype(jnp.bfloat16)
    return first, second, third


def finish_kernel(count_ref, rows_ref, own_ref, back_ref, solved_ref, vec_ref, out_ref):
    owned_n = own_ref.shape[1]
    kmax_here = vec_ref.shape[0]
    keep = lax.broadcasted_iota(jnp.int32, (kmax_here, 1), 0) < count_ref[0]
    chunk = 512
    rows = rows_ref[...]
    back = back_ref[...]
    s1, s2, _ = split3(solved_ref[...])
    for start in range(0, owned_n, chunk):
        width = min(chunk, owned_n - start)
        cols = pl.ds(start, width)
        here = lax.broadcasted_iota(jnp.int32, (rows.shape[0], width), 1) + start
        onehot = (rows == here).astype(jnp.bfloat16)
        total = own_ref[:, cols].astype(jnp.float32)
        total += jnp.dot(back, onehot, preferred_element_type=jnp.float32)
        v1, v2, _ = split3(jnp.where(keep, vec_ref[:, cols], 0.0))
        for left, right in ((s1, v1), (s1, v2), (s2, v1)):
            total += jnp.dot(left, right, preferred_element_type=jnp.float32)
        out_ref[:, cols] = total


def finish(send_rows, counts, own, returned, solved, deflation):
    vmem = pltpu.VMEM
    return pl.pallas_call(
        finish_kernel,
        out_shape=jax.ShapeDtypeStruct(own.shape, jnp.float32),
        in_specs=[pl.BlockSpec(memory_space=pltpu.SMEM)] + [pl.BlockSpec(memory_space=vmem)] * 5,
        out_specs=pl.BlockSpec(memory_space=vmem),
        compiler_params=pltpu.CompilerParams(vmem_limit_bytes=48 * 1024 * 1024),
    )(counts, send_rows.reshape(-1, 1), own, returned, solved, deflation)


def matchings(count):
    first = [(i, i + 1) for i in range(0, count - 1, 2)] + [(i + 1, i) for i in range(0, count - 1, 2)]
    second = [(i, i + 1) for i in range(1, count - 1, 2)] + [(i + 1, i) for i in range(1, count - 1, 2)]
    return first, second


def swap(value, axis, pairs, extra=None):
    if not pairs:
        return jnp.zeros_like(value), None
    if extra is None:
        return lax.ppermute(value, axis, pairs), None
    rows = value.shape[0]
    packed = jnp.concatenate([value.astype(extra.dtype), extra], axis=0)
    got = lax.ppermute(packed, axis, pairs)
    return got[:rows].astype(value.dtype), got[rows:]


def halo_out(down, up, axis, extra=None):
    even = lax.axis_index(axis) % 2 == 0
    first, second = matchings(lax.axis_size(axis))
    r1, got = swap(jnp.where(even, up, down), axis, first, extra)
    r2, _ = swap(jnp.where(even, down, up), axis, second)
    return jnp.where(even, r1, r2), jnp.where(even, r2, r1), got


def halo_back(lo, hi, axis, extra=None):
    even = lax.axis_index(axis) % 2 == 0
    first, second = matchings(lax.axis_size(axis))
    r1, got = swap(jnp.where(even, lo, hi), axis, first, extra)
    r2, _ = swap(jnp.where(even, hi, lo), axis, second)
    return jnp.where(even, r2, r1), jnp.where(even, r1, r2), got


def doubling(axis):
    count = lax.axis_size(axis)
    return count > 1 and not count & (count - 1)


def merge(held, other, axis, dim, step):
    low = (lax.axis_index(axis) // step) % 2 == 0
    return jnp.where(
        low,
        jnp.concatenate([held, other], axis=dim),
        jnp.concatenate([other, held], axis=dim),
    )


def gather_axis(held, axis, dim, step=1):
    count = lax.axis_size(axis)
    if not doubling(axis):
        return lax.all_gather(held, axis, axis=dim, tiled=True)
    while step < count:
        pairs = [(i, i ^ step) for i in range(count)]
        held = merge(held, lax.ppermute(held, axis, pairs), axis, dim, step)
        step *= 2
    return held


def rows_of(held):
    return held.reshape(-1, held.shape[-1])


def per_device(
    residual, diag_inverse, coupling, parent, send_rows, counts, deflation, coarse_inverse
):
    nrhs_here, owned_n = residual.shape
    slots_n, face_w = send_rows.shape
    kmax_here = deflation.shape[0]
    mask = (lax.iota(jnp.int32, kmax_here) < counts[0]).astype(jnp.float32)
    vectors = deflation * mask[:, None]
    coeffs_t = lax.dot_general(
        vectors, residual, NT, precision=lax.Precision.HIGH, preferred_element_type=jnp.float32
    )
    total_dev = coarse_inverse.shape[1] // kmax_here

    outgoing = jnp.take(residual, send_rows, axis=1)
    incoming = []
    for axis_pos, axis in enumerate(AXES):
        low, high, _ = halo_out(outgoing[:, 2 * axis_pos], outgoing[:, 2 * axis_pos + 1], axis)
        incoming += [low, high]
    slots = jnp.concatenate(incoming, axis=1)
    slots, coeffs_t = lax.optimization_barrier((slots, coeffs_t))
    spread = jnp.broadcast_to(coeffs_t[None], (total_dev,) + coeffs_t.shape)
    held = lax.all_to_all(spread, AXES, 0, 0, tiled=True)
    after = coeffs_t

    own, zslots = local_solve(parent, residual, slots, diag_inverse, coupling, after)
    zslots, held = lax.optimization_barrier((zslots, held))

    returned = []
    for axis_pos, axis in enumerate(AXES):
        low, high, _ = halo_back(
            zslots[:, (2 * axis_pos) * face_w : (2 * axis_pos + 1) * face_w],
            zslots[:, (2 * axis_pos + 1) * face_w : (2 * axis_pos + 2) * face_w],
            axis,
        )
        returned += [low, high]
    returned = jnp.concatenate(returned, axis=1)

    solved_t = jnp.dot(
        coarse_inverse, rows_of(held), precision=lax.Precision.HIGH, preferred_element_type=jnp.float32
    )
    return finish(send_rows, counts, own, returned, solved_t.T, deflation)


def solution(mesh):
    return jax.shard_map(
        per_device,
        mesh=mesh,
        in_specs=(
            P(None, AXES),
            P(AXES, None, None),
            P(AXES, None, None),
            P(AXES),
            P(AXES, None),
            P(AXES),
            P(None, AXES),
            P(AXES, None),
        ),
        out_specs=P(None, AXES),
        check_vma=False,
    )
```

```python
import functools

import jax
import jax.numpy as jnp
from jax import lax
from jax.experimental import pallas as pl
from jax.experimental.pallas import tpu as pltpu
from jax.sharding import PartitionSpec as P

AXES = ("gx", "gy", "gz")
NT = (((1,), (1,)), ((), ()))


def solve_kernel(
    parent_ref, res_ref, slot_ref, inv_ref, cpl_ref, after_ref, own_ref, zslot_ref, y_ref, carry_ref
):
    del after_ref
    blocks_n, block_w, _ = inv_ref.shape
    owned_blocks = res_ref.shape[1] // block_w

    def columns(b):
        if b < owned_blocks:
            return res_ref, pl.ds(b * block_w, block_w)
        return slot_ref, pl.ds((b - owned_blocks) * block_w, block_w)

    def link(b):
        return jnp.clip(parent_ref[b], 0, blocks_n - 1)

    for b in range(blocks_n):
        ref, cols = columns(b)
        if b < owned_blocks:
            x = ref[:, cols]
        else:
            x = ref[cols, :].T
        if b == 0:
            lower = x.astype(jnp.bfloat16)
        else:
            prior = y_ref[link(b)]
            lower = (
                x - lax.dot_general(prior, cpl_ref[b - 1], NT, preferred_element_type=jnp.float32)
            ).astype(jnp.bfloat16)
        y_ref[b] = lax.dot_general(
            lower, inv_ref[b], NT, preferred_element_type=jnp.float32
        ).astype(jnp.bfloat16)

    carry_ref[...] = jnp.zeros(carry_ref.shape, carry_ref.dtype)
    for b in reversed(range(blocks_n)):
        upper = (y_ref[b].astype(jnp.float32) - carry_ref[b]).astype(jnp.bfloat16)
        result = jnp.dot(upper, inv_ref[b], preferred_element_type=jnp.float32).astype(jnp.bfloat16)
        if b < owned_blocks:
            own_ref[:, pl.ds(b * block_w, block_w)] = result
        else:
            zslot_ref[:, pl.ds((b - owned_blocks) * block_w, block_w)] = result
        if b > 0:
            push = jnp.dot(result, cpl_ref[b - 1], preferred_element_type=jnp.float32)
            p = link(b)
            carry_ref[p] = carry_ref[p] + push


def local_solve(parent, residual, slots, diag_inverse, coupling, after):
    nrhs_here, owned_n = residual.shape
    blocks_n, block_w, _ = diag_inverse.shape
    vmem = pltpu.VMEM
    return pl.pallas_call(
        solve_kernel,
        out_shape=(
            jax.ShapeDtypeStruct((nrhs_here, owned_n), jnp.bfloat16),
            jax.ShapeDtypeStruct(slots.shape[::-1], jnp.bfloat16),
        ),
        in_specs=[
            pl.BlockSpec(memory_space=pltpu.SMEM),
            pl.BlockSpec(memory_space=vmem),
            pl.BlockSpec(memory_space=vmem),
            pl.BlockSpec(memory_space=vmem),
            pl.BlockSpec(memory_space=vmem),
            pl.BlockSpec(memory_space=pl.ANY),
        ],
        out_specs=(pl.BlockSpec(memory_space=vmem), pl.BlockSpec(memory_space=vmem)),
        scratch_shapes=[
            pltpu.VMEM((blocks_n, nrhs_here, block_w), jnp.bfloat16),
            pltpu.VMEM((blocks_n, nrhs_here, block_w), jnp.float32),
        ],
        compiler_params=pltpu.CompilerParams(vmem_limit_bytes=48 * 1024 * 1024),
    )(parent, residual, slots, diag_inverse, coupling, after)


def split3(value):
    first = value.astype(jnp.bfloat16)
    rest = value - first.astype(jnp.float32)
    second = rest.astype(jnp.bfloat16)
    third = (rest - second.astype(jnp.float32)).astype(jnp.bfloat16)
    return first, second, third


def finish_kernel(count_ref, rows_ref, own_ref, back_ref, solved_ref, vec_ref, out_ref):
    owned_n = own_ref.shape[1]
    kmax_here = vec_ref.shape[0]
    keep = lax.broadcasted_iota(jnp.int32, (kmax_here, 1), 0) < count_ref[0]
    chunk = 512
    rows = rows_ref[...]
    back = back_ref[...]
    s1, s2, _ = split3(solved_ref[...])
    for start in range(0, owned_n, chunk):
        width = min(chunk, owned_n - start)
        cols = pl.ds(start, width)
        here = lax.broadcasted_iota(jnp.int32, (rows.shape[0], width), 1) + start
        onehot = (rows == here).astype(jnp.bfloat16)
        total = own_ref[:, cols].astype(jnp.float32)
        total += jnp.dot(back, onehot, preferred_element_type=jnp.float32)
        v1, v2, _ = split3(jnp.where(keep, vec_ref[:, cols], 0.0))
        for left, right in ((s1, v1), (s1, v2), (s2, v1)):
            total += jnp.dot(left, right, preferred_element_type=jnp.float32)
        out_ref[:, cols] = total


def finish(send_rows, counts, own, returned, solved, deflation):
    vmem = pltpu.VMEM
    return pl.pallas_call(
        finish_kernel,
        out_shape=jax.ShapeDtypeStruct(own.shape, jnp.float32),
        in_specs=[pl.BlockSpec(memory_space=pltpu.SMEM)] + [pl.BlockSpec(memory_space=vmem)] * 5,
        out_specs=pl.BlockSpec(memory_space=vmem),
        compiler_params=pltpu.CompilerParams(vmem_limit_bytes=48 * 1024 * 1024),
    )(counts, send_rows.reshape(-1, 1), own, returned, solved, deflation)


def matchings(count):
    first = [(i, i + 1) for i in range(0, count - 1, 2)] + [(i + 1, i) for i in range(0, count - 1, 2)]
    second = [(i, i + 1) for i in range(1, count - 1, 2)] + [(i + 1, i) for i in range(1, count - 1, 2)]
    return first, second


def swap(value, axis, pairs, extra=None):
    if not pairs:
        return jnp.zeros_like(value), None
    if extra is None:
        return lax.ppermute(value, axis, pairs), None
    rows = value.shape[0]
    packed = jnp.concatenate([value.astype(extra.dtype), extra], axis=0)
    got = lax.ppermute(packed, axis, pairs)
    return got[:rows].astype(value.dtype), got[rows:]


def halo_out(down, up, axis, extra=None):
    even = lax.axis_index(axis) % 2 == 0
    first, second = matchings(lax.axis_size(axis))
    r1, got = swap(jnp.where(even, up, down), axis, first, extra)
    r2, _ = swap(jnp.where(even, down, up), axis, second)
    return jnp.where(even, r1, r2), jnp.where(even, r2, r1), got


def halo_back(lo, hi, axis, extra=None):
    even = lax.axis_index(axis) % 2 == 0
    first, second = matchings(lax.axis_size(axis))
    r1, got = swap(jnp.where(even, lo, hi), axis, first, extra)
    r2, _ = swap(jnp.where(even, hi, lo), axis, second)
    return jnp.where(even, r2, r1), jnp.where(even, r1, r2), got


def doubling(axis):
    count = lax.axis_size(axis)
    return count > 1 and not count & (count - 1)


def merge(held, other, axis, dim, step):
    low = (lax.axis_index(axis) // step) % 2 == 0
    return jnp.where(
        low,
        jnp.concatenate([held, other], axis=dim),
        jnp.concatenate([other, held], axis=dim),
    )


def gather_axis(held, axis, dim, step=1):
    count = lax.axis_size(axis)
    if not doubling(axis):
        return lax.all_gather(held, axis, axis=dim, tiled=True)
    while step < count:
        pairs = [(i, i ^ step) for i in range(count)]
        held = merge(held, lax.ppermute(held, axis, pairs), axis, dim, step)
        step *= 2
    return held


def rows_of(held):
    return held.reshape(-1, held.shape[-1])


def per_device(
    residual, diag_inverse, coupling, parent, send_rows, counts, deflation, coarse_inverse
):
    nrhs_here, owned_n = residual.shape
    slots_n, face_w = send_rows.shape
    kmax_here = deflation.shape[0]
    mask = (lax.iota(jnp.int32, kmax_here) < counts[0]).astype(jnp.float32)
    vectors = deflation * mask[:, None]
    coeffs_t = lax.dot_general(
        vectors, residual, NT, precision=lax.Precision.HIGH, preferred_element_type=jnp.float32
    )
    total_dev = coarse_inverse.shape[1] // kmax_here

    outgoing = jnp.take(residual.T, send_rows, axis=0)
    incoming = []
    for axis_pos, axis in enumerate(AXES):
        low, high, _ = halo_out(outgoing[2 * axis_pos], outgoing[2 * axis_pos + 1], axis)
        incoming += [low, high]
    slots = jnp.concatenate(incoming, axis=0)
    slots, coeffs_t = lax.optimization_barrier((slots, coeffs_t))
    spread = jnp.broadcast_to(coeffs_t[None], (total_dev,) + coeffs_t.shape)
    held = lax.all_to_all(spread, AXES, 0, 0, tiled=True)
    after = coeffs_t

    own, zslots = local_solve(parent, residual, slots, diag_inverse, coupling, after)
    zslots, held = lax.optimization_barrier((zslots, held))

    returned = []
    for axis_pos, axis in enumerate(AXES):
        low, high, _ = halo_back(
            zslots[:, (2 * axis_pos) * face_w : (2 * axis_pos + 1) * face_w],
            zslots[:, (2 * axis_pos + 1) * face_w : (2 * axis_pos + 2) * face_w],
            axis,
        )
        returned += [low, high]
    returned = jnp.concatenate(returned, axis=1)

    solved_t = jnp.dot(
        coarse_inverse, rows_of(held), precision=lax.Precision.HIGH, preferred_element_type=jnp.float32
    )
    return finish(send_rows, counts, own, returned, solved_t.T, deflation)


def solution(mesh):
    return jax.shard_map(
        per_device,
        mesh=mesh,
        in_specs=(
            P(None, AXES),
            P(AXES, None, None),
            P(AXES, None, None),
            P(AXES),
            P(AXES, None),
            P(AXES),
            P(None, AXES),
            P(AXES, None),
        ),
        out_specs=P(None, AXES),
        check_vma=False,
    )
```

```python
import functools

import jax
import jax.numpy as jnp
from jax import lax
from jax.experimental import pallas as pl
from jax.experimental.pallas import tpu as pltpu
from jax.sharding import PartitionSpec as P

AXES = ("gx", "gy", "gz")
NT = (((1,), (1,)), ((), ()))


def solve_kernel(
    parent_ref, res_ref, slot_ref, inv_ref, cpl_ref, after_ref, own_ref, zslot_ref, y_ref, carry_ref
):
    del after_ref
    blocks_n, block_w, _ = inv_ref.shape
    owned_blocks = res_ref.shape[1] // block_w

    def columns(b):
        if b < owned_blocks:
            return res_ref, pl.ds(b * block_w, block_w)
        return slot_ref, pl.ds((b - owned_blocks) * block_w, block_w)

    def link(b):
        return jnp.clip(parent_ref[b], 0, blocks_n - 1)

    for b in range(blocks_n):
        ref, cols = columns(b)
        x = ref[:, cols]
        if b == 0:
            lower = x.astype(jnp.bfloat16)
        else:
            prior = y_ref[link(b)]
            lower = (
                x - lax.dot_general(prior, cpl_ref[b - 1], NT, preferred_element_type=jnp.float32)
            ).astype(jnp.bfloat16)
        y_ref[b] = lax.dot_general(
            lower, inv_ref[b], NT, preferred_element_type=jnp.float32
        ).astype(jnp.bfloat16)

    carry_ref[...] = jnp.zeros(carry_ref.shape, carry_ref.dtype)
    for b in reversed(range(blocks_n)):
        upper = (y_ref[b].astype(jnp.float32) - carry_ref[b]).astype(jnp.bfloat16)
        result = jnp.dot(upper, inv_ref[b], preferred_element_type=jnp.float32).astype(jnp.bfloat16)
        if b < owned_blocks:
            own_ref[:, pl.ds(b * block_w, block_w)] = result
        else:
            zslot_ref[:, pl.ds((b - owned_blocks) * block_w, block_w)] = result
        if b > 0:
            push = jnp.dot(result, cpl_ref[b - 1], preferred_element_type=jnp.float32)
            p = link(b)
            carry_ref[p] = carry_ref[p] + push


def local_solve(parent, residual, slots, diag_inverse, coupling, after):
    nrhs_here, owned_n = residual.shape
    blocks_n, block_w, _ = diag_inverse.shape
    vmem = pltpu.VMEM
    return pl.pallas_call(
        solve_kernel,
        out_shape=(
            jax.ShapeDtypeStruct((nrhs_here, owned_n), jnp.bfloat16),
            jax.ShapeDtypeStruct(slots.shape, jnp.bfloat16),
        ),
        in_specs=[
            pl.BlockSpec(memory_space=pltpu.SMEM),
            pl.BlockSpec(memory_space=vmem),
            pl.BlockSpec(memory_space=vmem),
            pl.BlockSpec(memory_space=vmem),
            pl.BlockSpec(memory_space=vmem),
            pl.BlockSpec(memory_space=pl.ANY),
        ],
        out_specs=(pl.BlockSpec(memory_space=vmem), pl.BlockSpec(memory_space=vmem)),
        scratch_shapes=[
            pltpu.VMEM((blocks_n, nrhs_here, block_w), jnp.bfloat16),
            pltpu.VMEM((blocks_n, nrhs_here, block_w), jnp.float32),
        ],
        compiler_params=pltpu.CompilerParams(vmem_limit_bytes=48 * 1024 * 1024),
    )(parent, residual, slots, diag_inverse, coupling, after)


def split3(value):
    first = value.astype(jnp.bfloat16)
    rest = value - first.astype(jnp.float32)
    second = rest.astype(jnp.bfloat16)
    third = (rest - second.astype(jnp.float32)).astype(jnp.bfloat16)
    return first, second, third


def finish_kernel(count_ref, rows_ref, own_ref, back_ref, solved_ref, vec_ref, out_ref):
    owned_n = own_ref.shape[1]
    kmax_here = vec_ref.shape[0]
    keep = lax.broadcasted_iota(jnp.int32, (kmax_here, 1), 0) < count_ref[0]
    chunk = 512
    rows = rows_ref[...]
    back = back_ref[...]
    s1, s2, _ = split3(solved_ref[...])
    for start in range(0, owned_n, chunk):
        width = min(chunk, owned_n - start)
        cols = pl.ds(start, width)
        here = lax.broadcasted_iota(jnp.int32, (rows.shape[0], width), 1) + start
        onehot = (rows == here).astype(jnp.bfloat16)
        total = own_ref[:, cols].astype(jnp.float32)
        total += jnp.dot(back, onehot, preferred_element_type=jnp.float32)
        v1, v2, _ = split3(jnp.where(keep, vec_ref[:, cols], 0.0))
        for left, right in ((s1, v1), (s1, v2), (s2, v1)):
            total += jnp.dot(left, right, preferred_element_type=jnp.float32)
        out_ref[:, cols] = total


def finish(send_rows, counts, own, returned, solved, deflation):
    vmem = pltpu.VMEM
    return pl.pallas_call(
        finish_kernel,
        out_shape=jax.ShapeDtypeStruct(own.shape, jnp.float32),
        in_specs=[pl.BlockSpec(memory_space=pltpu.SMEM)] + [pl.BlockSpec(memory_space=vmem)] * 5,
        out_specs=pl.BlockSpec(memory_space=vmem),
        compiler_params=pltpu.CompilerParams(vmem_limit_bytes=48 * 1024 * 1024),
    )(counts, send_rows.reshape(-1, 1), own, returned, solved, deflation)


def matchings(count):
    first = [(i, i + 1) for i in range(0, count - 1, 2)] + [(i + 1, i) for i in range(0, count - 1, 2)]
    second = [(i, i + 1) for i in range(1, count - 1, 2)] + [(i + 1, i) for i in range(1, count - 1, 2)]
    return first, second


def swap(value, axis, pairs, extra=None):
    if not pairs:
        return jnp.zeros_like(value), None
    if extra is None:
        return lax.ppermute(value, axis, pairs), None
    rows = value.shape[0]
    packed = jnp.concatenate([value.astype(extra.dtype), extra], axis=0)
    got = lax.ppermute(packed, axis, pairs)
    return got[:rows].astype(value.dtype), got[rows:]


def halo_out(one, two, axis, extra=None):
    even = lax.axis_index(axis) % 2 == 0
    first, second = matchings(lax.axis_size(axis))
    r1, got = swap(one, axis, first, extra)
    r2, _ = swap(two, axis, second)
    return jnp.where(even, r1, r2), jnp.where(even, r2, r1), got


def halo_back(lo, hi, axis, extra=None):
    even = lax.axis_index(axis) % 2 == 0
    first, second = matchings(lax.axis_size(axis))
    r1, got = swap(jnp.where(even, lo, hi), axis, first, extra)
    r2, _ = swap(jnp.where(even, hi, lo), axis, second)
    return jnp.where(even, r2, r1), jnp.where(even, r1, r2), got


def doubling(axis):
    count = lax.axis_size(axis)
    return count > 1 and not count & (count - 1)


def merge(held, other, axis, dim, step):
    low = (lax.axis_index(axis) // step) % 2 == 0
    return jnp.where(
        low,
        jnp.concatenate([held, other], axis=dim),
        jnp.concatenate([other, held], axis=dim),
    )


def gather_axis(held, axis, dim, step=1):
    count = lax.axis_size(axis)
    if not doubling(axis):
        return lax.all_gather(held, axis, axis=dim, tiled=True)
    while step < count:
        pairs = [(i, i ^ step) for i in range(count)]
        held = merge(held, lax.ppermute(held, axis, pairs), axis, dim, step)
        step *= 2
    return held


def rows_of(held):
    return held.reshape(-1, held.shape[-1])


def per_device(
    residual, diag_inverse, coupling, parent, send_rows, counts, deflation, coarse_inverse
):
    nrhs_here, owned_n = residual.shape
    slots_n, face_w = send_rows.shape
    kmax_here = deflation.shape[0]
    mask = (lax.iota(jnp.int32, kmax_here) < counts[0]).astype(jnp.float32)
    vectors = deflation * mask[:, None]
    coeffs_t = lax.dot_general(
        vectors, residual, NT, precision=lax.Precision.HIGH, preferred_element_type=jnp.float32
    )
    total_dev = coarse_inverse.shape[1] // kmax_here

    order = []
    for axis_pos, axis in enumerate(AXES):
        even = lax.axis_index(axis) % 2 == 0
        down, up = send_rows[2 * axis_pos], send_rows[2 * axis_pos + 1]
        order += [jnp.where(even, up, down), jnp.where(even, down, up)]
    outgoing = jnp.take(residual, jnp.stack(order), axis=1)
    incoming = []
    for axis_pos, axis in enumerate(AXES):
        low, high, _ = halo_out(outgoing[:, 2 * axis_pos], outgoing[:, 2 * axis_pos + 1], axis)
        incoming += [low, high]
    slots = jnp.concatenate(incoming, axis=1)
    slots, coeffs_t = lax.optimization_barrier((slots, coeffs_t))
    spread = jnp.broadcast_to(coeffs_t[None], (total_dev,) + coeffs_t.shape)
    held = lax.all_to_all(spread, AXES, 0, 0, tiled=True)
    after = coeffs_t

    own, zslots = local_solve(parent, residual, slots, diag_inverse, coupling, after)
    zslots, held = lax.optimization_barrier((zslots, held))

    returned = []
    for axis_pos, axis in enumerate(AXES):
        low, high, _ = halo_back(
            zslots[:, (2 * axis_pos) * face_w : (2 * axis_pos + 1) * face_w],
            zslots[:, (2 * axis_pos + 1) * face_w : (2 * axis_pos + 2) * face_w],
            axis,
        )
        returned += [low, high]
    returned = jnp.concatenate(returned, axis=1)

    solved_t = jnp.dot(
        coarse_inverse, rows_of(held), precision=lax.Precision.HIGH, preferred_element_type=jnp.float32
    )
    return finish(send_rows, counts, own, returned, solved_t.T, deflation)


def solution(mesh):
    return jax.shard_map(
        per_device,
        mesh=mesh,
        in_specs=(
            P(None, AXES),
            P(AXES, None, None),
            P(AXES, None, None),
            P(AXES),
            P(AXES, None),
            P(AXES),
            P(None, AXES),
            P(AXES, None),
        ),
        out_specs=P(None, AXES),
        check_vma=False,
    )
```

```python
import functools

import jax
import jax.numpy as jnp
from jax import lax
from jax.experimental import pallas as pl
from jax.experimental.pallas import tpu as pltpu
from jax.sharding import PartitionSpec as P

AXES = ("gx", "gy", "gz")
NT = (((1,), (1,)), ((), ()))


def solve_kernel(
    parent_ref, res_ref, slot_ref, inv_ref, cpl_ref, after_ref, own_ref, zslot_ref, y_ref, carry_ref
):
    del after_ref
    blocks_n, block_w, _ = inv_ref.shape
    owned_blocks = res_ref.shape[1] // block_w

    def columns(b):
        if b < owned_blocks:
            return res_ref, pl.ds(b * block_w, block_w)
        return slot_ref, pl.ds((b - owned_blocks) * block_w, block_w)

    def link(b):
        return jnp.clip(parent_ref[b], 0, blocks_n - 1)

    for b in range(blocks_n):
        ref, cols = columns(b)
        x = ref[:, cols]
        if b == 0:
            lower = x.astype(jnp.bfloat16)
        else:
            prior = y_ref[link(b)]
            lower = (
                x - lax.dot_general(prior, cpl_ref[b - 1], NT, preferred_element_type=jnp.float32)
            ).astype(jnp.bfloat16)
        y_ref[b] = lax.dot_general(
            lower, inv_ref[b], NT, preferred_element_type=jnp.float32
        ).astype(jnp.bfloat16)

    carry_ref[...] = jnp.zeros(carry_ref.shape, carry_ref.dtype)
    for b in reversed(range(blocks_n)):
        upper = (y_ref[b].astype(jnp.float32) - carry_ref[b]).astype(jnp.bfloat16)
        result = jnp.dot(upper, inv_ref[b], preferred_element_type=jnp.float32).astype(jnp.bfloat16)
        if b < owned_blocks:
            own_ref[:, pl.ds(b * block_w, block_w)] = result
        else:
            zslot_ref[:, pl.ds((b - owned_blocks) * block_w, block_w)] = result
        if b > 0:
            push = jnp.dot(result, cpl_ref[b - 1], preferred_element_type=jnp.float32)
            p = link(b)
            carry_ref[p] = carry_ref[p] + push


def local_solve(parent, residual, slots, diag_inverse, coupling, after):
    nrhs_here, owned_n = residual.shape
    blocks_n, block_w, _ = diag_inverse.shape
    vmem = pltpu.VMEM
    return pl.pallas_call(
        solve_kernel,
        out_shape=(
            jax.ShapeDtypeStruct((nrhs_here, owned_n), jnp.bfloat16),
            jax.ShapeDtypeStruct(slots.shape, jnp.bfloat16),
        ),
        in_specs=[
            pl.BlockSpec(memory_space=pltpu.SMEM),
            pl.BlockSpec(memory_space=vmem),
            pl.BlockSpec(memory_space=vmem),
            pl.BlockSpec(memory_space=vmem),
            pl.BlockSpec(memory_space=vmem),
            pl.BlockSpec(memory_space=pl.ANY),
        ],
        out_specs=(pl.BlockSpec(memory_space=vmem), pl.BlockSpec(memory_space=vmem)),
        scratch_shapes=[
            pltpu.VMEM((blocks_n, nrhs_here, block_w), jnp.bfloat16),
            pltpu.VMEM((blocks_n, nrhs_here, block_w), jnp.float32),
        ],
        compiler_params=pltpu.CompilerParams(vmem_limit_bytes=48 * 1024 * 1024),
    )(parent, residual, slots, diag_inverse, coupling, after)


def split3(value):
    first = value.astype(jnp.bfloat16)
    rest = value - first.astype(jnp.float32)
    second = rest.astype(jnp.bfloat16)
    third = (rest - second.astype(jnp.float32)).astype(jnp.bfloat16)
    return first, second, third


def finish_kernel(count_ref, rows_ref, own_ref, back_ref, solved_ref, vec_ref, out_ref):
    owned_n = own_ref.shape[1]
    kmax_here = vec_ref.shape[0]
    keep = lax.broadcasted_iota(jnp.int32, (kmax_here, 1), 0) < count_ref[0]
    chunk = 512
    rows = rows_ref[...]
    back = back_ref[...]
    s1, s2, _ = split3(solved_ref[...])
    for start in range(0, owned_n, chunk):
        width = min(chunk, owned_n - start)
        cols = pl.ds(start, width)
        here = lax.broadcasted_iota(jnp.int32, (rows.shape[0], width), 1) + start
        onehot = (rows == here).astype(jnp.bfloat16)
        total = own_ref[:, cols].astype(jnp.float32)
        total += jnp.dot(back, onehot, preferred_element_type=jnp.float32)
        v1, v2, _ = split3(jnp.where(keep, vec_ref[:, cols], 0.0))
        for left, right in ((s1, v1), (s1, v2), (s2, v1)):
            total += jnp.dot(left, right, preferred_element_type=jnp.float32)
        out_ref[:, cols] = total


def finish(send_rows, counts, own, returned, solved, deflation):
    vmem = pltpu.VMEM
    return pl.pallas_call(
        finish_kernel,
        out_shape=jax.ShapeDtypeStruct(own.shape, jnp.float32),
        in_specs=[pl.BlockSpec(memory_space=pltpu.SMEM)] + [pl.BlockSpec(memory_space=vmem)] * 5,
        out_specs=pl.BlockSpec(memory_space=vmem),
        compiler_params=pltpu.CompilerParams(vmem_limit_bytes=48 * 1024 * 1024),
    )(counts, send_rows.reshape(-1, 1), own, returned, solved, deflation)


def matchings(count):
    first = [(i, i + 1) for i in range(0, count - 1, 2)] + [(i + 1, i) for i in range(0, count - 1, 2)]
    second = [(i, i + 1) for i in range(1, count - 1, 2)] + [(i + 1, i) for i in range(1, count - 1, 2)]
    return first, second


def swap(value, axis, pairs, extra=None):
    if not pairs:
        return jnp.zeros_like(value), None
    if extra is None:
        return lax.ppermute(value, axis, pairs), None
    rows = value.shape[0]
    packed = jnp.concatenate([value.astype(extra.dtype), extra], axis=0)
    got = lax.ppermute(packed, axis, pairs)
    return got[:rows].astype(value.dtype), got[rows:]


def halo_out(one, two, axis, extra=None):
    even = lax.axis_index(axis) % 2 == 0
    first, second = matchings(lax.axis_size(axis))
    r1, got = swap(one, axis, first, extra)
    r2, _ = swap(two, axis, second)
    return jnp.where(even, r1, r2), jnp.where(even, r2, r1), got


def halo_back(lo, hi, axis, extra=None):
    even = lax.axis_index(axis) % 2 == 0
    first, second = matchings(lax.axis_size(axis))
    r1, got = swap(jnp.where(even, lo, hi), axis, first, extra)
    r2, _ = swap(jnp.where(even, hi, lo), axis, second)
    return jnp.where(even, r2, r1), jnp.where(even, r1, r2), got


def doubling(axis):
    count = lax.axis_size(axis)
    return count > 1 and not count & (count - 1)


def merge(held, other, axis, dim, step):
    low = (lax.axis_index(axis) // step) % 2 == 0
    return jnp.where(
        low,
        jnp.concatenate([held, other], axis=dim),
        jnp.concatenate([other, held], axis=dim),
    )


def gather_axis(held, axis, dim, step=1):
    count = lax.axis_size(axis)
    if not doubling(axis):
        return lax.all_gather(held, axis, axis=dim, tiled=True)
    while step < count:
        pairs = [(i, i ^ step) for i in range(count)]
        held = merge(held, lax.ppermute(held, axis, pairs), axis, dim, step)
        step *= 2
    return held


def rows_of(held):
    return held.reshape(-1, held.shape[-1])


def per_device(
    residual, diag_inverse, coupling, parent, send_rows, counts, deflation, coarse_inverse
):
    nrhs_here, owned_n = residual.shape
    slots_n, face_w = send_rows.shape
    kmax_here = deflation.shape[0]
    mask = (lax.iota(jnp.int32, kmax_here) < counts[0]).astype(jnp.float32)
    vectors = deflation * mask[:, None]
    coeffs_t = lax.dot_general(
        vectors, residual, NT, precision=lax.Precision.HIGH, preferred_element_type=jnp.float32
    )
    total_dev = coarse_inverse.shape[1] // kmax_here

    sizes = [lax.axis_size(axis) for axis in AXES]
    strides = [1] * len(AXES)
    for axis_pos in reversed(range(len(AXES) - 1)):
        strides[axis_pos] = strides[axis_pos + 1] * sizes[axis_pos + 1]
    face_stride = jnp.array([strides[f // 2] for f in range(slots_n)], jnp.int32)
    face_size = jnp.array([sizes[f // 2] for f in range(slots_n)], jnp.int32)
    even = (lax.axis_index(AXES) // face_stride) % face_size % 2 == 0
    flip = jnp.array([f ^ 1 for f in range(slots_n)], jnp.int32)
    order = jnp.where(even[:, None], send_rows[flip], send_rows)
    outgoing = jnp.take(residual, order, axis=1)
    incoming = []
    for axis_pos, axis in enumerate(AXES):
        low, high, _ = halo_out(outgoing[:, 2 * axis_pos], outgoing[:, 2 * axis_pos + 1], axis)
        incoming += [low, high]
    slots = jnp.concatenate(incoming, axis=1)
    slots, coeffs_t = lax.optimization_barrier((slots, coeffs_t))
    spread = jnp.broadcast_to(coeffs_t[None], (total_dev,) + coeffs_t.shape)
    held = lax.all_to_all(spread, AXES, 0, 0, tiled=True)
    after = coeffs_t

    own, zslots = local_solve(parent, residual, slots, diag_inverse, coupling, after)
    zslots, held = lax.optimization_barrier((zslots, held))

    returned = []
    for axis_pos, axis in enumerate(AXES):
        low, high, _ = halo_back(
            zslots[:, (2 * axis_pos) * face_w : (2 * axis_pos + 1) * face_w],
            zslots[:, (2 * axis_pos + 1) * face_w : (2 * axis_pos + 2) * face_w],
            axis,
        )
        returned += [low, high]
    returned = jnp.concatenate(returned, axis=1)

    solved_t = jnp.dot(
        coarse_inverse, rows_of(held), precision=lax.Precision.HIGH, preferred_element_type=jnp.float32
    )
    return finish(send_rows, counts, own, returned, solved_t.T, deflation)


def solution(mesh):
    return jax.shard_map(
        per_device,
        mesh=mesh,
        in_specs=(
            P(None, AXES),
            P(AXES, None, None),
            P(AXES, None, None),
            P(AXES),
            P(AXES, None),
            P(AXES),
            P(None, AXES),
            P(AXES, None),
        ),
        out_specs=P(None, AXES),
        check_vma=False,
    )
```

```python
import functools

import jax
import jax.numpy as jnp
from jax import lax
from jax.experimental import pallas as pl
from jax.experimental.pallas import tpu as pltpu
from jax.sharding import PartitionSpec as P

AXES = ("gx", "gy", "gz")
NT = (((1,), (1,)), ((), ()))


def solve_kernel(
    parent_ref, res_ref, slot_ref, inv_ref, cpl_ref, after_ref, own_ref, zslot_ref, y_ref, carry_ref
):
    del after_ref
    blocks_n, block_w, _ = inv_ref.shape
    owned_blocks = res_ref.shape[1] // block_w

    def columns(b):
        if b < owned_blocks:
            return res_ref, pl.ds(b * block_w, block_w)
        return slot_ref, pl.ds((b - owned_blocks) * block_w, block_w)

    def link(b):
        return jnp.clip(parent_ref[b], 0, blocks_n - 1)

    for b in range(blocks_n):
        ref, cols = columns(b)
        x = ref[:, cols]
        if b == 0:
            lower = x.astype(jnp.bfloat16)
        else:
            prior = y_ref[link(b)]
            lower = (
                x - lax.dot_general(prior, cpl_ref[b - 1], NT, preferred_element_type=jnp.float32)
            ).astype(jnp.bfloat16)
        y_ref[b] = lax.dot_general(
            lower, inv_ref[b], NT, preferred_element_type=jnp.float32
        ).astype(jnp.bfloat16)

    carry_ref[...] = jnp.zeros(carry_ref.shape, carry_ref.dtype)
    for b in reversed(range(blocks_n)):
        upper = (y_ref[b].astype(jnp.float32) - carry_ref[b]).astype(jnp.bfloat16)
        result = jnp.dot(upper, inv_ref[b], preferred_element_type=jnp.float32).astype(jnp.bfloat16)
        if b < owned_blocks:
            own_ref[:, pl.ds(b * block_w, block_w)] = result
        else:
            zslot_ref[:, pl.ds((b - owned_blocks) * block_w, block_w)] = result
        if b > 0:
            push = jnp.dot(result, cpl_ref[b - 1], preferred_element_type=jnp.float32)
            p = link(b)
            carry_ref[p] = carry_ref[p] + push


def local_solve(parent, residual, slots, diag_inverse, coupling, after):
    nrhs_here, owned_n = residual.shape
    blocks_n, block_w, _ = diag_inverse.shape
    vmem = pltpu.VMEM
    return pl.pallas_call(
        solve_kernel,
        out_shape=(
            jax.ShapeDtypeStruct((nrhs_here, owned_n), jnp.bfloat16),
            jax.ShapeDtypeStruct(slots.shape, jnp.bfloat16),
        ),
        in_specs=[
            pl.BlockSpec(memory_space=pltpu.SMEM),
            pl.BlockSpec(memory_space=vmem),
            pl.BlockSpec(memory_space=vmem),
            pl.BlockSpec(memory_space=vmem),
            pl.BlockSpec(memory_space=vmem),
            pl.BlockSpec(memory_space=pl.ANY),
        ],
        out_specs=(pl.BlockSpec(memory_space=vmem), pl.BlockSpec(memory_space=vmem)),
        scratch_shapes=[
            pltpu.VMEM((blocks_n, nrhs_here, block_w), jnp.bfloat16),
            pltpu.VMEM((blocks_n, nrhs_here, block_w), jnp.float32),
        ],
        compiler_params=pltpu.CompilerParams(vmem_limit_bytes=48 * 1024 * 1024),
    )(parent, residual, slots, diag_inverse, coupling, after)


def split3(value):
    first = value.astype(jnp.bfloat16)
    rest = value - first.astype(jnp.float32)
    second = rest.astype(jnp.bfloat16)
    third = (rest - second.astype(jnp.float32)).astype(jnp.bfloat16)
    return first, second, third


def finish_kernel(count_ref, rows_ref, own_ref, back_ref, held_ref, inverse_ref, vec_ref, out_ref):
    owned_n = own_ref.shape[1]
    kmax_here = vec_ref.shape[0]
    keep = lax.broadcasted_iota(jnp.int32, (kmax_here, 1), 0) < count_ref[0]
    chunk = 512
    rows = rows_ref[...]
    back = back_ref[...]
    h1, h2, _ = split3(held_ref[...])
    c1, c2, _ = split3(inverse_ref[...])
    solved = sum(
        lax.dot_general(left, right, NT, preferred_element_type=jnp.float32)
        for left, right in ((h1, c1), (h1, c2), (h2, c1))
    )
    s1, s2, _ = split3(solved)
    for start in range(0, owned_n, chunk):
        width = min(chunk, owned_n - start)
        cols = pl.ds(start, width)
        here = lax.broadcasted_iota(jnp.int32, (rows.shape[0], width), 1) + start
        onehot = (rows == here).astype(jnp.bfloat16)
        total = own_ref[:, cols].astype(jnp.float32)
        total += jnp.dot(back, onehot, preferred_element_type=jnp.float32)
        v1, v2, _ = split3(jnp.where(keep, vec_ref[:, cols], 0.0))
        for left, right in ((s1, v1), (s1, v2), (s2, v1)):
            total += jnp.dot(left, right, preferred_element_type=jnp.float32)
        out_ref[:, cols] = total


def finish(send_rows, counts, own, returned, held_t, coarse_inverse, deflation):
    vmem = pltpu.VMEM
    return pl.pallas_call(
        finish_kernel,
        out_shape=jax.ShapeDtypeStruct(own.shape, jnp.float32),
        in_specs=[pl.BlockSpec(memory_space=pltpu.SMEM)] + [pl.BlockSpec(memory_space=vmem)] * 6,
        out_specs=pl.BlockSpec(memory_space=vmem),
        compiler_params=pltpu.CompilerParams(vmem_limit_bytes=48 * 1024 * 1024),
    )(counts, send_rows.reshape(-1, 1), own, returned, held_t, coarse_inverse, deflation)


def matchings(count):
    first = [(i, i + 1) for i in range(0, count - 1, 2)] + [(i + 1, i) for i in range(0, count - 1, 2)]
    second = [(i, i + 1) for i in range(1, count - 1, 2)] + [(i + 1, i) for i in range(1, count - 1, 2)]
    return first, second


def swap(value, axis, pairs, extra=None):
    if not pairs:
        return jnp.zeros_like(value), None
    if extra is None:
        return lax.ppermute(value, axis, pairs), None
    rows = value.shape[0]
    packed = jnp.concatenate([value.astype(extra.dtype), extra], axis=0)
    got = lax.ppermute(packed, axis, pairs)
    return got[:rows].astype(value.dtype), got[rows:]


def halo_out(down, up, axis, extra=None):
    even = lax.axis_index(axis) % 2 == 0
    first, second = matchings(lax.axis_size(axis))
    r1, got = swap(jnp.where(even, up, down), axis, first, extra)
    r2, _ = swap(jnp.where(even, down, up), axis, second)
    return jnp.where(even, r1, r2), jnp.where(even, r2, r1), got


def halo_back(lo, hi, axis, extra=None):
    even = lax.axis_index(axis) % 2 == 0
    first, second = matchings(lax.axis_size(axis))
    r1, got = swap(jnp.where(even, lo, hi), axis, first, extra)
    r2, _ = swap(jnp.where(even, hi, lo), axis, second)
    return jnp.where(even, r2, r1), jnp.where(even, r1, r2), got


def doubling(axis):
    count = lax.axis_size(axis)
    return count > 1 and not count & (count - 1)


def merge(held, other, axis, dim, step):
    low = (lax.axis_index(axis) // step) % 2 == 0
    return jnp.where(
        low,
        jnp.concatenate([held, other], axis=dim),
        jnp.concatenate([other, held], axis=dim),
    )


def gather_axis(held, axis, dim, step=1):
    count = lax.axis_size(axis)
    if not doubling(axis):
        return lax.all_gather(held, axis, axis=dim, tiled=True)
    while step < count:
        pairs = [(i, i ^ step) for i in range(count)]
        held = merge(held, lax.ppermute(held, axis, pairs), axis, dim, step)
        step *= 2
    return held


def rows_of(held):
    return held.reshape(-1, held.shape[-1])


def per_device(
    residual, diag_inverse, coupling, parent, send_rows, counts, deflation, coarse_inverse
):
    nrhs_here, owned_n = residual.shape
    slots_n, face_w = send_rows.shape
    kmax_here = deflation.shape[0]
    mask = (lax.iota(jnp.int32, kmax_here) < counts[0]).astype(jnp.float32)
    vectors = deflation * mask[:, None]
    coeffs_t = lax.dot_general(
        vectors, residual, NT, precision=lax.Precision.HIGH, preferred_element_type=jnp.float32
    )
    total_dev = coarse_inverse.shape[1] // kmax_here

    outgoing = jnp.take(residual, send_rows, axis=1)
    incoming = []
    for axis_pos, axis in enumerate(AXES):
        low, high, _ = halo_out(outgoing[:, 2 * axis_pos], outgoing[:, 2 * axis_pos + 1], axis)
        incoming += [low, high]
    slots = jnp.concatenate(incoming, axis=1)
    slots, coeffs_t = lax.optimization_barrier((slots, coeffs_t))
    spread = jnp.broadcast_to(coeffs_t[None], (total_dev,) + coeffs_t.shape)
    held = lax.all_to_all(spread, AXES, 0, 0, tiled=True)
    after = coeffs_t

    own, zslots = local_solve(parent, residual, slots, diag_inverse, coupling, after)
    zslots, held = lax.optimization_barrier((zslots, held))

    returned = []
    for axis_pos, axis in enumerate(AXES):
        low, high, _ = halo_back(
            zslots[:, (2 * axis_pos) * face_w : (2 * axis_pos + 1) * face_w],
            zslots[:, (2 * axis_pos + 1) * face_w : (2 * axis_pos + 2) * face_w],
            axis,
        )
        returned += [low, high]
    returned = jnp.concatenate(returned, axis=1)

    return finish(send_rows, counts, own, returned, rows_of(held).T, coarse_inverse, deflation)


def solution(mesh):
    return jax.shard_map(
        per_device,
        mesh=mesh,
        in_specs=(
            P(None, AXES),
            P(AXES, None, None),
            P(AXES, None, None),
            P(AXES),
            P(AXES, None),
            P(AXES),
            P(None, AXES),
            P(AXES, None),
        ),
        out_specs=P(None, AXES),
        check_vma=False,
    )
```

```python
import functools

import jax
import jax.numpy as jnp
from jax import lax
from jax.experimental import pallas as pl
from jax.experimental.pallas import tpu as pltpu
from jax.sharding import PartitionSpec as P

AXES = ("gx", "gy", "gz")
NT = (((1,), (1,)), ((), ()))


def solve_kernel(
    parent_ref, res_ref, slot_ref, inv_ref, cpl_ref, after_ref, own_ref, zslot_ref, y_ref, carry_ref
):
    del after_ref
    blocks_n, block_w, _ = inv_ref.shape
    owned_blocks = res_ref.shape[1] // block_w

    def columns(b):
        if b < owned_blocks:
            return res_ref, pl.ds(b * block_w, block_w)
        return slot_ref, pl.ds((b - owned_blocks) * block_w, block_w)

    def link(b):
        return jnp.clip(parent_ref[b], 0, blocks_n - 1)

    for b in range(blocks_n):
        ref, cols = columns(b)
        x = ref[:, cols]
        if b == 0:
            lower = x.astype(jnp.bfloat16)
        else:
            prior = y_ref[link(b)]
            lower = (
                x - lax.dot_general(prior, cpl_ref[b - 1], NT, preferred_element_type=jnp.float32)
            ).astype(jnp.bfloat16)
        y_ref[b] = lax.dot_general(
            lower, inv_ref[b], NT, preferred_element_type=jnp.float32
        ).astype(jnp.bfloat16)

    carry_ref[...] = jnp.zeros(carry_ref.shape, carry_ref.dtype)
    for b in reversed(range(blocks_n)):
        upper = (y_ref[b].astype(jnp.float32) - carry_ref[b]).astype(jnp.bfloat16)
        result = jnp.dot(upper, inv_ref[b], preferred_element_type=jnp.float32).astype(jnp.bfloat16)
        if b < owned_blocks:
            own_ref[:, pl.ds(b * block_w, block_w)] = result
        else:
            zslot_ref[:, pl.ds((b - owned_blocks) * block_w, block_w)] = result
        if b > 0:
            push = jnp.dot(result, cpl_ref[b - 1], preferred_element_type=jnp.float32)
            p = link(b)
            carry_ref[p] = carry_ref[p] + push


def local_solve(parent, residual, slots, diag_inverse, coupling, after):
    nrhs_here, owned_n = residual.shape
    blocks_n, block_w, _ = diag_inverse.shape
    vmem = pltpu.VMEM
    return pl.pallas_call(
        solve_kernel,
        out_shape=(
            jax.ShapeDtypeStruct((nrhs_here, owned_n), jnp.bfloat16),
            jax.ShapeDtypeStruct(slots.shape, jnp.bfloat16),
        ),
        in_specs=[
            pl.BlockSpec(memory_space=pltpu.SMEM),
            pl.BlockSpec(memory_space=vmem),
            pl.BlockSpec(memory_space=vmem),
            pl.BlockSpec(memory_space=vmem),
            pl.BlockSpec(memory_space=vmem),
            pl.BlockSpec(memory_space=pl.ANY),
        ],
        out_specs=(pl.BlockSpec(memory_space=vmem), pl.BlockSpec(memory_space=vmem)),
        scratch_shapes=[
            pltpu.VMEM((blocks_n, nrhs_here, block_w), jnp.bfloat16),
            pltpu.VMEM((blocks_n, nrhs_here, block_w), jnp.float32),
        ],
        compiler_params=pltpu.CompilerParams(vmem_limit_bytes=48 * 1024 * 1024),
    )(parent, residual, slots, diag_inverse, coupling, after)


def split3(value):
    first = value.astype(jnp.bfloat16)
    rest = value - first.astype(jnp.float32)
    second = rest.astype(jnp.bfloat16)
    third = (rest - second.astype(jnp.float32)).astype(jnp.bfloat16)
    return first, second, third


def finish_kernel(count_ref, rows_ref, own_ref, back_ref, solved_ref, vec_ref, out_ref):
    owned_n = own_ref.shape[1]
    kmax_here = vec_ref.shape[0]
    keep = lax.broadcasted_iota(jnp.int32, (kmax_here, 1), 0) < count_ref[0]
    chunk = 1024
    rows = rows_ref[...]
    back = back_ref[...]
    s1, s2, _ = split3(solved_ref[...])
    for start in range(0, owned_n, chunk):
        width = min(chunk, owned_n - start)
        cols = pl.ds(start, width)
        here = lax.broadcasted_iota(jnp.int32, (rows.shape[0], width), 1) + start
        onehot = (rows == here).astype(jnp.bfloat16)
        total = own_ref[:, cols].astype(jnp.float32)
        total += jnp.dot(back, onehot, preferred_element_type=jnp.float32)
        v1, v2, _ = split3(jnp.where(keep, vec_ref[:, cols], 0.0))
        for left, right in ((s1, v1), (s1, v2), (s2, v1)):
            total += jnp.dot(left, right, preferred_element_type=jnp.float32)
        out_ref[:, cols] = total


def finish(send_rows, counts, own, returned, solved, deflation):
    vmem = pltpu.VMEM
    return pl.pallas_call(
        finish_kernel,
        out_shape=jax.ShapeDtypeStruct(own.shape, jnp.float32),
        in_specs=[pl.BlockSpec(memory_space=pltpu.SMEM)] + [pl.BlockSpec(memory_space=vmem)] * 5,
        out_specs=pl.BlockSpec(memory_space=vmem),
        compiler_params=pltpu.CompilerParams(vmem_limit_bytes=48 * 1024 * 1024),
    )(counts, send_rows.reshape(-1, 1), own, returned, solved, deflation)


def matchings(count):
    first = [(i, i + 1) for i in range(0, count - 1, 2)] + [(i + 1, i) for i in range(0, count - 1, 2)]
    second = [(i, i + 1) for i in range(1, count - 1, 2)] + [(i + 1, i) for i in range(1, count - 1, 2)]
    return first, second


def swap(value, axis, pairs, extra=None):
    if not pairs:
        return jnp.zeros_like(value), None
    if extra is None:
        return lax.ppermute(value, axis, pairs), None
    rows = value.shape[0]
    packed = jnp.concatenate([value.astype(extra.dtype), extra], axis=0)
    got = lax.ppermute(packed, axis, pairs)
    return got[:rows].astype(value.dtype), got[rows:]


def halo_out(down, up, axis, extra=None):
    even = lax.axis_index(axis) % 2 == 0
    first, second = matchings(lax.axis_size(axis))
    r1, got = swap(jnp.where(even, up, down), axis, first, extra)
    r2, _ = swap(jnp.where(even, down, up), axis, second)
    return jnp.where(even, r1, r2), jnp.where(even, r2, r1), got


def halo_back(lo, hi, axis, extra=None):
    even = lax.axis_index(axis) % 2 == 0
    first, second = matchings(lax.axis_size(axis))
    r1, got = swap(jnp.where(even, lo, hi), axis, first, extra)
    r2, _ = swap(jnp.where(even, hi, lo), axis, second)
    return jnp.where(even, r2, r1), jnp.where(even, r1, r2), got


def doubling(axis):
    count = lax.axis_size(axis)
    return count > 1 and not count & (count - 1)


def merge(held, other, axis, dim, step):
    low = (lax.axis_index(axis) // step) % 2 == 0
    return jnp.where(
        low,
        jnp.concatenate([held, other], axis=dim),
        jnp.concatenate([other, held], axis=dim),
    )


def gather_axis(held, axis, dim, step=1):
    count = lax.axis_size(axis)
    if not doubling(axis):
        return lax.all_gather(held, axis, axis=dim, tiled=True)
    while step < count:
        pairs = [(i, i ^ step) for i in range(count)]
        held = merge(held, lax.ppermute(held, axis, pairs), axis, dim, step)
        step *= 2
    return held


def rows_of(held):
    return held.reshape(-1, held.shape[-1])


def per_device(
    residual, diag_inverse, coupling, parent, send_rows, counts, deflation, coarse_inverse
):
    nrhs_here, owned_n = residual.shape
    slots_n, face_w = send_rows.shape
    kmax_here = deflation.shape[0]
    mask = (lax.iota(jnp.int32, kmax_here) < counts[0]).astype(jnp.float32)
    vectors = deflation * mask[:, None]
    coeffs_t = lax.dot_general(
        vectors, residual, NT, precision=lax.Precision.HIGH, preferred_element_type=jnp.float32
    )
    total_dev = coarse_inverse.shape[1] // kmax_here

    outgoing = jnp.take(residual, send_rows, axis=1)
    incoming = []
    for axis_pos, axis in enumerate(AXES):
        low, high, _ = halo_out(outgoing[:, 2 * axis_pos], outgoing[:, 2 * axis_pos + 1], axis)
        incoming += [low, high]
    slots = jnp.concatenate(incoming, axis=1)
    slots, coeffs_t = lax.optimization_barrier((slots, coeffs_t))
    spread = jnp.broadcast_to(coeffs_t[None], (total_dev,) + coeffs_t.shape)
    held = lax.all_to_all(spread, AXES, 0, 0, tiled=True)
    after = coeffs_t

    own, zslots = local_solve(parent, residual, slots, diag_inverse, coupling, after)
    zslots, held = lax.optimization_barrier((zslots, held))

    returned = []
    for axis_pos, axis in enumerate(AXES):
        low, high, _ = halo_back(
            zslots[:, (2 * axis_pos) * face_w : (2 * axis_pos + 1) * face_w],
            zslots[:, (2 * axis_pos + 1) * face_w : (2 * axis_pos + 2) * face_w],
            axis,
        )
        returned += [low, high]
    returned = jnp.concatenate(returned, axis=1)

    solved_t = jnp.dot(
        coarse_inverse, rows_of(held), precision=lax.Precision.HIGH, preferred_element_type=jnp.float32
    )
    return finish(send_rows, counts, own, returned, solved_t.T, deflation)


def solution(mesh):
    return jax.shard_map(
        per_device,
        mesh=mesh,
        in_specs=(
            P(None, AXES),
            P(AXES, None, None),
            P(AXES, None, None),
            P(AXES),
            P(AXES, None),
            P(AXES),
            P(None, AXES),
            P(AXES, None),
        ),
        out_specs=P(None, AXES),
        check_vma=False,
    )
```
